256 devices in a mesh: gx: 16 (over x, y), gy: 16 (over z, core).
Axes of the slice: x: 4, y: 4, z: 8, core: 2. Of those that a mesh axis runs over, the one named last changes fastest.
Arguments:
- tokens: bfloat16 [2048, 2048], P('gy', 'gx'), may hold values from -6 to 6
- gain: bfloat16 [2048], P('gx'), may hold values from 0.5 to 1.5
- w_router: bfloat16 [2048, 8], P('gx'), may hold values from -0.25 to 0.25
- expert_query_weight: bfloat16 [8, 2048, 16, 128], P(None, 'gx', 'gy'), may hold values from -0.25 to 0.25
- key_value_weight: bfloat16 [2048, 16, 256], P('gx', 'gy'), may hold values from -0.125 to 0.125
- expert_output_weight: bfloat16 [8, 16, 128, 2048], P(None, 'gy', None, 'gx'), may hold values from -0.25 to 0.25
- cache_keys: bfloat16 [16, 16, 4096, 128], P('gx', 'gy'), may hold values from -1220 to 1220
- cached_value_slots: bfloat16 [16, 16, 4096, 128], P('gx', 'gy'), may hold values from -6 to 6
- lengths: int32 [16], replicated, may hold values from 1 to 4096, 34816 in all
- deal: int32 [16], replicated, may hold values from 0 to 15, each once
- route: int32 [2048, 2], replicated, may hold values from 0 to 7, all different within a row
Outputs:
- mixed: bfloat16 [2048, 2048], P('gy', 'gx')
The draws below stay inside these ranges and needn't reach their ends.
Inputs may be any that keep to these rules, and one draw needn't show every extreme that they name: `lengths`: each request's cache holds between 1 and 4096 keys, and the longest holds exactly 4096. deal[r] is the cache slot of request r; every slot is used once. `route`: each token names 2 different attention experts.
All inputs are finite; a program needn't handle non-finite values.
Results may differ from the reference program's by a relative error of at most 0.01.
The reference program's roundings to bfloat16 on the way count: a program that leaves them out, or rounds other values in their place, can miss the bound.
Values may be sent and summed in bfloat16 or wider, within the bound.
No kernel may reach another device: no remote copies, remote signals or barrier semaphores. Data moves between devices by JAX's collectives and lax.ppermute only.
A program may use at most 64 MiB of HBM per device.

```python
import math
import jax
import jax.numpy as jnp
import numpy as np
from jax import lax

MODEL_WIDTH = 2048
KEY_VALUE_HEADS = 16
HEAD_SIZE = 128
ATTENTION_EXPERTS = 8
EXPERTS_PER_TOKEN = 2
REQUEST_TOKENS = 128
CACHE_LENGTH = 4096
REQUEST_COUNT = 16
TOKEN_COUNT = 2048


def draw_cache_keys(key, part):
    cache_offset = jax.random.normal(jax.random.fold_in(key, 11), (REQUEST_COUNT, KEY_VALUE_HEADS, CACHE_LENGTH, HEAD_SIZE), jnp.float32)
    cache_offset = jnp.clip(cache_offset, -6.0, 6.0)
    return cache_offset.astype(jnp.bfloat16)


def shard_levels(own_key, extent, split, low, largest):
    level, own = 1.0, jax.random.fold_in(own_key, 6)
    for position, blocks in split:
        steps = jnp.exp(jax.random.uniform(jax.random.fold_in(own, position), (blocks,), jnp.float32, low / len(split), largest / len(split)))
        level = level * jnp.repeat(steps, extent[position] // blocks).reshape([-1 if axis == position else 1 for axis in range(len(extent))])
    return level


def picks_of(stream_key, rows, number_of, top, lift):
    sequence = jax.random.permutation(jax.random.fold_in(stream_key, 1), number_of)
    boost = sequence
    for power in range(3):
        boost = boost * boost // number_of
    boost = boost * lift // number_of
    chance = jax.random.randint(jax.random.fold_in(stream_key, 2), (rows, number_of), 0, 4096) + boost
    sure = jax.random.permutation(jax.random.fold_in(stream_key, 3), rows)[jnp.arange(number_of) % rows]
    chance = jnp.where(jnp.arange(rows)[:, None] == sure[None, :], 1 << 14, chance)
    score = chance * number_of + jnp.arange(number_of)
    return lax.top_k(score.astype(jnp.int32), top)[1].astype(jnp.int32)


def length_profile(number_of, total, bound, lean):
    portions = [(1 << 20) // math.isqrt(rank ** lean) + 1 for rank in range(2, number_of + 1)]
    spare, holding = total - bound - (number_of - 1), [1] * (number_of - 1)
    while spare > 0:
        candidates = [i for i in range(number_of - 1) if holding[i] < bound]
        mass, remaining = sum([portions[i] for i in candidates]), spare
        for i in candidates:
            addition = min(bound - holding[i], max(1, remaining * portions[i] // mass), spare)
            holding[i] = holding[i] + addition
            spare = spare - addition
    return np.array([bound] + holding)


def ragged(rng, number_of, total, limit, slope):
    if number_of == 2:
        one = jax.random.randint(rng, (), max(1, total - limit), min(limit, total - 1) + 1)
        return jnp.stack([one, total - one])
    sizes = jnp.asarray(length_profile(number_of, total, limit, slope), jnp.int32)
    couples = (number_of - 1) // 2
    giver, taker = sizes[1:1 + 2 * couples:2], sizes[2:2 + 2 * couples:2]
    margin = jnp.minimum(giver - 1, limit - taker)
    passed = jax.random.randint(jax.random.fold_in(rng, 1), (couples,), 0, 1 << 20) % (margin + 1)
    sizes = sizes.at[1:1 + 2 * couples:2].set(giver - passed).at[2:2 + 2 * couples:2].set(taker + passed)
    return sizes[jax.random.permutation(jax.random.fold_in(rng, 2), number_of)]


def scatter_about(key, extent, spread, limit, split=(), held_as=jnp.bfloat16):
    result = jax.random.normal(key, extent, jnp.float32) * spread
    if len(split) > 0:
        result = shard_levels(key, extent, split, -0.22, 0.18) * result
    return jnp.clip(result, min=-limit, max=limit).astype(held_as)


def setup_inputs(seed: int = 0) -> dict:
    key_of = jax.random.split(jax.random.key(seed), 12)
    tokens = scatter_about(key_of[0], (TOKEN_COUNT, MODEL_WIDTH), 1.0, 6.0, ((0, 16), (1, 16)))
    gain = jnp.clip(1.0 + 0.1 * jax.random.normal(key_of[1], (MODEL_WIDTH,), jnp.float32), 0.5, 1.5).astype(jnp.bfloat16)
    w_router = scatter_about(key_of[2], (MODEL_WIDTH, ATTENTION_EXPERTS), (MODEL_WIDTH // 4) ** -0.5, 0.25, ((0, 16),))
    expert_query_weight = scatter_about(key_of[3], (ATTENTION_EXPERTS, MODEL_WIDTH, KEY_VALUE_HEADS, HEAD_SIZE), (MODEL_WIDTH // 4) ** -0.5, 0.25, ((1, 16), (2, 16)))
    key_value_weight = scatter_about(key_of[4], (MODEL_WIDTH, KEY_VALUE_HEADS, 2 * HEAD_SIZE), MODEL_WIDTH ** -0.5, 0.125, ((0, 16), (1, 16)))
    expert_output_weight = scatter_about(key_of[5], (ATTENTION_EXPERTS, KEY_VALUE_HEADS, HEAD_SIZE, MODEL_WIDTH), (HEAD_SIZE * 4) ** -0.5, 0.25, ((1, 16), (3, 16)))
    cache_keys = draw_cache_keys(jax.random.fold_in(key_of[11], 71), 0)
    cached_value_slots = scatter_about(key_of[7], (REQUEST_COUNT, KEY_VALUE_HEADS, CACHE_LENGTH, HEAD_SIZE), 1.0, 6.0, ((0, 16), (1, 16)))
    lengths = ragged(key_of[8], REQUEST_COUNT, (REQUEST_COUNT + 1) * CACHE_LENGTH // 2, CACHE_LENGTH, 1).astype(jnp.int32)
    deal = jax.random.permutation(key_of[9], REQUEST_COUNT).astype(jnp.int32)
    route = picks_of(key_of[10], TOKEN_COUNT, ATTENTION_EXPERTS, EXPERTS_PER_TOKEN, 2048)
    return {"tokens": tokens, "gain": gain, "w_router": w_router, "expert_query_weight": expert_query_weight, "key_value_weight": key_value_weight, "expert_output_weight": expert_output_weight, "cache_keys": cache_keys, "cached_value_slots": cached_value_slots, "lengths": lengths, "deal": deal, "route": route}


masked_score = -1e+30
norm_eps = 1e-06

def attend_head(operand_set, length):
    query_by_head, cache_k, cache_v, fresh_k, fresh_v = operand_set
    keys = jnp.concatenate([cache_k, fresh_k], axis=0)
    values = jnp.concatenate([cache_v, fresh_v], axis=0)
    scores = jnp.dot(query_by_head, keys.T, preferred_element_type=jnp.float32) * HEAD_SIZE ** (-0.5)
    query_rows = query_by_head.shape[0]
    token_of_row = jnp.arange(query_rows, dtype=jnp.int32) // EXPERTS_PER_TOKEN
    cache_visible = jnp.broadcast_to(jnp.arange(CACHE_LENGTH, dtype=jnp.int32)[None, :] < length, (query_rows, CACHE_LENGTH))
    fresh_visible = jnp.arange(REQUEST_TOKENS, dtype=jnp.int32)[None, :] <= token_of_row[:, None]
    visible = jnp.concatenate([cache_visible, fresh_visible], axis=1)
    scores = jnp.where(visible, scores, masked_score)
    weights = jnp.exp(scores - lax.optimization_barrier(jnp.max(scores, axis=1, keepdims=True)))
    denominator = lax.optimization_barrier(jnp.sum(weights, axis=1, keepdims=True))
    summed = jnp.dot(weights.astype(jnp.bfloat16), values, preferred_element_type=jnp.float32)
    return (summed / denominator).astype(jnp.bfloat16)

def reference(tokens, gain, w_router, expert_query_weight, key_value_weight, expert_output_weight, cache_keys, cached_value_slots, lengths, deal, route):
    widened = tokens.astype(jnp.float32)
    inverse_root_mean = lax.rsqrt(lax.optimization_barrier(jnp.mean(widened * widened, axis=1)) + norm_eps)
    scaled_input = (widened * gain.astype(jnp.float32)[None, :]).astype(jnp.bfloat16)
    logits = jnp.dot(scaled_input, w_router, preferred_element_type=jnp.float32) * inverse_root_mean[:, None]
    onehot = (route[:, :, None] == jnp.arange(ATTENTION_EXPERTS, dtype=jnp.int32)[None, None, :]).astype(jnp.float32)
    chosen = lax.optimization_barrier(jnp.sum(onehot * logits[:, None, :], axis=2))
    gate_gap = chosen[:, 0] - chosen[:, 1]
    gate_weights = jnp.stack([jax.nn.sigmoid(gate_gap), jax.nn.sigmoid(-gate_gap)], axis=1).astype(jnp.bfloat16)
    flattened_query = expert_query_weight.reshape(ATTENTION_EXPERTS, MODEL_WIDTH, KEY_VALUE_HEADS * HEAD_SIZE)
    query_totals = jnp.zeros((TOKEN_COUNT, EXPERTS_PER_TOKEN, KEY_VALUE_HEADS * HEAD_SIZE), jnp.float32)
    for expert_index in range(ATTENTION_EXPERTS):
        projected = jnp.dot(scaled_input, flattened_query[expert_index], preferred_element_type=jnp.float32)
        query_totals = query_totals + onehot[:, :, expert_index][:, :, None] * projected[:, None, :]
    query_matrix = (query_totals * inverse_root_mean[:, None, None]).astype(jnp.bfloat16).reshape(TOKEN_COUNT, EXPERTS_PER_TOKEN, KEY_VALUE_HEADS, HEAD_SIZE)
    key_value_rows = jnp.dot(scaled_input, key_value_weight.reshape(MODEL_WIDTH, KEY_VALUE_HEADS * 2 * HEAD_SIZE), preferred_element_type=jnp.float32)
    key_value_rows = (key_value_rows * inverse_root_mean[:, None]).astype(jnp.bfloat16).reshape(TOKEN_COUNT, KEY_VALUE_HEADS, 2 * HEAD_SIZE)
    expert_parts = []
    for request in range(REQUEST_COUNT):
        request_token_rows = slice(request * REQUEST_TOKENS, (request + 1) * REQUEST_TOKENS)
        cache_slot = deal[request]
        length = lengths[request]
        query_by_head = jnp.transpose(query_matrix[request_token_rows], (2, 0, 1, 3)).reshape(KEY_VALUE_HEADS, REQUEST_TOKENS * EXPERTS_PER_TOKEN, HEAD_SIZE)
        fresh_keyval = jnp.transpose(key_value_rows[request_token_rows], (1, 0, 2))
        operand_set = (query_by_head, cache_keys[cache_slot], cached_value_slots[cache_slot], fresh_keyval[:, :, :HEAD_SIZE], fresh_keyval[:, :, HEAD_SIZE:])
        layer_output = lax.map(lambda member: attend_head(member, length), operand_set)
        expert_parts.append(jnp.transpose(layer_output.reshape(KEY_VALUE_HEADS, REQUEST_TOKENS, EXPERTS_PER_TOKEN, HEAD_SIZE), (1, 2, 0, 3)))
    attended_output = jnp.concatenate(expert_parts, axis=0).reshape(TOKEN_COUNT * EXPERTS_PER_TOKEN, KEY_VALUE_HEADS * HEAD_SIZE)
    mixing = onehot * gate_weights.astype(jnp.float32)[:, :, None]
    output_sum = jnp.zeros((TOKEN_COUNT, MODEL_WIDTH), jnp.float32)
    for expert_index in range(ATTENTION_EXPERTS):
        expert_output = jnp.dot(attended_output, expert_output_weight[expert_index].reshape(KEY_VALUE_HEADS * HEAD_SIZE, MODEL_WIDTH), preferred_element_type=jnp.float32).reshape(TOKEN_COUNT, EXPERTS_PER_TOKEN, MODEL_WIDTH)
        output_sum = output_sum + lax.optimization_barrier(jnp.sum(mixing[:, :, expert_index][:, :, None] * expert_output, axis=1))
    return output_sum.astype(jnp.bfloat16)
```

```python
import jax
import jax.numpy as jnp
from jax import lax
from jax.sharding import PartitionSpec as P

masked_score = -1e30
norm_eps = 1e-06
LANES = 128


def expert_onehot(route_rows, experts):
    return (route_rows[:, :, None] == jnp.arange(experts, dtype=jnp.int32)[None, None, :]).astype(
        jnp.float32
    )


def padded_width(width):
    return -(-width // LANES) * LANES


def scatter_sum(part, axis_name):
    members = lax.axis_size(axis_name)
    blocks = lax.all_to_all(
        part.reshape((members, part.shape[0] // members) + part.shape[1:]),
        axis_name,
        0,
        0,
        tiled=True,
    )
    return jnp.sum(blocks, axis=0)


def gather_rows(piece, axis_name):
    members = lax.axis_size(axis_name)
    copies = jnp.broadcast_to(piece[None], (members,) + piece.shape)
    gathered = lax.all_to_all(copies, axis_name, 0, 0, tiled=True)
    return gathered.reshape((members * piece.shape[0],) + piece.shape[1:])


def absorb(carry_state, scores, value_rows):
    running_max, running_sum, accumulated = carry_state
    new_max = jnp.maximum(running_max, jnp.max(scores, axis=2))
    shrink = jnp.exp(running_max - new_max)
    weights = jnp.exp(scores - new_max[:, :, None])
    running_sum = running_sum * shrink + jnp.sum(weights, axis=2)
    accumulated = accumulated * shrink[:, :, None] + jnp.einsum(
        "hrk,hkd->hrd", weights.astype(jnp.bfloat16), value_rows, preferred_element_type=jnp.float32
    )
    return (new_max, running_sum, accumulated)


def per_device(
    tokens,
    gain,
    w_router,
    expert_query_weight,
    key_value_weight,
    expert_output_weight,
    cache_keys,
    cached_value_slots,
    lengths,
    deal,
    route,
):
    requests = lengths.shape[0]
    experts = expert_query_weight.shape[0]
    heads_local = expert_query_weight.shape[2]
    head_dim = expert_query_weight.shape[3]
    top_count = route.shape[1]
    gathered = lax.all_gather(tokens, "gy", axis=0, tiled=True)
    total_rows, local_width = gathered.shape
    new_len = total_rows // requests
    full_width = local_width * lax.axis_size("gx")
    slot_index = lax.axis_index("gx")
    inverse = jnp.zeros((requests,), jnp.int32).at[deal].set(jnp.arange(requests, dtype=jnp.int32))
    ordered = jnp.take(gathered.reshape(requests, new_len, local_width), inverse, axis=0).reshape(
        total_rows, local_width
    )
    slot_route = jnp.take(route.reshape(requests, new_len, top_count), inverse, axis=0).reshape(
        total_rows, top_count
    )
    slot_onehot = expert_onehot(slot_route, experts)
    widened = ordered.astype(jnp.float32)
    squares = jnp.sum(widened * widened, axis=1)
    scaled_input = (widened * gain.astype(jnp.float32)[None, :]).astype(jnp.bfloat16)
    router_part = jnp.dot(scaled_input, w_router, preferred_element_type=jnp.float32)
    chosen_part = jnp.sum(slot_onehot * router_part[:, None, :], axis=2)
    routed_input = scaled_input[:, None, None, :] * slot_onehot[:, :, :, None].astype(jnp.bfloat16)
    query_part = jnp.einsum(
        "tsed,edhk->tshk", routed_input, expert_query_weight, preferred_element_type=jnp.float32
    )
    keyval_part = jnp.einsum(
        "td,dhk->thk", scaled_input, key_value_weight, preferred_element_type=jnp.float32
    )
    query_cols = top_count * heads_local * head_dim
    keyval_cols = heads_local * 2 * head_dim
    small_cols = top_count + 1
    packed_cols = query_cols + keyval_cols + padded_width(small_cols)
    packed = jnp.concatenate(
        [
            query_part.reshape(total_rows, query_cols),
            keyval_part.reshape(total_rows, keyval_cols),
            chosen_part,
            squares[:, None],
            jnp.zeros((total_rows, padded_width(small_cols) - small_cols), jnp.float32),
        ],
        axis=1,
    )
    summed = scatter_sum(packed, "gx")
    query_totals = summed[:, :query_cols].reshape(new_len, top_count, heads_local, head_dim)
    keyval_sums = summed[:, query_cols : query_cols + keyval_cols].reshape(
        new_len, heads_local, 2 * head_dim
    )
    chosen_sums = summed[:, query_cols + keyval_cols : query_cols + keyval_cols + top_count]
    square_sums = summed[:, query_cols + keyval_cols + top_count]
    inverse_root_mean = lax.rsqrt(square_sums / full_width + norm_eps)
    chosen = chosen_sums * inverse_root_mean[:, None]
    gate_gap = chosen[:, 0] - chosen[:, 1]
    gate_weights = jnp.stack([jax.nn.sigmoid(gate_gap), jax.nn.sigmoid(-gate_gap)], axis=1).astype(
        jnp.bfloat16
    )
    query_matrix = (query_totals * inverse_root_mean[:, None, None, None]).astype(jnp.bfloat16)
    key_value_rows = (keyval_sums * inverse_root_mean[:, None, None]).astype(jnp.bfloat16)
    query_rows = new_len * top_count
    query_by_head = jnp.transpose(query_matrix, (2, 0, 1, 3)).reshape(
        heads_local, query_rows, head_dim
    )
    fresh_keyval = jnp.transpose(key_value_rows, (1, 0, 2))
    fresh_keys = fresh_keyval[:, :, :head_dim]
    fresh_values = fresh_keyval[:, :, head_dim:]
    length = jnp.take(lengths, jnp.take(inverse, slot_index))
    local_keys = cache_keys[0]
    local_values = cached_value_slots[0]
    cache_span = local_keys.shape[1]
    key_block = min(1024, cache_span)
    score_scale = head_dim ** (-0.5)
    initial = (
        jnp.full((heads_local, query_rows), masked_score, jnp.float32),
        jnp.zeros((heads_local, query_rows), jnp.float32),
        jnp.zeros((heads_local, query_rows, head_dim), jnp.float32),
    )

    def visit_block(block_index, carry_state):
        first_key = block_index * key_block
        key_rows = lax.dynamic_slice_in_dim(local_keys, first_key, key_block, 1)
        value_rows = lax.dynamic_slice_in_dim(local_values, first_key, key_block, 1)
        scores = (
            jnp.einsum("hrd,hkd->hrk", query_by_head, key_rows, preferred_element_type=jnp.float32)
            * score_scale
        )
        visible = first_key + jnp.arange(key_block, dtype=jnp.int32) < length
        scores = jnp.where(visible[None, None, :], scores, masked_score)
        return absorb(carry_state, scores, value_rows)

    block_count = (length + key_block - 1) // key_block
    carry_state = lax.fori_loop(0, block_count, visit_block, initial)
    fresh_scores = (
        jnp.einsum("hrd,hkd->hrk", query_by_head, fresh_keys, preferred_element_type=jnp.float32)
        * score_scale
    )
    causal = (
        jnp.arange(new_len, dtype=jnp.int32)[None, :]
        <= (jnp.arange(query_rows, dtype=jnp.int32) // top_count)[:, None]
    )
    fresh_scores = jnp.where(causal[None], fresh_scores, masked_score)
    running_max, running_sum, accumulated = absorb(carry_state, fresh_scores, fresh_values)
    attended_output = (accumulated / running_sum[:, :, None]).astype(jnp.bfloat16)
    attended_output = jnp.transpose(
        attended_output.reshape(heads_local, new_len, top_count, head_dim), (1, 2, 0, 3)
    ).reshape(new_len, query_cols)
    shipped = jnp.concatenate(
        [
            attended_output,
            gate_weights,
            jnp.zeros((new_len, padded_width(top_count) - top_count), jnp.bfloat16),
        ],
        axis=1,
    )
    all_shipped = gather_rows(shipped, "gx")
    by_request = jnp.take(
        all_shipped.reshape(requests, new_len, all_shipped.shape[1]), deal, axis=0
    ).reshape(total_rows, all_shipped.shape[1])
    token_attended = by_request[:, :query_cols].reshape(total_rows, top_count, heads_local, head_dim)
    token_gates = by_request[:, query_cols : query_cols + top_count].astype(jnp.float32)
    onehot = expert_onehot(route, experts)
    routed_attended = token_attended[:, :, None, :, :] * onehot[:, :, :, None, None].astype(
        jnp.bfloat16
    )
    projected = jnp.einsum(
        "tsehk,ehko->tso", routed_attended, expert_output_weight, preferred_element_type=jnp.float32
    )
    mixed_part = jnp.sum(token_gates[:, :, None] * projected, axis=1)
    output_sum = scatter_sum(mixed_part, "gy")
    return output_sum.astype(jnp.bfloat16)


def solution(mesh):
    placed = (
        P("gy", "gx"),
        P("gx"),
        P("gx", None),
        P(None, "gx", "gy", None),
        P("gx", "gy", None),
        P(None, "gy", None, "gx"),
        P("gx", "gy", None, None),
        P("gx", "gy", None, None),
        P(),
        P(),
        P(),
    )
    return jax.shard_map(
        per_device, mesh=mesh, in_specs=placed, out_specs=P("gy", "gx"), check_vma=False
    )
```

```python
import jax
import jax.numpy as jnp
from jax import lax
from jax.experimental import pallas as pl
from jax.experimental.pallas import tpu as pltpu
from jax.sharding import PartitionSpec as P

masked_score = -1e30
norm_eps = 1e-06
LANES = 128


def expert_onehot(route_rows, experts):
    return (route_rows[:, :, None] == jnp.arange(experts, dtype=jnp.int32)[None, None, :]).astype(
        jnp.float32
    )


def padded_width(width):
    return -(-width // LANES) * LANES


def scatter_sum(part, axis_name):
    members = lax.axis_size(axis_name)
    blocks = lax.all_to_all(
        part.reshape((members, part.shape[0] // members) + part.shape[1:]),
        axis_name,
        0,
        0,
        tiled=True,
    )
    return jnp.sum(blocks, axis=0)


def gather_rows(piece, axis_name):
    members = lax.axis_size(axis_name)
    copies = jnp.broadcast_to(piece[None], (members,) + piece.shape)
    gathered = lax.all_to_all(copies, axis_name, 0, 0, tiled=True)
    return gathered.reshape((members * piece.shape[0],) + piece.shape[1:])


def pack_kernel(order_ref, tok_ref, gain_ref, router_ref, query_ref, keyval_ref, route_ref, out_ref):
    rows, width = tok_ref.shape
    experts = query_ref.shape[0]
    head_dim = query_ref.shape[2]
    keyval_cols = keyval_ref.shape[1]
    widened = tok_ref[...].astype(jnp.float32)
    squares = jnp.sum(widened * widened, axis=1, keepdims=True)
    scaled = (widened * gain_ref[...].astype(jnp.float32)).astype(jnp.bfloat16)
    logits = jnp.dot(scaled, router_ref[...], preferred_element_type=jnp.float32)
    first = route_ref[:, 0:1]
    second = route_ref[:, 1:2]
    expert_lane = lax.broadcasted_iota(jnp.int32, logits.shape, 1)
    chosen_first = jnp.sum(jnp.where(expert_lane == first, logits, 0.0), axis=1, keepdims=True)
    chosen_second = jnp.sum(jnp.where(expert_lane == second, logits, 0.0), axis=1, keepdims=True)
    query_first = jnp.zeros((rows, head_dim), jnp.float32)
    query_second = jnp.zeros((rows, head_dim), jnp.float32)
    for expert in range(experts):
        projected = jnp.dot(scaled, query_ref[expert], preferred_element_type=jnp.float32)
        query_first = query_first + jnp.where(first == expert, projected, 0.0)
        query_second = query_second + jnp.where(second == expert, projected, 0.0)
    keyval = jnp.dot(scaled, keyval_ref[...], preferred_element_type=jnp.float32)
    lane = lax.broadcasted_iota(jnp.int32, (rows, LANES), 1)
    small = jnp.where(
        lane == 0,
        chosen_first,
        jnp.where(lane == 1, chosen_second, jnp.where(lane == 2, squares, 0.0)),
    )
    out_ref[:, 0:head_dim] = query_first
    out_ref[:, head_dim : 2 * head_dim] = query_second
    out_ref[:, 2 * head_dim : 2 * head_dim + keyval_cols] = keyval
    out_ref[:, 2 * head_dim + keyval_cols :] = small


def packed_partials(order, gathered, gain, w_router, query_weight, keyval_weight, route):
    total_rows, width = gathered.shape
    requests = order.shape[0]
    rows = total_rows // requests
    experts, _, head_dim = query_weight.shape
    keyval_cols = keyval_weight.shape[1]
    packed_cols = 2 * head_dim + keyval_cols + LANES
    flops = 2 * total_rows * width * (experts * head_dim + keyval_cols + w_router.shape[1])
    moved = 2 * total_rows * width + 4 * total_rows * packed_cols + 2 * query_weight.size
    return pl.pallas_call(
        pack_kernel,
        out_shape=jax.ShapeDtypeStruct((total_rows, packed_cols), jnp.float32),
        grid_spec=pltpu.PrefetchScalarGridSpec(
            num_scalar_prefetch=1,
            grid=(requests,),
            in_specs=[
                pl.BlockSpec((rows, width), lambda s, order_ref: (order_ref[s], 0)),
                pl.BlockSpec((1, width), lambda s, order_ref: (0, 0)),
                pl.BlockSpec(w_router.shape, lambda s, order_ref: (0, 0)),
                pl.BlockSpec(query_weight.shape, lambda s, order_ref: (0, 0, 0)),
                pl.BlockSpec(keyval_weight.shape, lambda s, order_ref: (0, 0)),
                pl.BlockSpec((rows, route.shape[1]), lambda s, order_ref: (order_ref[s], 0)),
            ],
            out_specs=pl.BlockSpec((rows, packed_cols), lambda s, order_ref: (s, 0)),
        ),
        cost_estimate=pl.CostEstimate(flops=flops, transcendentals=0, bytes_accessed=moved),
    )(order, gathered, gain.reshape(1, width), w_router, query_weight, keyval_weight, route)


def absorb(carry_state, scores, value_rows):
    running_max, running_sum, accumulated = carry_state
    new_max = jnp.maximum(running_max, jnp.max(scores, axis=2))
    shrink = jnp.exp(running_max - new_max)
    weights = jnp.exp(scores - new_max[:, :, None])
    running_sum = running_sum * shrink + jnp.sum(weights, axis=2)
    accumulated = accumulated * shrink[:, :, None] + jnp.einsum(
        "hrk,hkd->hrd", weights.astype(jnp.bfloat16), value_rows, preferred_element_type=jnp.float32
    )
    return (new_max, running_sum, accumulated)


def per_device(
    tokens,
    gain,
    w_router,
    expert_query_weight,
    key_value_weight,
    expert_output_weight,
    cache_keys,
    cached_value_slots,
    lengths,
    deal,
    route,
):
    requests = lengths.shape[0]
    experts = expert_query_weight.shape[0]
    heads_local = expert_query_weight.shape[2]
    head_dim = expert_query_weight.shape[3]
    top_count = route.shape[1]
    gathered = lax.all_gather(tokens, "gy", axis=0, tiled=True)
    total_rows, local_width = gathered.shape
    new_len = total_rows // requests
    full_width = local_width * lax.axis_size("gx")
    slot_index = lax.axis_index("gx")
    inverse = jnp.zeros((requests,), jnp.int32).at[deal].set(jnp.arange(requests, dtype=jnp.int32))
    assert heads_local == 1
    packed = packed_partials(
        inverse,
        gathered,
        gain,
        w_router,
        expert_query_weight.reshape(experts, local_width, head_dim),
        key_value_weight.reshape(local_width, 2 * head_dim),
        route,
    )
    query_cols = top_count * heads_local * head_dim
    keyval_cols = heads_local * 2 * head_dim
    summed = scatter_sum(packed, "gx")
    query_totals = summed[:, :query_cols].reshape(new_len, top_count, heads_local, head_dim)
    keyval_sums = summed[:, query_cols : query_cols + keyval_cols].reshape(
        new_len, heads_local, 2 * head_dim
    )
    chosen_sums = summed[:, query_cols + keyval_cols : query_cols + keyval_cols + top_count]
    square_sums = summed[:, query_cols + keyval_cols + top_count]
    inverse_root_mean = lax.rsqrt(square_sums / full_width + norm_eps)
    chosen = chosen_sums * inverse_root_mean[:, None]
    gate_gap = chosen[:, 0] - chosen[:, 1]
    gate_weights = jnp.stack([jax.nn.sigmoid(gate_gap), jax.nn.sigmoid(-gate_gap)], axis=1).astype(
        jnp.bfloat16
    )
    query_matrix = (query_totals * inverse_root_mean[:, None, None, None]).astype(jnp.bfloat16)
    key_value_rows = (keyval_sums * inverse_root_mean[:, None, None]).astype(jnp.bfloat16)
    query_rows = new_len * top_count
    query_by_head = jnp.transpose(query_matrix, (2, 0, 1, 3)).reshape(
        heads_local, query_rows, head_dim
    )
    fresh_keyval = jnp.transpose(key_value_rows, (1, 0, 2))
    fresh_keys = fresh_keyval[:, :, :head_dim]
    fresh_values = fresh_keyval[:, :, head_dim:]
    length = jnp.take(lengths, jnp.take(inverse, slot_index))
    local_keys = cache_keys[0]
    local_values = cached_value_slots[0]
    cache_span = local_keys.shape[1]
    key_block = min(1024, cache_span)
    score_scale = head_dim ** (-0.5)
    initial = (
        jnp.full((heads_local, query_rows), masked_score, jnp.float32),
        jnp.zeros((heads_local, query_rows), jnp.float32),
        jnp.zeros((heads_local, query_rows, head_dim), jnp.float32),
    )

    def visit_block(block_index, carry_state):
        first_key = block_index * key_block
        key_rows = lax.dynamic_slice_in_dim(local_keys, first_key, key_block, 1)
        value_rows = lax.dynamic_slice_in_dim(local_values, first_key, key_block, 1)
        scores = (
            jnp.einsum("hrd,hkd->hrk", query_by_head, key_rows, preferred_element_type=jnp.float32)
            * score_scale
        )
        visible = first_key + jnp.arange(key_block, dtype=jnp.int32) < length
        scores = jnp.where(visible[None, None, :], scores, masked_score)
        return absorb(carry_state, scores, value_rows)

    block_count = (length + key_block - 1) // key_block
    carry_state = lax.fori_loop(0, block_count, visit_block, initial)
    fresh_scores = (
        jnp.einsum("hrd,hkd->hrk", query_by_head, fresh_keys, preferred_element_type=jnp.float32)
        * score_scale
    )
    causal = (
        jnp.arange(new_len, dtype=jnp.int32)[None, :]
        <= (jnp.arange(query_rows, dtype=jnp.int32) // top_count)[:, None]
    )
    fresh_scores = jnp.where(causal[None], fresh_scores, masked_score)
    running_max, running_sum, accumulated = absorb(carry_state, fresh_scores, fresh_values)
    attended_output = (accumulated / running_sum[:, :, None]).astype(jnp.bfloat16)
    attended_output = jnp.transpose(
        attended_output.reshape(heads_local, new_len, top_count, head_dim), (1, 2, 0, 3)
    ).reshape(new_len, query_cols)
    gate_row = jnp.transpose(gate_weights).reshape(1, top_count * new_len)
    assert gate_row.shape[1] <= query_cols
    extra_rows = 8
    shipped = jnp.concatenate(
        [
            attended_output,
            jnp.pad(gate_row, ((0, extra_rows - 1), (0, query_cols - gate_row.shape[1]))),
        ],
        axis=0,
    )
    all_shipped = gather_rows(shipped, "gx").reshape(requests, new_len + extra_rows, query_cols)
    by_request = jnp.take(all_shipped, deal, axis=0)
    token_attended = by_request[:, :new_len].reshape(total_rows, top_count, heads_local, head_dim)
    token_gates = (
        jnp.transpose(
            by_request[:, new_len, : top_count * new_len].reshape(requests, top_count, new_len),
            (0, 2, 1),
        )
        .reshape(total_rows, top_count)
        .astype(jnp.float32)
    )
    onehot = expert_onehot(route, experts)
    routed_attended = token_attended[:, :, None, :, :] * onehot[:, :, :, None, None].astype(
        jnp.bfloat16
    )
    projected = jnp.einsum(
        "tsehk,ehko->tso", routed_attended, expert_output_weight, preferred_element_type=jnp.float32
    )
    mixed_part = jnp.sum(token_gates[:, :, None] * projected, axis=1)
    output_sum = scatter_sum(mixed_part, "gy")
    return output_sum.astype(jnp.bfloat16)


def solution(mesh):
    placed = (
        P("gy", "gx"),
        P("gx"),
        P("gx", None),
        P(None, "gx", "gy", None),
        P("gx", "gy", None),
        P(None, "gy", None, "gx"),
        P("gx", "gy", None, None),
        P("gx", "gy", None, None),
        P(),
        P(),
        P(),
    )
    return jax.shard_map(
        per_device, mesh=mesh, in_specs=placed, out_specs=P("gy", "gx"), check_vma=False
    )
```

```python
import jax
import jax.numpy as jnp
from jax import lax
from jax.experimental import pallas as pl
from jax.experimental.pallas import tpu as pltpu
from jax.sharding import Mesh, PartitionSpec as P

masked_score = -1e30
norm_eps = 1e-06
LANES = 128


def expert_onehot(route_rows, experts):
    return (route_rows[:, :, None] == jnp.arange(experts, dtype=jnp.int32)[None, None, :]).astype(
        jnp.float32
    )


def padded_width(width):
    return -(-width // LANES) * LANES


def scatter_sum(part, axis_name):
    members = lax.axis_size(axis_name)
    blocks = lax.all_to_all(
        part.reshape((members, part.shape[0] // members) + part.shape[1:]),
        axis_name,
        0,
        0,
        tiled=True,
    )
    return jnp.sum(blocks, axis=0)


def gather_rows(piece, axis_name):
    members = lax.axis_size(axis_name)
    copies = jnp.broadcast_to(piece[None], (members,) + piece.shape)
    gathered = lax.all_to_all(copies, axis_name, 0, 0, tiled=True)
    return gathered.reshape((members * piece.shape[0],) + piece.shape[1:])


def pack_kernel(
    order_ref, tok_ref, gain_ref, router_ref, query_ref, keyval_ref, route_ref, route_t_ref, out_ref
):
    width = tok_ref.shape[1]
    rows = tok_ref.shape[0]
    experts = query_ref.shape[0]
    head_dim = query_ref.shape[2]
    keyval_cols = keyval_ref.shape[1]
    widened = tok_ref[...].astype(jnp.float32)
    scaled = (widened * gain_ref[...].astype(jnp.float32)).astype(jnp.bfloat16)
    first = route_ref[:, 0:1]
    second = route_ref[:, 1:2]
    query_first = jnp.zeros((rows, head_dim), jnp.float32)
    query_second = jnp.zeros((rows, head_dim), jnp.float32)
    for expert in range(experts):
        projected = jnp.dot(scaled, query_ref[expert], preferred_element_type=jnp.float32)
        query_first = query_first + jnp.where(first == expert, projected, 0.0)
        query_second = query_second + jnp.where(second == expert, projected, 0.0)
    keyval = jnp.dot(scaled, keyval_ref[...], preferred_element_type=jnp.float32)
    out_ref[0:rows, 0:head_dim] = query_first
    out_ref[0:rows, head_dim : 2 * head_dim] = query_second
    out_ref[0:rows, 2 * head_dim : 2 * head_dim + keyval_cols] = keyval
    widened_t = jnp.transpose(widened)
    squares_row = jnp.sum(widened_t * widened_t, axis=0, keepdims=True)
    logits_t = lax.dot_general(
        router_ref[...], scaled, (((1,), (1,)), ((), ())), preferred_element_type=jnp.float32
    )
    expert_row = lax.broadcasted_iota(jnp.int32, logits_t.shape, 0)
    route_t = route_t_ref[...]
    chosen_first = jnp.sum(jnp.where(expert_row == route_t[0:1, :], logits_t, 0.0), axis=0, keepdims=True)
    chosen_second = jnp.sum(jnp.where(expert_row == route_t[1:2, :], logits_t, 0.0), axis=0, keepdims=True)
    extra = out_ref.shape[0] - rows
    out_ref[rows:, :] = jnp.zeros((extra, out_ref.shape[1]), jnp.float32)
    out_ref[rows : rows + 1, 0:rows] = chosen_first
    out_ref[rows : rows + 1, rows : 2 * rows] = chosen_second
    out_ref[rows : rows + 1, 2 * rows : 3 * rows] = squares_row


EXTRA_ROWS = 8


def packed_partials(order, gathered, gain, w_router, query_weight, keyval_weight, route):
    total_rows, width = gathered.shape
    requests = order.shape[0]
    rows = total_rows // requests
    experts, _, head_dim = query_weight.shape
    keyval_cols = keyval_weight.shape[1]
    packed_cols = 2 * head_dim + keyval_cols
    assert 3 * rows <= packed_cols
    block_rows = rows + EXTRA_ROWS
    flops = 2 * total_rows * width * (experts * head_dim + keyval_cols + w_router.shape[1])
    moved = 2 * total_rows * width + 4 * requests * block_rows * packed_cols + 2 * query_weight.size
    return pl.pallas_call(
        pack_kernel,
        out_shape=jax.ShapeDtypeStruct((requests * block_rows, packed_cols), jnp.float32),
        grid_spec=pltpu.PrefetchScalarGridSpec(
            num_scalar_prefetch=1,
            grid=(requests,),
            in_specs=[
                pl.BlockSpec((rows, width), lambda s, order_ref: (order_ref[s], 0)),
                pl.BlockSpec((1, width), lambda s, order_ref: (0, 0)),
                pl.BlockSpec((w_router.shape[1], width), lambda s, order_ref: (0, 0)),
                pl.BlockSpec(query_weight.shape, lambda s, order_ref: (0, 0, 0)),
                pl.BlockSpec(keyval_weight.shape, lambda s, order_ref: (0, 0)),
                pl.BlockSpec((rows, route.shape[1]), lambda s, order_ref: (order_ref[s], 0)),
                pl.BlockSpec((route.shape[1], rows), lambda s, order_ref: (0, order_ref[s])),
            ],
            out_specs=pl.BlockSpec((block_rows, packed_cols), lambda s, order_ref: (s, 0)),
        ),
        cost_estimate=pl.CostEstimate(flops=flops, transcendentals=0, bytes_accessed=moved),
    )(order, gathered, gain.reshape(1, width), jnp.transpose(w_router), query_weight, keyval_weight, route, jnp.transpose(route))


def absorb(carry_state, scores, value_rows):
    running_max, running_sum, accumulated = carry_state
    new_max = jnp.maximum(running_max, jnp.max(scores, axis=2))
    shrink = jnp.exp(running_max - new_max)
    weights = jnp.exp(scores - new_max[:, :, None])
    running_sum = running_sum * shrink + jnp.sum(weights, axis=2)
    accumulated = accumulated * shrink[:, :, None] + jnp.einsum(
        "hrk,hkd->hrd", weights.astype(jnp.bfloat16), value_rows, preferred_element_type=jnp.float32
    )
    return (new_max, running_sum, accumulated)


def per_device(
    tokens,
    gain,
    w_router,
    expert_query_weight,
    key_value_weight,
    expert_output_weight,
    cache_keys,
    cached_value_slots,
    lengths,
    deal,
    route,
):
    requests = lengths.shape[0]
    experts = expert_query_weight.shape[0]
    heads_local = expert_query_weight.shape[2]
    head_dim = expert_query_weight.shape[3]
    top_count = route.shape[1]
    gathered = lax.all_gather(tokens, TOKEN_AXES, axis=0, tiled=True)
    total_rows, local_width = gathered.shape
    new_len = total_rows // requests
    full_width = local_width * lax.axis_size("gx")
    slot_index = lax.axis_index("gx")
    inverse = jnp.zeros((requests,), jnp.int32).at[deal].set(jnp.arange(requests, dtype=jnp.int32))
    assert heads_local == 1
    packed = packed_partials(
        inverse,
        gathered,
        gain,
        w_router,
        expert_query_weight.reshape(experts, local_width, head_dim),
        key_value_weight.reshape(local_width, 2 * head_dim),
        route,
    )
    query_cols = top_count * heads_local * head_dim
    keyval_cols = heads_local * 2 * head_dim
    summed = scatter_sum(packed, "gx")
    query_totals = summed[:new_len, :query_cols].reshape(new_len, top_count, heads_local, head_dim)
    keyval_sums = summed[:new_len, query_cols : query_cols + keyval_cols].reshape(
        new_len, heads_local, 2 * head_dim
    )
    chosen_sums = jnp.transpose(summed[new_len, : top_count * new_len].reshape(top_count, new_len))
    square_sums = summed[new_len, top_count * new_len : (top_count + 1) * new_len]
    inverse_root_mean = lax.rsqrt(square_sums / full_width + norm_eps)
    chosen = chosen_sums * inverse_root_mean[:, None]
    gate_gap = chosen[:, 0] - chosen[:, 1]
    gate_weights = jnp.stack([jax.nn.sigmoid(gate_gap), jax.nn.sigmoid(-gate_gap)], axis=1).astype(
        jnp.bfloat16
    )
    query_matrix = (query_totals * inverse_root_mean[:, None, None, None]).astype(jnp.bfloat16)
    key_value_rows = (keyval_sums * inverse_root_mean[:, None, None]).astype(jnp.bfloat16)
    query_rows = new_len * top_count
    query_by_head = jnp.transpose(query_matrix, (2, 0, 1, 3)).reshape(
        heads_local, query_rows, head_dim
    )
    fresh_keyval = jnp.transpose(key_value_rows, (1, 0, 2))
    fresh_keys = fresh_keyval[:, :, :head_dim]
    fresh_values = fresh_keyval[:, :, head_dim:]
    length = jnp.take(lengths, jnp.take(inverse, slot_index))
    local_keys = cache_keys[0]
    local_values = cached_value_slots[0]
    cache_span = local_keys.shape[1]
    key_block = min(1024, cache_span)
    score_scale = head_dim ** (-0.5)
    initial = (
        jnp.full((heads_local, query_rows), masked_score, jnp.float32),
        jnp.zeros((heads_local, query_rows), jnp.float32),
        jnp.zeros((heads_local, query_rows, head_dim), jnp.float32),
    )

    def visit_block(block_index, carry_state):
        first_key = block_index * key_block
        key_rows = lax.dynamic_slice_in_dim(local_keys, first_key, key_block, 1)
        value_rows = lax.dynamic_slice_in_dim(local_values, first_key, key_block, 1)
        scores = (
            jnp.einsum("hrd,hkd->hrk", query_by_head, key_rows, preferred_element_type=jnp.float32)
            * score_scale
        )
        visible = first_key + jnp.arange(key_block, dtype=jnp.int32) < length
        scores = jnp.where(visible[None, None, :], scores, masked_score)
        return absorb(carry_state, scores, value_rows)

    block_count = (length + key_block - 1) // key_block
    carry_state = lax.fori_loop(0, block_count, visit_block, initial)
    fresh_scores = (
        jnp.einsum("hrd,hkd->hrk", query_by_head, fresh_keys, preferred_element_type=jnp.float32)
        * score_scale
    )
    causal = (
        jnp.arange(new_len, dtype=jnp.int32)[None, :]
        <= (jnp.arange(query_rows, dtype=jnp.int32) // top_count)[:, None]
    )
    fresh_scores = jnp.where(causal[None], fresh_scores, masked_score)
    running_max, running_sum, accumulated = absorb(carry_state, fresh_scores, fresh_values)
    attended_output = (accumulated / running_sum[:, :, None]).astype(jnp.bfloat16)
    attended_output = jnp.transpose(
        attended_output.reshape(heads_local, new_len, top_count, head_dim), (1, 2, 0, 3)
    ).reshape(new_len, query_cols)
    gate_row = jnp.transpose(gate_weights).reshape(1, top_count * new_len)
    assert gate_row.shape[1] <= query_cols
    extra_rows = 8
    shipped = jnp.concatenate(
        [
            attended_output,
            jnp.pad(gate_row, ((0, extra_rows - 1), (0, query_cols - gate_row.shape[1]))),
        ],
        axis=0,
    )
    all_shipped = gather_rows(shipped, "gx").reshape(requests, new_len + extra_rows, query_cols)
    cores = lax.axis_size("cc")
    chips = lax.axis_size("zz")
    staged = jnp.arange(requests, dtype=jnp.int32).reshape(chips, cores).T.reshape(requests)
    by_request = jnp.take(all_shipped, jnp.take(deal, staged), axis=0)
    route = jnp.take(route.reshape(requests, new_len, top_count), staged, axis=0).reshape(
        total_rows, top_count
    )
    token_attended = by_request[:, :new_len].reshape(total_rows, top_count, heads_local, head_dim)
    token_gates = (
        jnp.transpose(
            by_request[:, new_len, : top_count * new_len].reshape(requests, top_count, new_len),
            (0, 2, 1),
        )
        .reshape(total_rows, top_count)
        .astype(jnp.float32)
    )
    onehot = expert_onehot(route, experts)
    routed_attended = token_attended[:, :, None, :, :] * onehot[:, :, :, None, None].astype(
        jnp.bfloat16
    )
    projected = jnp.einsum(
        "tsehk,ehko->tso", routed_attended, expert_output_weight, preferred_element_type=jnp.float32
    )
    mixed_part = jnp.sum(token_gates[:, :, None] * projected, axis=1)
    output_sum = scatter_sum(scatter_sum(mixed_part, "cc"), "zz")
    return output_sum.astype(jnp.bfloat16)


TOKEN_AXES = ("zz", "cc")


def solution(mesh):
    gx_size, gy_size = mesh.devices.shape
    staged_mesh = Mesh(mesh.devices.reshape(gx_size, gy_size // 2, 2), ("gx",) + TOKEN_AXES)
    gy = TOKEN_AXES
    placed = (
        P(gy, "gx"),
        P("gx"),
        P("gx", None),
        P(None, "gx", gy, None),
        P("gx", gy, None),
        P(None, gy, None, "gx"),
        P("gx", gy, None, None),
        P("gx", gy, None, None),
        P(),
        P(),
        P(),
    )
    return jax.shard_map(
        per_device, mesh=staged_mesh, in_specs=placed, out_specs=P(gy, "gx"), check_vma=False
    )
```

```python
import jax
import jax.numpy as jnp
from jax import lax
from jax.experimental import pallas as pl
from jax.experimental.pallas import tpu as pltpu
from jax.sharding import Mesh, PartitionSpec as P

masked_score = -1e30
norm_eps = 1e-06
LANES = 128


def expert_onehot(route_rows, experts):
    return (route_rows[:, :, None] == jnp.arange(experts, dtype=jnp.int32)[None, None, :]).astype(
        jnp.float32
    )


def padded_width(width):
    return -(-width // LANES) * LANES


def scatter_sum(part, axis_name):
    members = lax.axis_size(axis_name)
    blocks = lax.all_to_all(
        part.reshape((members, part.shape[0] // members) + part.shape[1:]),
        axis_name,
        0,
        0,
        tiled=True,
    )
    return jnp.sum(blocks, axis=0)


def gather_rows(piece, axis_name):
    members = lax.axis_size(axis_name)
    copies = jnp.broadcast_to(piece[None], (members,) + piece.shape)
    gathered = lax.all_to_all(copies, axis_name, 0, 0, tiled=True)
    return gathered.reshape((members * piece.shape[0],) + piece.shape[1:])


def pack_kernel(
    order_ref, tok_ref, gain_ref, router_ref, query_ref, keyval_ref, route_ref, route_t_ref, out_ref
):
    width = tok_ref.shape[1]
    rows = tok_ref.shape[0]
    experts = query_ref.shape[0]
    head_dim = query_ref.shape[2]
    keyval_cols = keyval_ref.shape[1]
    widened = tok_ref[...].astype(jnp.float32)
    scaled = (widened * gain_ref[...].astype(jnp.float32)).astype(jnp.bfloat16)
    first = route_ref[:, 0:1]
    second = route_ref[:, 1:2]
    query_first = jnp.zeros((rows, head_dim), jnp.float32)
    query_second = jnp.zeros((rows, head_dim), jnp.float32)
    for expert in range(experts):
        projected = jnp.dot(scaled, query_ref[expert], preferred_element_type=jnp.float32)
        query_first = query_first + jnp.where(first == expert, projected, 0.0)
        query_second = query_second + jnp.where(second == expert, projected, 0.0)
    keyval = jnp.dot(scaled, keyval_ref[...], preferred_element_type=jnp.float32)
    out_ref[0:rows, 0:head_dim] = query_first
    out_ref[0:rows, head_dim : 2 * head_dim] = query_second
    out_ref[0:rows, 2 * head_dim : 2 * head_dim + keyval_cols] = keyval
    widened_t = jnp.transpose(widened)
    squares_row = jnp.sum(widened_t * widened_t, axis=0, keepdims=True)
    logits_t = lax.dot_general(
        router_ref[...], scaled, (((1,), (1,)), ((), ())), preferred_element_type=jnp.float32
    )
    expert_row = lax.broadcasted_iota(jnp.int32, logits_t.shape, 0)
    route_t = route_t_ref[...]
    chosen_first = jnp.sum(jnp.where(expert_row == route_t[0:1, :], logits_t, 0.0), axis=0, keepdims=True)
    chosen_second = jnp.sum(jnp.where(expert_row == route_t[1:2, :], logits_t, 0.0), axis=0, keepdims=True)
    extra = out_ref.shape[0] - rows
    out_ref[rows:, :] = jnp.zeros((extra, out_ref.shape[1]), jnp.float32)
    out_ref[rows : rows + 1, 0:rows] = chosen_first
    out_ref[rows : rows + 1, rows : 2 * rows] = chosen_second
    out_ref[rows : rows + 1, 2 * rows : 3 * rows] = squares_row


EXTRA_ROWS = 8


def attend_kernel(length_ref, query_ref, cache_k_ref, cache_v_ref, fresh_ref, out_ref):
    rows, head_dim = query_ref.shape
    fresh_len = fresh_ref.shape[0]
    top_count = rows // fresh_len
    score_scale = head_dim ** (-0.5)
    contract_last = (((1,), (1,)), ((), ()))
    query = query_ref[...]
    cached = lax.dot_general(query, cache_k_ref[...], contract_last, preferred_element_type=jnp.float32)
    cached = cached * score_scale
    key_col = lax.broadcasted_iota(jnp.int32, cached.shape, 1)
    cached = jnp.where(key_col < length_ref[0], cached, masked_score)
    fresh_keys = fresh_ref[:, 0:head_dim]
    fresh_values = fresh_ref[:, head_dim : 2 * head_dim]
    fresh = lax.dot_general(query, fresh_keys, contract_last, preferred_element_type=jnp.float32)
    fresh = fresh * score_scale
    fresh_col = lax.broadcasted_iota(jnp.int32, fresh.shape, 1)
    query_token = lax.broadcasted_iota(jnp.int32, fresh.shape, 0) // top_count
    fresh = jnp.where(fresh_col <= query_token, fresh, masked_score)
    top = jnp.maximum(
        jnp.max(cached, axis=1, keepdims=True), jnp.max(fresh, axis=1, keepdims=True)
    )
    cached_weights = jnp.exp(cached - top)
    fresh_weights = jnp.exp(fresh - top)
    denominator = jnp.sum(cached_weights, axis=1, keepdims=True) + jnp.sum(
        fresh_weights, axis=1, keepdims=True
    )
    summed = jnp.dot(
        cached_weights.astype(jnp.bfloat16), cache_v_ref[...], preferred_element_type=jnp.float32
    ) + jnp.dot(fresh_weights.astype(jnp.bfloat16), fresh_values, preferred_element_type=jnp.float32)
    out_ref[...] = (summed / denominator).astype(jnp.bfloat16)


def attend(length, query, cache_k, cache_v, fresh):
    rows, head_dim = query.shape
    span = cache_k.shape[0]
    full = lambda shape: pl.BlockSpec(shape, lambda i, length_ref: (0,) * len(shape))
    keys = span + fresh.shape[0]
    return pl.pallas_call(
        attend_kernel,
        out_shape=jax.ShapeDtypeStruct((rows, head_dim), jnp.bfloat16),
        grid_spec=pltpu.PrefetchScalarGridSpec(
            num_scalar_prefetch=1,
            grid=(1,),
            in_specs=[full(query.shape), full(cache_k.shape), full(cache_v.shape), full(fresh.shape)],
            out_specs=full((rows, head_dim)),
        ),
        cost_estimate=pl.CostEstimate(
            flops=4 * rows * keys * head_dim,
            transcendentals=rows * keys,
            bytes_accessed=2 * (2 * span * head_dim + 2 * rows * head_dim + fresh.size),
        ),
    )(length.reshape(1), query, cache_k, cache_v, fresh)


def packed_partials(order, gathered, gain, w_router, query_weight, keyval_weight, route):
    total_rows, width = gathered.shape
    requests = order.shape[0]
    rows = total_rows // requests
    experts, _, head_dim = query_weight.shape
    keyval_cols = keyval_weight.shape[1]
    packed_cols = 2 * head_dim + keyval_cols
    assert 3 * rows <= packed_cols
    block_rows = rows + EXTRA_ROWS
    flops = 2 * total_rows * width * (experts * head_dim + keyval_cols + w_router.shape[1])
    moved = 2 * total_rows * width + 4 * requests * block_rows * packed_cols + 2 * query_weight.size
    return pl.pallas_call(
        pack_kernel,
        out_shape=jax.ShapeDtypeStruct((requests * block_rows, packed_cols), jnp.float32),
        grid_spec=pltpu.PrefetchScalarGridSpec(
            num_scalar_prefetch=1,
            grid=(requests,),
            in_specs=[
                pl.BlockSpec((rows, width), lambda s, order_ref: (order_ref[s], 0)),
                pl.BlockSpec((1, width), lambda s, order_ref: (0, 0)),
                pl.BlockSpec((w_router.shape[1], width), lambda s, order_ref: (0, 0)),
                pl.BlockSpec(query_weight.shape, lambda s, order_ref: (0, 0, 0)),
                pl.BlockSpec(keyval_weight.shape, lambda s, order_ref: (0, 0)),
                pl.BlockSpec((rows, route.shape[1]), lambda s, order_ref: (order_ref[s], 0)),
                pl.BlockSpec((route.shape[1], rows), lambda s, order_ref: (0, order_ref[s])),
            ],
            out_specs=pl.BlockSpec((block_rows, packed_cols), lambda s, order_ref: (s, 0)),
        ),
        cost_estimate=pl.CostEstimate(flops=flops, transcendentals=0, bytes_accessed=moved),
    )(order, gathered, gain.reshape(1, width), jnp.transpose(w_router), query_weight, keyval_weight, route, jnp.transpose(route))


def per_device(
    tokens,
    gain,
    w_router,
    expert_query_weight,
    key_value_weight,
    expert_output_weight,
    cache_keys,
    cached_value_slots,
    lengths,
    deal,
    route,
):
    requests = lengths.shape[0]
    experts = expert_query_weight.shape[0]
    heads_local = expert_query_weight.shape[2]
    head_dim = expert_query_weight.shape[3]
    top_count = route.shape[1]
    gathered = lax.all_gather(tokens, TOKEN_AXES, axis=0, tiled=True)
    total_rows, local_width = gathered.shape
    new_len = total_rows // requests
    full_width = local_width * lax.axis_size("gx")
    slot_index = lax.axis_index("gx")
    inverse = jnp.zeros((requests,), jnp.int32).at[deal].set(jnp.arange(requests, dtype=jnp.int32))
    assert heads_local == 1
    packed = packed_partials(
        inverse,
        gathered,
        gain,
        w_router,
        expert_query_weight.reshape(experts, local_width, head_dim),
        key_value_weight.reshape(local_width, 2 * head_dim),
        route,
    )
    query_cols = top_count * heads_local * head_dim
    keyval_cols = heads_local * 2 * head_dim
    summed = scatter_sum(packed, "gx")
    query_totals = summed[:new_len, :query_cols].reshape(new_len, top_count, heads_local, head_dim)
    keyval_sums = summed[:new_len, query_cols : query_cols + keyval_cols].reshape(
        new_len, heads_local, 2 * head_dim
    )
    chosen_sums = jnp.transpose(summed[new_len, : top_count * new_len].reshape(top_count, new_len))
    square_sums = summed[new_len, top_count * new_len : (top_count + 1) * new_len]
    inverse_root_mean = lax.rsqrt(square_sums / full_width + norm_eps)
    chosen = chosen_sums * inverse_root_mean[:, None]
    gate_gap = chosen[:, 0] - chosen[:, 1]
    gate_weights = jnp.stack([jax.nn.sigmoid(gate_gap), jax.nn.sigmoid(-gate_gap)], axis=1).astype(
        jnp.bfloat16
    )
    query_matrix = (query_totals * inverse_root_mean[:, None, None, None]).astype(jnp.bfloat16)
    key_value_rows = (keyval_sums * inverse_root_mean[:, None, None]).astype(jnp.bfloat16)
    query_rows = new_len * top_count
    length = jnp.take(lengths, jnp.take(inverse, slot_index))
    attended_output = attend(
        length,
        query_matrix.reshape(query_rows, head_dim),
        cache_keys[0, 0],
        cached_value_slots[0, 0],
        key_value_rows.reshape(new_len, 2 * head_dim),
    ).reshape(new_len, query_cols)
    gate_row = jnp.transpose(gate_weights).reshape(1, top_count * new_len)
    assert gate_row.shape[1] <= query_cols
    extra_rows = 8
    shipped = jnp.concatenate(
        [
            attended_output,
            jnp.pad(gate_row, ((0, extra_rows - 1), (0, query_cols - gate_row.shape[1]))),
        ],
        axis=0,
    )
    all_shipped = gather_rows(shipped, "gx").reshape(requests, new_len + extra_rows, query_cols)
    cores = lax.axis_size("cc")
    chips = lax.axis_size("zz")
    staged = jnp.arange(requests, dtype=jnp.int32).reshape(chips, cores).T.reshape(requests)
    by_request = jnp.take(all_shipped, jnp.take(deal, staged), axis=0)
    route = jnp.take(route.reshape(requests, new_len, top_count), staged, axis=0).reshape(
        total_rows, top_count
    )
    token_attended = by_request[:, :new_len].reshape(total_rows, top_count, heads_local, head_dim)
    token_gates = (
        jnp.transpose(
            by_request[:, new_len, : top_count * new_len].reshape(requests, top_count, new_len),
            (0, 2, 1),
        )
        .reshape(total_rows, top_count)
        .astype(jnp.float32)
    )
    onehot = expert_onehot(route, experts)
    routed_attended = token_attended[:, :, None, :, :] * onehot[:, :, :, None, None].astype(
        jnp.bfloat16
    )
    projected = jnp.einsum(
        "tsehk,ehko->tso", routed_attended, expert_output_weight, preferred_element_type=jnp.float32
    )
    mixed_part = jnp.sum(token_gates[:, :, None] * projected, axis=1)
    output_sum = scatter_sum(scatter_sum(mixed_part, "cc"), "zz")
    return output_sum.astype(jnp.bfloat16)


TOKEN_AXES = ("zz", "cc")


def solution(mesh):
    gx_size, gy_size = mesh.devices.shape
    staged_mesh = Mesh(mesh.devices.reshape(gx_size, gy_size // 2, 2), ("gx",) + TOKEN_AXES)
    gy = TOKEN_AXES
    placed = (
        P(gy, "gx"),
        P("gx"),
        P("gx", None),
        P(None, "gx", gy, None),
        P("gx", gy, None),
        P(None, gy, None, "gx"),
        P("gx", gy, None, None),
        P("gx", gy, None, None),
        P(),
        P(),
        P(),
    )
    return jax.shard_map(
        per_device, mesh=staged_mesh, in_specs=placed, out_specs=P(gy, "gx"), check_vma=False
    )
```

```python
import jax
import jax.numpy as jnp
from jax import lax
from jax.experimental import pallas as pl
from jax.experimental.pallas import tpu as pltpu
from jax.sharding import Mesh, PartitionSpec as P

masked_score = -1e30
norm_eps = 1e-06
LANES = 128


def expert_onehot(route_rows, experts):
    return (route_rows[:, :, None] == jnp.arange(experts, dtype=jnp.int32)[None, None, :]).astype(
        jnp.float32
    )


def padded_width(width):
    return -(-width // LANES) * LANES


def scatter_sum(part, axis_name):
    members = lax.axis_size(axis_name)
    blocks = lax.all_to_all(
        part.reshape((members, part.shape[0] // members) + part.shape[1:]),
        axis_name,
        0,
        0,
        tiled=True,
    )
    return jnp.sum(blocks, axis=0)


def gather_rows(piece, axis_name):
    members = lax.axis_size(axis_name)
    copies = jnp.broadcast_to(piece[None], (members,) + piece.shape)
    gathered = lax.all_to_all(copies, axis_name, 0, 0, tiled=True)
    return gathered.reshape((members * piece.shape[0],) + piece.shape[1:])


def pack_kernel(tok_ref, gain_ref, router_ref, weight_ref, route_ref, route_t_ref, out_ref):
    rows = route_t_ref.shape[2]
    block_rows = rows + EXTRA_ROWS
    per_step = tok_ref.shape[0] // rows
    head_dim = out_ref.shape[1] // 4
    experts = (weight_ref.shape[1] - 2 * head_dim) // head_dim
    widened = tok_ref[...].astype(jnp.float32)
    scaled = (widened * gain_ref[...].astype(jnp.float32)).astype(jnp.bfloat16)
    projected = jnp.dot(scaled, weight_ref[...], preferred_element_type=jnp.float32)
    first = route_ref[:, 0:1]
    second = route_ref[:, 1:2]
    query_first = jnp.zeros((tok_ref.shape[0], head_dim), jnp.float32)
    query_second = jnp.zeros((tok_ref.shape[0], head_dim), jnp.float32)
    for expert in range(experts):
        part = projected[:, expert * head_dim : (expert + 1) * head_dim]
        query_first = query_first + jnp.where(first == expert, part, 0.0)
        query_second = query_second + jnp.where(second == expert, part, 0.0)
    keyval = projected[:, experts * head_dim :]
    contract_last = (((1,), (1,)), ((), ()))
    for block in range(per_step):
        low = block * rows
        top = block * block_rows
        out_ref[top : top + rows, 0:head_dim] = query_first[low : low + rows]
        out_ref[top : top + rows, head_dim : 2 * head_dim] = query_second[low : low + rows]
        out_ref[top : top + rows, 2 * head_dim :] = keyval[low : low + rows]
        widened_t = jnp.transpose(widened[low : low + rows])
        squares_row = jnp.sum(widened_t * widened_t, axis=0, keepdims=True)
        logits_t = lax.dot_general(
            router_ref[...], scaled[low : low + rows], contract_last, preferred_element_type=jnp.float32
        )
        expert_row = lax.broadcasted_iota(jnp.int32, logits_t.shape, 0)
        route_t = route_t_ref[block]
        chosen_first = jnp.sum(
            jnp.where(expert_row == route_t[0:1, :], logits_t, 0.0), axis=0, keepdims=True
        )
        chosen_second = jnp.sum(
            jnp.where(expert_row == route_t[1:2, :], logits_t, 0.0), axis=0, keepdims=True
        )
        out_ref[top + rows : top + block_rows, :] = jnp.zeros((EXTRA_ROWS, out_ref.shape[1]), jnp.float32)
        out_ref[top + rows : top + rows + 1, 0:rows] = chosen_first
        out_ref[top + rows : top + rows + 1, rows : 2 * rows] = chosen_second
        out_ref[top + rows : top + rows + 1, 2 * rows : 3 * rows] = squares_row


EXTRA_ROWS = 8
REQUESTS_PER_STEP = 4


def packed_partials(ordered, gain, w_router, query_weight, keyval_weight, route, requests):
    total_rows, width = ordered.shape
    rows = total_rows // requests
    experts, _, head_dim = query_weight.shape
    keyval_cols = keyval_weight.shape[1]
    packed_cols = 2 * head_dim + keyval_cols
    assert 3 * rows <= packed_cols and keyval_cols == 2 * head_dim
    block_rows = rows + EXTRA_ROWS
    step_rows = REQUESTS_PER_STEP * rows
    weight = jnp.concatenate(
        [jnp.transpose(query_weight, (1, 0, 2)).reshape(width, experts * head_dim), keyval_weight],
        axis=1,
    )
    route_t = jnp.transpose(route.reshape(requests, rows, route.shape[1]), (0, 2, 1))
    flops = 2 * total_rows * width * (weight.shape[1] + w_router.shape[1])
    moved = 2 * total_rows * width + 4 * requests * block_rows * packed_cols + 2 * weight.size
    return pl.pallas_call(
        pack_kernel,
        out_shape=jax.ShapeDtypeStruct((requests * block_rows, packed_cols), jnp.float32),
        grid=(requests // REQUESTS_PER_STEP,),
        in_specs=[
            pl.BlockSpec((step_rows, width), lambda s: (s, 0)),
            pl.BlockSpec((1, width), lambda s: (0, 0)),
            pl.BlockSpec((w_router.shape[1], width), lambda s: (0, 0)),
            pl.BlockSpec(weight.shape, lambda s: (0, 0)),
            pl.BlockSpec((step_rows, route.shape[1]), lambda s: (s, 0)),
            pl.BlockSpec((REQUESTS_PER_STEP, route.shape[1], rows), lambda s: (s, 0, 0)),
        ],
        out_specs=pl.BlockSpec((REQUESTS_PER_STEP * block_rows, packed_cols), lambda s: (s, 0)),
        cost_estimate=pl.CostEstimate(flops=flops, transcendentals=0, bytes_accessed=moved),
    )(ordered, gain.reshape(1, width), jnp.transpose(w_router), weight, route, route_t)


def attend_kernel(length_ref, query_ref, cache_k_ref, cache_v_ref, fresh_ref, out_ref):
    rows, head_dim = query_ref.shape
    fresh_len = fresh_ref.shape[0]
    top_count = rows // fresh_len
    score_scale = head_dim ** (-0.5)
    contract_last = (((1,), (1,)), ((), ()))
    query = query_ref[...]
    cached = lax.dot_general(query, cache_k_ref[...], contract_last, preferred_element_type=jnp.float32)
    cached = cached * score_scale
    key_col = lax.broadcasted_iota(jnp.int32, cached.shape, 1)
    cached = jnp.where(key_col < length_ref[0], cached, masked_score)
    fresh_keys = fresh_ref[:, 0:head_dim]
    fresh_values = fresh_ref[:, head_dim : 2 * head_dim]
    fresh = lax.dot_general(query, fresh_keys, contract_last, preferred_element_type=jnp.float32)
    fresh = fresh * score_scale
    fresh_col = lax.broadcasted_iota(jnp.int32, fresh.shape, 1)
    query_token = lax.broadcasted_iota(jnp.int32, fresh.shape, 0) // top_count
    fresh = jnp.where(fresh_col <= query_token, fresh, masked_score)
    top = jnp.maximum(
        jnp.max(cached, axis=1, keepdims=True), jnp.max(fresh, axis=1, keepdims=True)
    )
    cached_weights = jnp.exp(cached - top)
    fresh_weights = jnp.exp(fresh - top)
    denominator = jnp.sum(cached_weights, axis=1, keepdims=True) + jnp.sum(
        fresh_weights, axis=1, keepdims=True
    )
    summed = jnp.dot(
        cached_weights.astype(jnp.bfloat16), cache_v_ref[...], preferred_element_type=jnp.float32
    ) + jnp.dot(fresh_weights.astype(jnp.bfloat16), fresh_values, preferred_element_type=jnp.float32)
    out_ref[...] = (summed / denominator).astype(jnp.bfloat16)


def attend(length, query, cache_k, cache_v, fresh):
    rows, head_dim = query.shape
    span = cache_k.shape[0]
    full = lambda shape: pl.BlockSpec(shape, lambda i, length_ref: (0,) * len(shape))
    keys = span + fresh.shape[0]
    return pl.pallas_call(
        attend_kernel,
        out_shape=jax.ShapeDtypeStruct((rows, head_dim), jnp.bfloat16),
        grid_spec=pltpu.PrefetchScalarGridSpec(
            num_scalar_prefetch=1,
            grid=(1,),
            in_specs=[full(query.shape), full(cache_k.shape), full(cache_v.shape), full(fresh.shape)],
            out_specs=full((rows, head_dim)),
        ),
        cost_estimate=pl.CostEstimate(
            flops=4 * rows * keys * head_dim,
            transcendentals=rows * keys,
            bytes_accessed=2 * (2 * span * head_dim + 2 * rows * head_dim + fresh.size),
        ),
    )(length.reshape(1), query, cache_k, cache_v, fresh)


def per_device(
    tokens,
    gain,
    w_router,
    expert_query_weight,
    key_value_weight,
    expert_output_weight,
    cache_keys,
    cached_value_slots,
    lengths,
    deal,
    route,
):
    requests = lengths.shape[0]
    experts = expert_query_weight.shape[0]
    heads_local = expert_query_weight.shape[2]
    head_dim = expert_query_weight.shape[3]
    top_count = route.shape[1]
    gathered = lax.all_gather(tokens, TOKEN_AXES, axis=0, tiled=True)
    total_rows, local_width = gathered.shape
    new_len = total_rows // requests
    full_width = local_width * lax.axis_size("gx")
    slot_index = lax.axis_index("gx")
    inverse = jnp.zeros((requests,), jnp.int32).at[deal].set(jnp.arange(requests, dtype=jnp.int32))
    assert heads_local == 1
    ordered = jnp.take(gathered.reshape(requests, new_len, local_width), inverse, axis=0).reshape(
        total_rows, local_width
    )
    slot_route = jnp.take(route.reshape(requests, new_len, top_count), inverse, axis=0).reshape(
        total_rows, top_count
    )
    packed = packed_partials(
        ordered,
        gain,
        w_router,
        expert_query_weight.reshape(experts, local_width, head_dim),
        key_value_weight.reshape(local_width, 2 * head_dim),
        slot_route,
        requests,
    )
    query_cols = top_count * heads_local * head_dim
    keyval_cols = heads_local * 2 * head_dim
    summed = scatter_sum(packed, "gx")
    query_totals = summed[:new_len, :query_cols].reshape(new_len, top_count, heads_local, head_dim)
    keyval_sums = summed[:new_len, query_cols : query_cols + keyval_cols].reshape(
        new_len, heads_local, 2 * head_dim
    )
    chosen_sums = jnp.transpose(summed[new_len, : top_count * new_len].reshape(top_count, new_len))
    square_sums = summed[new_len, top_count * new_len : (top_count + 1) * new_len]
    inverse_root_mean = lax.rsqrt(square_sums / full_width + norm_eps)
    chosen = chosen_sums * inverse_root_mean[:, None]
    gate_gap = chosen[:, 0] - chosen[:, 1]
    gate_weights = jnp.stack([jax.nn.sigmoid(gate_gap), jax.nn.sigmoid(-gate_gap)], axis=1).astype(
        jnp.bfloat16
    )
    query_matrix = (query_totals * inverse_root_mean[:, None, None, None]).astype(jnp.bfloat16)
    key_value_rows = (keyval_sums * inverse_root_mean[:, None, None]).astype(jnp.bfloat16)
    query_rows = new_len * top_count
    length = jnp.take(lengths, jnp.take(inverse, slot_index))
    attended_output = attend(
        length,
        query_matrix.reshape(query_rows, head_dim),
        cache_keys[0, 0],
        cached_value_slots[0, 0],
        key_value_rows.reshape(new_len, 2 * head_dim),
    ).reshape(new_len, query_cols)
    gate_row = jnp.transpose(gate_weights).reshape(1, top_count * new_len)
    assert gate_row.shape[1] <= query_cols
    extra_rows = 8
    shipped = jnp.concatenate(
        [
            attended_output,
            jnp.pad(gate_row, ((0, extra_rows - 1), (0, query_cols - gate_row.shape[1]))),
        ],
        axis=0,
    )
    all_shipped = gather_rows(shipped, "gx").reshape(requests, new_len + extra_rows, query_cols)
    cores = lax.axis_size("cc")
    chips = lax.axis_size("zz")
    staged = jnp.arange(requests, dtype=jnp.int32).reshape(chips, cores).T.reshape(requests)
    by_request = jnp.take(all_shipped, jnp.take(deal, staged), axis=0)
    route = jnp.take(route.reshape(requests, new_len, top_count), staged, axis=0).reshape(
        total_rows, top_count
    )
    token_attended = by_request[:, :new_len].reshape(total_rows, top_count, heads_local, head_dim)
    token_gates = (
        jnp.transpose(
            by_request[:, new_len, : top_count * new_len].reshape(requests, top_count, new_len),
            (0, 2, 1),
        )
        .reshape(total_rows, top_count)
        .astype(jnp.float32)
    )
    onehot = expert_onehot(route, experts)
    routed_attended = token_attended[:, :, None, :, :] * onehot[:, :, :, None, None].astype(
        jnp.bfloat16
    )
    projected = jnp.einsum(
        "tsehk,ehko->tso", routed_attended, expert_output_weight, preferred_element_type=jnp.float32
    )
    mixed_part = jnp.sum(token_gates[:, :, None] * projected, axis=1)
    output_sum = scatter_sum(scatter_sum(mixed_part, "cc"), "zz")
    return output_sum.astype(jnp.bfloat16)


TOKEN_AXES = ("zz", "cc")


def solution(mesh):
    gx_size, gy_size = mesh.devices.shape
    staged_mesh = Mesh(mesh.devices.reshape(gx_size, gy_size // 2, 2), ("gx",) + TOKEN_AXES)
    gy = TOKEN_AXES
    placed = (
        P(gy, "gx"),
        P("gx"),
        P("gx", None),
        P(None, "gx", gy, None),
        P("gx", gy, None),
        P(None, gy, None, "gx"),
        P("gx", gy, None, None),
        P("gx", gy, None, None),
        P(),
        P(),
        P(),
    )
    return jax.shard_map(
        per_device, mesh=staged_mesh, in_specs=placed, out_specs=P(gy, "gx"), check_vma=False
    )
```

```python
import jax
import jax.numpy as jnp
from jax import lax
from jax.experimental import pallas as pl
from jax.experimental.pallas import tpu as pltpu
from jax.sharding import Mesh, PartitionSpec as P

masked_score = -1e30
norm_eps = 1e-06
LANES = 128


def expert_onehot(route_rows, experts):
    return (route_rows[:, :, None] == jnp.arange(experts, dtype=jnp.int32)[None, None, :]).astype(
        jnp.float32
    )


def padded_width(width):
    return -(-width // LANES) * LANES


def scatter_sum(part, axis_name):
    members = lax.axis_size(axis_name)
    blocks = lax.all_to_all(
        part.reshape((members, part.shape[0] // members) + part.shape[1:]),
        axis_name,
        0,
        0,
        tiled=True,
    )
    return jnp.sum(blocks, axis=0)


def gather_rows(piece, axis_name):
    members = lax.axis_size(axis_name)
    copies = jnp.broadcast_to(piece[None], (members,) + piece.shape)
    gathered = lax.all_to_all(copies, axis_name, 0, 0, tiled=True)
    return gathered.reshape((members * piece.shape[0],) + piece.shape[1:])


def pack_kernel(tok_ref, gain_ref, router_ref, weight_ref, route_ref, route_t_ref, out_ref):
    rows = route_t_ref.shape[2]
    block_rows = rows + EXTRA_ROWS
    per_step = tok_ref.shape[0] // rows
    head_dim = out_ref.shape[1] // 4
    experts = (weight_ref.shape[1] - 2 * head_dim) // head_dim
    widened = tok_ref[...].astype(jnp.float32)
    scaled = (widened * gain_ref[...].astype(jnp.float32)).astype(jnp.bfloat16)
    projected = jnp.dot(scaled, weight_ref[...], preferred_element_type=jnp.float32)
    first = route_ref[:, 0:1]
    second = route_ref[:, 1:2]
    query_first = jnp.zeros((tok_ref.shape[0], head_dim), jnp.float32)
    query_second = jnp.zeros((tok_ref.shape[0], head_dim), jnp.float32)
    for expert in range(experts):
        part = projected[:, expert * head_dim : (expert + 1) * head_dim]
        query_first = query_first + jnp.where(first == expert, part, 0.0)
        query_second = query_second + jnp.where(second == expert, part, 0.0)
    keyval = projected[:, experts * head_dim :]
    contract_last = (((1,), (1,)), ((), ()))
    for block in range(per_step):
        low = block * rows
        top = block * block_rows
        out_ref[top : top + rows, 0:head_dim] = query_first[low : low + rows]
        out_ref[top : top + rows, head_dim : 2 * head_dim] = query_second[low : low + rows]
        out_ref[top : top + rows, 2 * head_dim :] = keyval[low : low + rows]
        widened_t = jnp.transpose(widened[low : low + rows])
        squares_row = jnp.sum(widened_t * widened_t, axis=0, keepdims=True)
        logits_t = lax.dot_general(
            router_ref[...], scaled[low : low + rows], contract_last, preferred_element_type=jnp.float32
        )
        expert_row = lax.broadcasted_iota(jnp.int32, logits_t.shape, 0)
        route_t = route_t_ref[block]
        chosen_first = jnp.sum(
            jnp.where(expert_row == route_t[0:1, :], logits_t, 0.0), axis=0, keepdims=True
        )
        chosen_second = jnp.sum(
            jnp.where(expert_row == route_t[1:2, :], logits_t, 0.0), axis=0, keepdims=True
        )
        out_ref[top + rows : top + block_rows, :] = jnp.zeros((EXTRA_ROWS, out_ref.shape[1]), jnp.float32)
        out_ref[top + rows : top + rows + 1, 0:rows] = chosen_first
        out_ref[top + rows : top + rows + 1, rows : 2 * rows] = chosen_second
        out_ref[top + rows : top + rows + 1, 2 * rows : 3 * rows] = squares_row


EXTRA_ROWS = 8
REQUESTS_PER_STEP = 4


def packed_partials(ordered, gain, w_router, query_weight, keyval_weight, route, requests):
    total_rows, width = ordered.shape
    rows = total_rows // requests
    experts, _, head_dim = query_weight.shape
    keyval_cols = keyval_weight.shape[1]
    packed_cols = 2 * head_dim + keyval_cols
    assert 3 * rows <= packed_cols and keyval_cols == 2 * head_dim
    block_rows = rows + EXTRA_ROWS
    step_rows = REQUESTS_PER_STEP * rows
    weight = jnp.concatenate(
        [jnp.transpose(query_weight, (1, 0, 2)).reshape(width, experts * head_dim), keyval_weight],
        axis=1,
    )
    route_t = jnp.transpose(route.reshape(requests, rows, route.shape[1]), (0, 2, 1))
    flops = 2 * total_rows * width * (weight.shape[1] + w_router.shape[1])
    moved = 2 * total_rows * width + 4 * requests * block_rows * packed_cols + 2 * weight.size
    return pl.pallas_call(
        pack_kernel,
        out_shape=jax.ShapeDtypeStruct((requests * block_rows, packed_cols), jnp.float32),
        grid=(requests // REQUESTS_PER_STEP,),
        in_specs=[
            pl.BlockSpec((step_rows, width), lambda s: (s, 0)),
            pl.BlockSpec((1, width), lambda s: (0, 0)),
            pl.BlockSpec((w_router.shape[1], width), lambda s: (0, 0)),
            pl.BlockSpec(weight.shape, lambda s: (0, 0)),
            pl.BlockSpec((step_rows, route.shape[1]), lambda s: (s, 0)),
            pl.BlockSpec((REQUESTS_PER_STEP, route.shape[1], rows), lambda s: (s, 0, 0)),
        ],
        out_specs=pl.BlockSpec((REQUESTS_PER_STEP * block_rows, packed_cols), lambda s: (s, 0)),
        cost_estimate=pl.CostEstimate(flops=flops, transcendentals=0, bytes_accessed=moved),
    )(ordered, gain.reshape(1, width), jnp.transpose(w_router), weight, route, route_t)


def attend_kernel(length_ref, query_ref, cache_k_ref, cache_v_ref, fresh_ref, out_ref):
    rows, head_dim = query_ref.shape
    fresh_len = fresh_ref.shape[0]
    top_count = rows // fresh_len
    score_scale = head_dim ** (-0.5)
    contract_last = (((1,), (1,)), ((), ()))
    query = query_ref[...]
    cached = lax.dot_general(query, cache_k_ref[...], contract_last, preferred_element_type=jnp.float32)
    cached = cached * score_scale
    key_col = lax.broadcasted_iota(jnp.int32, cached.shape, 1)
    cached = jnp.where(key_col < length_ref[0], cached, masked_score)
    fresh_keys = fresh_ref[:, 0:head_dim]
    fresh_values = fresh_ref[:, head_dim : 2 * head_dim]
    fresh = lax.dot_general(query, fresh_keys, contract_last, preferred_element_type=jnp.float32)
    fresh = fresh * score_scale
    fresh_col = lax.broadcasted_iota(jnp.int32, fresh.shape, 1)
    query_token = lax.broadcasted_iota(jnp.int32, fresh.shape, 0) // top_count
    fresh = jnp.where(fresh_col <= query_token, fresh, masked_score)
    top = jnp.maximum(
        jnp.max(cached, axis=1, keepdims=True), jnp.max(fresh, axis=1, keepdims=True)
    )
    cached_weights = jnp.exp(cached - top)
    fresh_weights = jnp.exp(fresh - top)
    denominator = jnp.sum(cached_weights, axis=1, keepdims=True) + jnp.sum(
        fresh_weights, axis=1, keepdims=True
    )
    summed = jnp.dot(
        cached_weights.astype(jnp.bfloat16), cache_v_ref[...], preferred_element_type=jnp.float32
    ) + jnp.dot(fresh_weights.astype(jnp.bfloat16), fresh_values, preferred_element_type=jnp.float32)
    out_ref[...] = (summed / denominator).astype(jnp.bfloat16)


def attend(length, query, cache_k, cache_v, fresh):
    rows, head_dim = query.shape
    span = cache_k.shape[0]
    full = lambda shape: pl.BlockSpec(shape, lambda i, length_ref: (0,) * len(shape))
    keys = span + fresh.shape[0]
    return pl.pallas_call(
        attend_kernel,
        out_shape=jax.ShapeDtypeStruct((rows, head_dim), jnp.bfloat16),
        grid_spec=pltpu.PrefetchScalarGridSpec(
            num_scalar_prefetch=1,
            grid=(1,),
            in_specs=[full(query.shape), full(cache_k.shape), full(cache_v.shape), full(fresh.shape)],
            out_specs=full((rows, head_dim)),
        ),
        cost_estimate=pl.CostEstimate(
            flops=4 * rows * keys * head_dim,
            transcendentals=rows * keys,
            bytes_accessed=2 * (2 * span * head_dim + 2 * rows * head_dim + fresh.size),
        ),
    )(length.reshape(1), query, cache_k, cache_v, fresh)


def mix_kernel(shipped_ref, route_ref, weight_ref, out_ref):
    block_rows = shipped_ref.shape[0] // REQUESTS_PER_STEP
    rows = block_rows - EXTRA_ROWS
    head_dim = weight_ref.shape[0]
    experts = weight_ref.shape[1] // out_ref.shape[1]
    width = out_ref.shape[1]
    top_count = shipped_ref.shape[1] // head_dim
    for block in range(REQUESTS_PER_STEP):
        top = block * block_rows
        low = block * rows
        gates = jnp.transpose(shipped_ref[top + rows : top + block_rows, :].astype(jnp.float32))
        mixed = jnp.zeros((rows, width), jnp.float32)
        for slot in range(top_count):
            attended = shipped_ref[top : top + rows, slot * head_dim : (slot + 1) * head_dim]
            projected = jnp.dot(attended, weight_ref[...], preferred_element_type=jnp.float32)
            chosen = route_ref[low : low + rows, slot : slot + 1]
            picked = jnp.zeros((rows, width), jnp.float32)
            for expert in range(experts):
                picked = picked + jnp.where(
                    chosen == expert, projected[:, expert * width : (expert + 1) * width], 0.0
                )
            mixed = mixed + gates[slot * rows : (slot + 1) * rows, 0:1] * picked
        out_ref[low : low + rows, :] = mixed


def mixed_partials(shipped, route, output_weight, requests):
    block_rows = shipped.shape[0] // requests
    rows = block_rows - EXTRA_ROWS
    experts, head_dim, width = output_weight.shape
    weight = jnp.transpose(output_weight, (1, 0, 2)).reshape(head_dim, experts * width)
    total_rows = requests * rows
    return pl.pallas_call(
        mix_kernel,
        out_shape=jax.ShapeDtypeStruct((total_rows, width), jnp.float32),
        grid=(requests // REQUESTS_PER_STEP,),
        in_specs=[
            pl.BlockSpec((REQUESTS_PER_STEP * block_rows, shipped.shape[1]), lambda s: (s, 0)),
            pl.BlockSpec((REQUESTS_PER_STEP * rows, route.shape[1]), lambda s: (s, 0)),
            pl.BlockSpec(weight.shape, lambda s: (0, 0)),
        ],
        out_specs=pl.BlockSpec((REQUESTS_PER_STEP * rows, width), lambda s: (s, 0)),
        cost_estimate=pl.CostEstimate(
            flops=2 * total_rows * route.shape[1] * head_dim * experts * width,
            transcendentals=0,
            bytes_accessed=2 * shipped.size + 2 * weight.size + 4 * total_rows * width,
        ),
    )(shipped, route, weight)


def per_device(
    tokens,
    gain,
    w_router,
    expert_query_weight,
    key_value_weight,
    expert_output_weight,
    cache_keys,
    cached_value_slots,
    lengths,
    deal,
    route,
):
    requests = lengths.shape[0]
    experts = expert_query_weight.shape[0]
    heads_local = expert_query_weight.shape[2]
    head_dim = expert_query_weight.shape[3]
    top_count = route.shape[1]
    gathered = lax.all_gather(tokens, TOKEN_AXES, axis=0, tiled=True)
    total_rows, local_width = gathered.shape
    new_len = total_rows // requests
    full_width = local_width * lax.axis_size("gx")
    slot_index = lax.axis_index("gx")
    inverse = jnp.zeros((requests,), jnp.int32).at[deal].set(jnp.arange(requests, dtype=jnp.int32))
    assert heads_local == 1
    ordered = jnp.take(gathered.reshape(requests, new_len, local_width), inverse, axis=0).reshape(
        total_rows, local_width
    )
    slot_route = jnp.take(route.reshape(requests, new_len, top_count), inverse, axis=0).reshape(
        total_rows, top_count
    )
    packed = packed_partials(
        ordered,
        gain,
        w_router,
        expert_query_weight.reshape(experts, local_width, head_dim),
        key_value_weight.reshape(local_width, 2 * head_dim),
        slot_route,
        requests,
    )
    query_cols = top_count * heads_local * head_dim
    keyval_cols = heads_local * 2 * head_dim
    summed = scatter_sum(packed, "gx")
    query_totals = summed[:new_len, :query_cols].reshape(new_len, top_count, heads_local, head_dim)
    keyval_sums = summed[:new_len, query_cols : query_cols + keyval_cols].reshape(
        new_len, heads_local, 2 * head_dim
    )
    chosen_sums = jnp.transpose(summed[new_len, : top_count * new_len].reshape(top_count, new_len))
    square_sums = summed[new_len, top_count * new_len : (top_count + 1) * new_len]
    inverse_root_mean = lax.rsqrt(square_sums / full_width + norm_eps)
    chosen = chosen_sums * inverse_root_mean[:, None]
    gate_gap = chosen[:, 0] - chosen[:, 1]
    gate_weights = jnp.stack([jax.nn.sigmoid(gate_gap), jax.nn.sigmoid(-gate_gap)], axis=1).astype(
        jnp.bfloat16
    )
    query_matrix = (query_totals * inverse_root_mean[:, None, None, None]).astype(jnp.bfloat16)
    key_value_rows = (keyval_sums * inverse_root_mean[:, None, None]).astype(jnp.bfloat16)
    query_rows = new_len * top_count
    length = jnp.take(lengths, jnp.take(inverse, slot_index))
    attended_output = attend(
        length,
        query_matrix.reshape(query_rows, head_dim),
        cache_keys[0, 0],
        cached_value_slots[0, 0],
        key_value_rows.reshape(new_len, 2 * head_dim),
    ).reshape(new_len, query_cols)
    gate_row = jnp.transpose(gate_weights).reshape(1, top_count * new_len)
    assert gate_row.shape[1] <= query_cols
    extra_rows = 8
    shipped = jnp.concatenate(
        [
            attended_output,
            jnp.pad(gate_row, ((0, extra_rows - 1), (0, query_cols - gate_row.shape[1]))),
        ],
        axis=0,
    )
    all_shipped = gather_rows(shipped, "gx").reshape(requests, new_len + extra_rows, query_cols)
    cores = lax.axis_size("cc")
    chips = lax.axis_size("zz")
    staged = jnp.arange(requests, dtype=jnp.int32).reshape(chips, cores).T.reshape(requests)
    by_request = jnp.take(all_shipped, jnp.take(deal, staged), axis=0)
    route = jnp.take(route.reshape(requests, new_len, top_count), staged, axis=0).reshape(
        total_rows, top_count
    )
    assert heads_local == 1
    mixed_part = mixed_partials(
        by_request.reshape(requests * (new_len + extra_rows), query_cols),
        route,
        expert_output_weight.reshape(experts, head_dim, expert_output_weight.shape[3]),
        requests,
    )
    output_sum = scatter_sum(scatter_sum(mixed_part, "cc"), "zz")
    return output_sum.astype(jnp.bfloat16)


TOKEN_AXES = ("zz", "cc")


def solution(mesh):
    gx_size, gy_size = mesh.devices.shape
    staged_mesh = Mesh(mesh.devices.reshape(gx_size, gy_size // 2, 2), ("gx",) + TOKEN_AXES)
    gy = TOKEN_AXES
    placed = (
        P(gy, "gx"),
        P("gx"),
        P("gx", None),
        P(None, "gx", gy, None),
        P("gx", gy, None),
        P(None, gy, None, "gx"),
        P("gx", gy, None, None),
        P("gx", gy, None, None),
        P(),
        P(),
        P(),
    )
    return jax.shard_map(
        per_device, mesh=staged_mesh, in_specs=placed, out_specs=P(gy, "gx"), check_vma=False
    )
```

```python
import jax
import jax.numpy as jnp
from jax import lax
from jax.experimental import pallas as pl
from jax.experimental.pallas import tpu as pltpu
from jax.sharding import Mesh, PartitionSpec as P


masked_score = -1e30
norm_eps = 1e-06
LANES = 128


def expert_onehot(route_rows, experts):
    return (route_rows[:, :, None] == jnp.arange(experts, dtype=jnp.int32)[None, None, :]).astype(
        jnp.float32
    )


def scatter_sum(part, axis_name):
    members = lax.axis_size(axis_name)
    blocks = lax.all_to_all(
        part.reshape((members, part.shape[0] // members) + part.shape[1:]),
        axis_name,
        0,
        0,
        tiled=True,
    )
    return jnp.sum(blocks, axis=0)


def gather_rows(piece, axis_name):
    members = lax.axis_size(axis_name)
    copies = jnp.broadcast_to(piece[None], (members,) + piece.shape)
    gathered = lax.all_to_all(copies, axis_name, 0, 0, tiled=True)
    return gathered.reshape((members * piece.shape[0],) + piece.shape[1:])


def attend_kernel(length_ref, query_ref, cache_k_ref, cache_v_ref, fresh_ref, out_ref):
    rows, head_dim = query_ref.shape
    fresh_len = fresh_ref.shape[0]
    top_count = rows // fresh_len
    score_scale = head_dim ** (-0.5)
    contract_last = (((1,), (1,)), ((), ()))
    query = query_ref[...]
    cached = lax.dot_general(query, cache_k_ref[...], contract_last, preferred_element_type=jnp.float32)
    cached = cached * score_scale
    key_col = lax.broadcasted_iota(jnp.int32, cached.shape, 1)
    cached = jnp.where(key_col < length_ref[0], cached, masked_score)
    fresh_keys = fresh_ref[:, 0:head_dim]
    fresh_values = fresh_ref[:, head_dim : 2 * head_dim]
    fresh = lax.dot_general(query, fresh_keys, contract_last, preferred_element_type=jnp.float32)
    fresh = fresh * score_scale
    fresh_col = lax.broadcasted_iota(jnp.int32, fresh.shape, 1)
    query_token = lax.broadcasted_iota(jnp.int32, fresh.shape, 0) // top_count
    fresh = jnp.where(fresh_col <= query_token, fresh, masked_score)
    top = jnp.maximum(
        jnp.max(cached, axis=1, keepdims=True), jnp.max(fresh, axis=1, keepdims=True)
    )
    cached_weights = jnp.exp(cached - top)
    fresh_weights = jnp.exp(fresh - top)
    denominator = jnp.sum(cached_weights, axis=1, keepdims=True) + jnp.sum(
        fresh_weights, axis=1, keepdims=True
    )
    summed = jnp.dot(
        cached_weights.astype(jnp.bfloat16), cache_v_ref[...], preferred_element_type=jnp.float32
    ) + jnp.dot(fresh_weights.astype(jnp.bfloat16), fresh_values, preferred_element_type=jnp.float32)
    out_ref[...] = (summed / denominator).astype(jnp.bfloat16)


def attend(length, query, cache_k, cache_v, fresh):
    rows, head_dim = query.shape
    span = cache_k.shape[0]
    full = lambda shape: pl.BlockSpec(shape, lambda i, length_ref: (0,) * len(shape))
    keys = span + fresh.shape[0]
    return pl.pallas_call(
        attend_kernel,
        out_shape=jax.ShapeDtypeStruct((rows, head_dim), jnp.bfloat16),
        grid_spec=pltpu.PrefetchScalarGridSpec(
            num_scalar_prefetch=1,
            grid=(1,),
            in_specs=[full(query.shape), full(cache_k.shape), full(cache_v.shape), full(fresh.shape)],
            out_specs=full((rows, head_dim)),
        ),
        cost_estimate=pl.CostEstimate(
            flops=4 * rows * keys * head_dim,
            transcendentals=rows * keys,
            bytes_accessed=2 * (2 * span * head_dim + 2 * rows * head_dim + fresh.size),
        ),
    )(length.reshape(1), query, cache_k, cache_v, fresh)


def per_device_body(
    tokens,
    gain,
    w_router,
    expert_query_weight,
    key_value_weight,
    expert_output_weight,
    cache_keys,
    cached_value_slots,
    lengths,
    deal,
    route,
):
    requests = lengths.shape[0]
    experts = expert_query_weight.shape[0]
    heads_local = expert_query_weight.shape[2]
    head_dim = expert_query_weight.shape[3]
    top_count = route.shape[1]
    assert heads_local == 1
    local_width = tokens.shape[1]
    members = lax.axis_size("gx")
    full_width = local_width * members
    slot_index = lax.axis_index("gx")
    new_len = tokens.shape[0]
    total_rows = new_len * requests
    query_cols = experts * head_dim
    keyval_cols = 2 * head_dim
    small_piece = jnp.concatenate(
        [
            w_router,
            gain[:, None],
            jnp.zeros((local_width, LANES - w_router.shape[1] - 1), jnp.bfloat16),
        ],
        axis=1,
    )
    weight_piece = jnp.concatenate(
        [
            jnp.transpose(expert_query_weight.reshape(experts, local_width, head_dim), (1, 0, 2)).reshape(
                local_width, query_cols
            ),
            key_value_weight.reshape(local_width, keyval_cols),
            small_piece,
        ],
        axis=1,
    )
    pieces = [None] * members
    pieces[0] = weight_piece
    for offset in range(1, members):
        pieces[offset] = lax.ppermute(
            weight_piece, "gx", [(source, (source + offset) % members) for source in range(members)]
        )
    received = jnp.stack(pieces)
    sources = (slot_index - jnp.arange(members, dtype=jnp.int32)) % members
    head_weights = jnp.zeros_like(received).at[sources].set(received)
    gathered = lax.all_gather(tokens, TOKEN_AXES, axis=0, tiled=True)
    inverse = jnp.zeros((requests,), jnp.int32).at[deal].set(jnp.arange(requests, dtype=jnp.int32))
    by_slot = jnp.take(gathered.reshape(requests, new_len, local_width), inverse, axis=0)
    own_tokens = lax.all_to_all(by_slot, "gx", 0, 0, tiled=True)
    my_request = jnp.take(inverse, slot_index)
    my_route = jnp.take(route.reshape(requests, new_len, top_count), my_request, axis=0)
    widened = own_tokens.astype(jnp.float32)
    square_sums = jnp.sum(widened * widened, axis=(0, 2))
    gain_full = head_weights[:, :, query_cols + keyval_cols + w_router.shape[1]]
    scaled_input = (widened * gain_full.astype(jnp.float32)[:, None, :]).astype(jnp.bfloat16)
    router_cols = slice(query_cols + keyval_cols, query_cols + keyval_cols + w_router.shape[1])
    logits_raw = jnp.einsum(
        "itd,ide->te", scaled_input, head_weights[:, :, router_cols], preferred_element_type=jnp.float32
    )
    projected = jnp.einsum(
        "itd,idk->tk",
        scaled_input,
        head_weights[:, :, : query_cols + keyval_cols],
        preferred_element_type=jnp.float32,
    )
    my_onehot = expert_onehot(my_route, experts)
    query_totals = jnp.sum(
        my_onehot[:, :, :, None] * projected[:, None, :query_cols].reshape(new_len, 1, experts, head_dim),
        axis=2,
    ).reshape(new_len, top_count, heads_local, head_dim)
    keyval_sums = projected[:, query_cols:].reshape(new_len, heads_local, keyval_cols)
    chosen_sums = jnp.sum(my_onehot * logits_raw[:, None, :], axis=2)
    query_cols = top_count * heads_local * head_dim
    inverse_root_mean = lax.rsqrt(square_sums / full_width + norm_eps)
    chosen = chosen_sums * inverse_root_mean[:, None]
    gate_gap = chosen[:, 0] - chosen[:, 1]
    gate_weights = jnp.stack([jax.nn.sigmoid(gate_gap), jax.nn.sigmoid(-gate_gap)], axis=1).astype(
        jnp.bfloat16
    )
    query_matrix = (query_totals * inverse_root_mean[:, None, None, None]).astype(jnp.bfloat16)
    key_value_rows = (keyval_sums * inverse_root_mean[:, None, None]).astype(jnp.bfloat16)
    query_rows = new_len * top_count
    length = jnp.take(lengths, jnp.take(inverse, slot_index))
    attended_output = attend(
        length,
        query_matrix.reshape(query_rows, head_dim),
        cache_keys[0, 0],
        cached_value_slots[0, 0],
        key_value_rows.reshape(new_len, 2 * head_dim),
    ).reshape(new_len, query_cols)
    gate_row = jnp.transpose(gate_weights).reshape(1, top_count * new_len)
    assert gate_row.shape[1] <= query_cols
    extra_rows = 8
    shipped = jnp.concatenate(
        [
            attended_output,
            jnp.pad(gate_row, ((0, extra_rows - 1), (0, query_cols - gate_row.shape[1]))),
        ],
        axis=0,
    )
    all_shipped = gather_rows(shipped, "gx").reshape(requests, new_len + extra_rows, query_cols)
    cores = lax.axis_size("cc")
    chips = lax.axis_size("zz")
    staged = jnp.arange(requests, dtype=jnp.int32).reshape(chips, cores).T.reshape(requests)
    by_request = jnp.take(all_shipped, jnp.take(deal, staged), axis=0)
    route = jnp.take(route.reshape(requests, new_len, top_count), staged, axis=0).reshape(
        total_rows, top_count
    )
    token_attended = by_request[:, :new_len].reshape(total_rows, top_count, heads_local, head_dim)
    token_gates = (
        jnp.transpose(
            by_request[:, new_len, : top_count * new_len].reshape(requests, top_count, new_len),
            (0, 2, 1),
        )
        .reshape(total_rows, top_count)
        .astype(jnp.float32)
    )
    onehot = expert_onehot(route, experts)
    routed_attended = token_attended[:, :, None, :, :] * onehot[:, :, :, None, None].astype(
        jnp.bfloat16
    )
    projected = jnp.einsum(
        "tsehk,ehko->tso", routed_attended, expert_output_weight, preferred_element_type=jnp.float32
    )
    mixed_part = jnp.sum(token_gates[:, :, None] * projected, axis=1)
    output_sum = scatter_sum(scatter_sum(mixed_part, "cc"), "zz")
    return output_sum.astype(jnp.bfloat16)


TOKEN_AXES = ("zz", "cc")


def solution(mesh):
    gx_size, gy_size = mesh.devices.shape
    staged_mesh = Mesh(mesh.devices.reshape(gx_size, gy_size // 2, 2), ("gx",) + TOKEN_AXES)
    gy = TOKEN_AXES
    placed = (
        P(gy, "gx"),
        P("gx"),
        P("gx", None),
        P(None, "gx", gy, None),
        P("gx", gy, None),
        P(None, gy, None, "gx"),
        P("gx", gy, None, None),
        P("gx", gy, None, None),
        P(),
        P(),
        P(),
    )
    return jax.shard_map(per_device_body, mesh=staged_mesh, in_specs=placed, out_specs=P(gy, "gx"), check_vma=False)
```

```python
import jax
import jax.numpy as jnp
from jax import lax
from jax.experimental import pallas as pl
from jax.experimental.pallas import tpu as pltpu
from jax.sharding import Mesh, PartitionSpec as P


masked_score = -1e30
norm_eps = 1e-06
LANES = 128


def expert_onehot(route_rows, experts):
    return (route_rows[:, :, None] == jnp.arange(experts, dtype=jnp.int32)[None, None, :]).astype(
        jnp.float32
    )


def scatter_sum(part, axis_name):
    members = lax.axis_size(axis_name)
    blocks = lax.all_to_all(
        part.reshape((members, part.shape[0] // members) + part.shape[1:]),
        axis_name,
        0,
        0,
        tiled=True,
    )
    return jnp.sum(blocks, axis=0)


def gather_rows(piece, axis_name):
    members = lax.axis_size(axis_name)
    copies = jnp.broadcast_to(piece[None], (members,) + piece.shape)
    gathered = lax.all_to_all(copies, axis_name, 0, 0, tiled=True)
    return gathered.reshape((members * piece.shape[0],) + piece.shape[1:])


def attend_kernel(length_ref, query_ref, cache_k_ref, cache_v_ref, fresh_ref, out_ref):
    rows, head_dim = query_ref.shape
    fresh_len = fresh_ref.shape[0]
    top_count = rows // fresh_len
    score_scale = head_dim ** (-0.5)
    contract_last = (((1,), (1,)), ((), ()))
    query = query_ref[...]
    cached = lax.dot_general(query, cache_k_ref[...], contract_last, preferred_element_type=jnp.float32)
    cached = cached * score_scale
    key_col = lax.broadcasted_iota(jnp.int32, cached.shape, 1)
    cached = jnp.where(key_col < length_ref[0], cached, masked_score)
    fresh_keys = fresh_ref[:, 0:head_dim]
    fresh_values = fresh_ref[:, head_dim : 2 * head_dim]
    fresh = lax.dot_general(query, fresh_keys, contract_last, preferred_element_type=jnp.float32)
    fresh = fresh * score_scale
    fresh_col = lax.broadcasted_iota(jnp.int32, fresh.shape, 1)
    query_token = lax.broadcasted_iota(jnp.int32, fresh.shape, 0) // top_count
    fresh = jnp.where(fresh_col <= query_token, fresh, masked_score)
    top = jnp.maximum(
        jnp.max(cached, axis=1, keepdims=True), jnp.max(fresh, axis=1, keepdims=True)
    )
    cached_weights = jnp.exp(cached - top)
    fresh_weights = jnp.exp(fresh - top)
    denominator = jnp.sum(cached_weights, axis=1, keepdims=True) + jnp.sum(
        fresh_weights, axis=1, keepdims=True
    )
    summed = jnp.dot(
        cached_weights.astype(jnp.bfloat16), cache_v_ref[...], preferred_element_type=jnp.float32
    ) + jnp.dot(fresh_weights.astype(jnp.bfloat16), fresh_values, preferred_element_type=jnp.float32)
    out_ref[...] = (summed / denominator).astype(jnp.bfloat16)


def attend(length, query, cache_k, cache_v, fresh):
    rows, head_dim = query.shape
    span = cache_k.shape[0]
    full = lambda shape: pl.BlockSpec(shape, lambda i, length_ref: (0,) * len(shape))
    keys = span + fresh.shape[0]
    return pl.pallas_call(
        attend_kernel,
        out_shape=jax.ShapeDtypeStruct((rows, head_dim), jnp.bfloat16),
        grid_spec=pltpu.PrefetchScalarGridSpec(
            num_scalar_prefetch=1,
            grid=(1,),
            in_specs=[full(query.shape), full(cache_k.shape), full(cache_v.shape), full(fresh.shape)],
            out_specs=full((rows, head_dim)),
        ),
        cost_estimate=pl.CostEstimate(
            flops=4 * rows * keys * head_dim,
            transcendentals=rows * keys,
            bytes_accessed=2 * (2 * span * head_dim + 2 * rows * head_dim + fresh.size),
        ),
    )(length.reshape(1), query, cache_k, cache_v, fresh)


def per_device_body(
    tokens,
    gain,
    w_router,
    expert_query_weight,
    key_value_weight,
    expert_output_weight,
    cache_keys,
    cached_value_slots,
    lengths,
    deal,
    route,
):
    requests = lengths.shape[0]
    experts = expert_query_weight.shape[0]
    heads_local = expert_query_weight.shape[2]
    head_dim = expert_query_weight.shape[3]
    top_count = route.shape[1]
    assert heads_local == 1
    local_width = tokens.shape[1]
    members = lax.axis_size("gx")
    full_width = local_width * members
    slot_index = lax.axis_index("gx")
    new_len = tokens.shape[0]
    total_rows = new_len * requests
    query_cols = experts * head_dim
    keyval_cols = 2 * head_dim
    small_piece = jnp.concatenate(
        [
            w_router,
            gain[:, None],
            jnp.zeros((local_width, LANES - w_router.shape[1] - 1), jnp.bfloat16),
        ],
        axis=1,
    )
    weight_piece = jnp.concatenate(
        [
            jnp.transpose(expert_query_weight.reshape(experts, local_width, head_dim), (1, 0, 2)).reshape(
                local_width, query_cols
            ),
            key_value_weight.reshape(local_width, keyval_cols),
            small_piece,
        ],
        axis=1,
    )
    head_weights = gather_rows(weight_piece, "gx")
    head_weights = head_weights.reshape(members, local_width, weight_piece.shape[1])
    gathered = lax.all_gather(tokens, TOKEN_AXES, axis=0, tiled=True)
    inverse = jnp.zeros((requests,), jnp.int32).at[deal].set(jnp.arange(requests, dtype=jnp.int32))
    by_slot = jnp.take(gathered.reshape(requests, new_len, local_width), inverse, axis=0)
    own_tokens = lax.all_to_all(by_slot, "gx", 0, 0, tiled=True)
    my_request = jnp.take(inverse, slot_index)
    my_route = jnp.take(route.reshape(requests, new_len, top_count), my_request, axis=0)
    widened = own_tokens.astype(jnp.float32)
    square_sums = jnp.sum(widened * widened, axis=(0, 2))
    gain_full = head_weights[:, :, query_cols + keyval_cols + w_router.shape[1]]
    scaled_input = (widened * gain_full.astype(jnp.float32)[:, None, :]).astype(jnp.bfloat16)
    router_cols = slice(query_cols + keyval_cols, query_cols + keyval_cols + w_router.shape[1])
    logits_raw = jnp.einsum(
        "itd,ide->te", scaled_input, head_weights[:, :, router_cols], preferred_element_type=jnp.float32
    )
    projected = jnp.einsum(
        "itd,idk->tk",
        scaled_input,
        head_weights[:, :, : query_cols + keyval_cols],
        preferred_element_type=jnp.float32,
    )
    my_onehot = expert_onehot(my_route, experts)
    query_totals = jnp.sum(
        my_onehot[:, :, :, None] * projected[:, None, :query_cols].reshape(new_len, 1, experts, head_dim),
        axis=2,
    ).reshape(new_len, top_count, heads_local, head_dim)
    keyval_sums = projected[:, query_cols:].reshape(new_len, heads_local, keyval_cols)
    chosen_sums = jnp.sum(my_onehot * logits_raw[:, None, :], axis=2)
    query_cols = top_count * heads_local * head_dim
    inverse_root_mean = lax.rsqrt(square_sums / full_width + norm_eps)
    chosen = chosen_sums * inverse_root_mean[:, None]
    gate_gap = chosen[:, 0] - chosen[:, 1]
    gate_weights = jnp.stack([jax.nn.sigmoid(gate_gap), jax.nn.sigmoid(-gate_gap)], axis=1).astype(
        jnp.bfloat16
    )
    query_matrix = (query_totals * inverse_root_mean[:, None, None, None]).astype(jnp.bfloat16)
    key_value_rows = (keyval_sums * inverse_root_mean[:, None, None]).astype(jnp.bfloat16)
    query_rows = new_len * top_count
    length = jnp.take(lengths, jnp.take(inverse, slot_index))
    attended_output = attend(
        length,
        query_matrix.reshape(query_rows, head_dim),
        cache_keys[0, 0],
        cached_value_slots[0, 0],
        key_value_rows.reshape(new_len, 2 * head_dim),
    ).reshape(new_len, query_cols)
    gate_row = jnp.transpose(gate_weights).reshape(1, top_count * new_len)
    assert gate_row.shape[1] <= query_cols
    extra_rows = 8
    shipped = jnp.concatenate(
        [
            attended_output,
            jnp.pad(gate_row, ((0, extra_rows - 1), (0, query_cols - gate_row.shape[1]))),
        ],
        axis=0,
    )
    all_shipped = gather_rows(shipped, "gx").reshape(requests, new_len + extra_rows, query_cols)
    cores = lax.axis_size("cc")
    chips = lax.axis_size("zz")
    staged = jnp.arange(requests, dtype=jnp.int32).reshape(chips, cores).T.reshape(requests)
    by_request = jnp.take(all_shipped, jnp.take(deal, staged), axis=0)
    route = jnp.take(route.reshape(requests, new_len, top_count), staged, axis=0).reshape(
        total_rows, top_count
    )
    token_attended = by_request[:, :new_len].reshape(total_rows, top_count, heads_local, head_dim)
    token_gates = (
        jnp.transpose(
            by_request[:, new_len, : top_count * new_len].reshape(requests, top_count, new_len),
            (0, 2, 1),
        )
        .reshape(total_rows, top_count)
        .astype(jnp.float32)
    )
    onehot = expert_onehot(route, experts)
    routed_attended = token_attended[:, :, None, :, :] * onehot[:, :, :, None, None].astype(
        jnp.bfloat16
    )
    projected = jnp.einsum(
        "tsehk,ehko->tso", routed_attended, expert_output_weight, preferred_element_type=jnp.float32
    )
    mixed_part = jnp.sum(token_gates[:, :, None] * projected, axis=1)
    output_sum = scatter_sum(scatter_sum(mixed_part, "cc"), "zz")
    return output_sum.astype(jnp.bfloat16)


TOKEN_AXES = ("zz", "cc")


def solution(mesh):
    gx_size, gy_size = mesh.devices.shape
    staged_mesh = Mesh(mesh.devices.reshape(gx_size, gy_size // 2, 2), ("gx",) + TOKEN_AXES)
    gy = TOKEN_AXES
    placed = (
        P(gy, "gx"),
        P("gx"),
        P("gx", None),
        P(None, "gx", gy, None),
        P("gx", gy, None),
        P(None, gy, None, "gx"),
        P("gx", gy, None, None),
        P("gx", gy, None, None),
        P(),
        P(),
        P(),
    )
    return jax.shard_map(per_device_body, mesh=staged_mesh, in_specs=placed, out_specs=P(gy, "gx"), check_vma=False)
```

```python
import jax
import jax.numpy as jnp
from jax import lax
from jax.experimental import pallas as pl
from jax.experimental.pallas import tpu as pltpu
from jax.sharding import Mesh, PartitionSpec as P

masked_score = -1e30
norm_eps = 1e-06
LANES = 128


def expert_onehot(route_rows, experts):
    return (route_rows[:, :, None] == jnp.arange(experts, dtype=jnp.int32)[None, None, :]).astype(
        jnp.float32
    )


def padded_width(width):
    return -(-width // LANES) * LANES


def scatter_sum(part, axis_name):
    members = lax.axis_size(axis_name)
    blocks = lax.all_to_all(
        part.reshape((members, part.shape[0] // members) + part.shape[1:]),
        axis_name,
        0,
        0,
        tiled=True,
    )
    return jnp.sum(blocks, axis=0)


def gather_rows(piece, axis_name):
    members = lax.axis_size(axis_name)
    copies = jnp.broadcast_to(piece[None], (members,) + piece.shape)
    gathered = lax.all_to_all(copies, axis_name, 0, 0, tiled=True)
    return gathered.reshape((members * piece.shape[0],) + piece.shape[1:])


def pack_kernel(tok_ref, gain_ref, router_ref, weight_ref, route_ref, route_t_ref, out_ref):
    rows = route_t_ref.shape[2]
    block_rows = rows + EXTRA_ROWS
    per_step = tok_ref.shape[0] // rows
    head_dim = out_ref.shape[1] // 4
    experts = (weight_ref.shape[1] - 2 * head_dim) // head_dim
    widened = tok_ref[...].astype(jnp.float32)
    scaled = (widened * gain_ref[...].astype(jnp.float32)).astype(jnp.bfloat16)
    projected = jnp.dot(scaled, weight_ref[...], preferred_element_type=jnp.float32)
    first = route_ref[:, 0:1]
    second = route_ref[:, 1:2]
    query_first = jnp.zeros((tok_ref.shape[0], head_dim), jnp.float32)
    query_second = jnp.zeros((tok_ref.shape[0], head_dim), jnp.float32)
    for expert in range(experts):
        part = projected[:, expert * head_dim : (expert + 1) * head_dim]
        query_first = query_first + jnp.where(first == expert, part, 0.0)
        query_second = query_second + jnp.where(second == expert, part, 0.0)
    keyval = projected[:, experts * head_dim :]
    contract_last = (((1,), (1,)), ((), ()))
    for block in range(per_step):
        low = block * rows
        top = block * block_rows
        out_ref[top : top + rows, 0:head_dim] = query_first[low : low + rows]
        out_ref[top : top + rows, head_dim : 2 * head_dim] = query_second[low : low + rows]
        out_ref[top : top + rows, 2 * head_dim :] = keyval[low : low + rows]
        widened_t = jnp.transpose(widened[low : low + rows])
        squares_row = jnp.sum(widened_t * widened_t, axis=0, keepdims=True)
        logits_t = lax.dot_general(
            router_ref[...], scaled[low : low + rows], contract_last, preferred_element_type=jnp.float32
        )
        expert_row = lax.broadcasted_iota(jnp.int32, logits_t.shape, 0)
        route_t = route_t_ref[block]
        chosen_first = jnp.sum(
            jnp.where(expert_row == route_t[0:1, :], logits_t, 0.0), axis=0, keepdims=True
        )
        chosen_second = jnp.sum(
            jnp.where(expert_row == route_t[1:2, :], logits_t, 0.0), axis=0, keepdims=True
        )
        out_ref[top + rows : top + block_rows, :] = jnp.zeros((EXTRA_ROWS, out_ref.shape[1]), jnp.float32)
        out_ref[top + rows : top + rows + 1, 0:rows] = chosen_first
        out_ref[top + rows : top + rows + 1, rows : 2 * rows] = chosen_second
        out_ref[top + rows : top + rows + 1, 2 * rows : 3 * rows] = squares_row


EXTRA_ROWS = 8
REQUESTS_PER_STEP = 4


def packed_partials(ordered, gain, w_router, query_weight, keyval_weight, route, requests):
    total_rows, width = ordered.shape
    rows = total_rows // requests
    experts, _, head_dim = query_weight.shape
    keyval_cols = keyval_weight.shape[1]
    packed_cols = 2 * head_dim + keyval_cols
    assert 3 * rows <= packed_cols and keyval_cols == 2 * head_dim
    block_rows = rows + EXTRA_ROWS
    step_rows = REQUESTS_PER_STEP * rows
    weight = jnp.concatenate(
        [jnp.transpose(query_weight, (1, 0, 2)).reshape(width, experts * head_dim), keyval_weight],
        axis=1,
    )
    route_t = jnp.transpose(route.reshape(requests, rows, route.shape[1]), (0, 2, 1))
    flops = 2 * total_rows * width * (weight.shape[1] + w_router.shape[1])
    moved = 2 * total_rows * width + 4 * requests * block_rows * packed_cols + 2 * weight.size
    return pl.pallas_call(
        pack_kernel,
        out_shape=jax.ShapeDtypeStruct((requests * block_rows, packed_cols), jnp.float32),
        grid=(requests // REQUESTS_PER_STEP,),
        in_specs=[
            pl.BlockSpec((step_rows, width), lambda s: (s, 0)),
            pl.BlockSpec((1, width), lambda s: (0, 0)),
            pl.BlockSpec((w_router.shape[1], width), lambda s: (0, 0)),
            pl.BlockSpec(weight.shape, lambda s: (0, 0)),
            pl.BlockSpec((step_rows, route.shape[1]), lambda s: (s, 0)),
            pl.BlockSpec((REQUESTS_PER_STEP, route.shape[1], rows), lambda s: (s, 0, 0)),
        ],
        out_specs=pl.BlockSpec((REQUESTS_PER_STEP * block_rows, packed_cols), lambda s: (s, 0)),
        cost_estimate=pl.CostEstimate(flops=flops, transcendentals=0, bytes_accessed=moved),
    )(ordered, gain.reshape(1, width), jnp.transpose(w_router), weight, route, route_t)


def attend_kernel(length_ref, blocks_ref, cache_k_ref, cache_v_ref, out_ref):
    members, block_rows, packed_cols = blocks_ref.shape
    rows = block_rows - EXTRA_ROWS
    head_dim = cache_k_ref.shape[1]
    full_width = members * LANES
    summed = blocks_ref[0]
    for member in range(1, members):
        summed = summed + blocks_ref[member]
    partials = summed[0:rows]
    extra = summed[rows:block_rows]
    extra_t = jnp.transpose(extra)
    inverse_col = lax.rsqrt(extra_t[2 * rows : 3 * rows, 0:1] / full_width + norm_eps)
    inverse_row = lax.rsqrt(extra[0:1, 2 * rows : 3 * rows] / full_width + norm_eps)
    gate_gap = extra[0:1, 0:rows] * inverse_row - extra[0:1, rows : 2 * rows] * inverse_row
    gate_row = jnp.concatenate([jax.nn.sigmoid(gate_gap), jax.nn.sigmoid(-gate_gap)], axis=1)
    gate_row = gate_row.astype(jnp.bfloat16).astype(jnp.float32)
    scaled = partials * inverse_col
    query = jnp.concatenate(
        [scaled[:, 0:head_dim], scaled[:, head_dim : 2 * head_dim]], axis=0
    ).astype(jnp.bfloat16)
    fresh_keys = scaled[:, 2 * head_dim : 3 * head_dim].astype(jnp.bfloat16)
    fresh_values = scaled[:, 3 * head_dim : 4 * head_dim].astype(jnp.bfloat16)
    score_scale = head_dim ** (-0.5)
    contract_last = (((1,), (1,)), ((), ()))
    cached = lax.dot_general(query, cache_k_ref[...], contract_last, preferred_element_type=jnp.float32)
    cached = cached * score_scale
    key_col = lax.broadcasted_iota(jnp.int32, cached.shape, 1)
    cached = jnp.where(key_col < length_ref[0], cached, masked_score)
    fresh = lax.dot_general(query, fresh_keys, contract_last, preferred_element_type=jnp.float32)
    fresh = fresh * score_scale
    fresh_col = lax.broadcasted_iota(jnp.int32, fresh.shape, 1)
    query_token = lax.broadcasted_iota(jnp.int32, fresh.shape, 0) % rows
    fresh = jnp.where(fresh_col <= query_token, fresh, masked_score)
    top = jnp.maximum(
        jnp.max(cached, axis=1, keepdims=True), jnp.max(fresh, axis=1, keepdims=True)
    )
    cached_weights = jnp.exp(cached - top)
    fresh_weights = jnp.exp(fresh - top)
    denominator = jnp.sum(cached_weights, axis=1, keepdims=True) + jnp.sum(
        fresh_weights, axis=1, keepdims=True
    )
    attended = jnp.dot(
        cached_weights.astype(jnp.bfloat16), cache_v_ref[...], preferred_element_type=jnp.float32
    ) + jnp.dot(fresh_weights.astype(jnp.bfloat16), fresh_values, preferred_element_type=jnp.float32)
    attended = (attended / denominator).astype(jnp.bfloat16)
    first_slot = attended[0:rows]
    second_slot = attended[rows : 2 * rows]
    extra_row = lax.broadcasted_iota(jnp.int32, (EXTRA_ROWS, 2 * rows), 0)
    gate_block = jnp.where(
        extra_row == 0, jnp.broadcast_to(gate_row, (EXTRA_ROWS, 2 * rows)), 0.0
    ).astype(jnp.bfloat16)
    for member in range(out_ref.shape[0]):
        out_ref[member, 0:rows, 0:head_dim] = first_slot
        out_ref[member, 0:rows, head_dim : 2 * head_dim] = second_slot
        out_ref[member, rows:block_rows, :] = gate_block


def attend(length, blocks, cache_k, cache_v):
    members, block_rows, packed_cols = blocks.shape
    rows = block_rows - EXTRA_ROWS
    span, head_dim = cache_k.shape
    full = lambda shape: pl.BlockSpec(shape, lambda i, length_ref: (0,) * len(shape))
    out_shape = (members, block_rows, 2 * head_dim)
    keys = span + rows
    query_rows = 2 * rows
    return pl.pallas_call(
        attend_kernel,
        out_shape=jax.ShapeDtypeStruct(out_shape, jnp.bfloat16),
        grid_spec=pltpu.PrefetchScalarGridSpec(
            num_scalar_prefetch=1,
            grid=(1,),
            in_specs=[full(blocks.shape), full(cache_k.shape), full(cache_v.shape)],
            out_specs=full(out_shape),
        ),
        cost_estimate=pl.CostEstimate(
            flops=4 * query_rows * keys * head_dim,
            transcendentals=query_rows * keys,
            bytes_accessed=4 * blocks.size + 4 * span * head_dim + 2 * members * block_rows * 2 * head_dim,
        ),
    )(length.reshape(1), blocks, cache_k, cache_v)


def per_device(
    tokens,
    gain,
    w_router,
    expert_query_weight,
    key_value_weight,
    expert_output_weight,
    cache_keys,
    cached_value_slots,
    lengths,
    deal,
    route,
):
    requests = lengths.shape[0]
    experts = expert_query_weight.shape[0]
    heads_local = expert_query_weight.shape[2]
    head_dim = expert_query_weight.shape[3]
    top_count = route.shape[1]
    gathered = lax.all_gather(tokens, TOKEN_AXES, axis=0, tiled=True)
    total_rows, local_width = gathered.shape
    new_len = total_rows // requests
    full_width = local_width * lax.axis_size("gx")
    slot_index = lax.axis_index("gx")
    inverse = jnp.zeros((requests,), jnp.int32).at[deal].set(jnp.arange(requests, dtype=jnp.int32))
    assert heads_local == 1
    ordered = jnp.take(gathered.reshape(requests, new_len, local_width), inverse, axis=0).reshape(
        total_rows, local_width
    )
    slot_route = jnp.take(route.reshape(requests, new_len, top_count), inverse, axis=0).reshape(
        total_rows, top_count
    )
    packed = packed_partials(
        ordered,
        gain,
        w_router,
        expert_query_weight.reshape(experts, local_width, head_dim),
        key_value_weight.reshape(local_width, 2 * head_dim),
        slot_route,
        requests,
    )
    query_cols = top_count * heads_local * head_dim
    keyval_cols = heads_local * 2 * head_dim
    members = lax.axis_size("gx")
    blocks = lax.all_to_all(
        packed.reshape(members, packed.shape[0] // members, packed.shape[1]), "gx", 0, 0, tiled=True
    )
    length = jnp.take(lengths, jnp.take(inverse, slot_index))
    copies = attend(length, blocks, cache_keys[0, 0], cached_value_slots[0, 0])
    extra_rows = EXTRA_ROWS
    all_shipped = lax.all_to_all(copies, "gx", 0, 0, tiled=True).reshape(
        requests, new_len + extra_rows, query_cols
    )
    cores = lax.axis_size("cc")
    chips = lax.axis_size("zz")
    staged = jnp.arange(requests, dtype=jnp.int32).reshape(chips, cores).T.reshape(requests)
    by_request = jnp.take(all_shipped, jnp.take(deal, staged), axis=0)
    route = jnp.take(route.reshape(requests, new_len, top_count), staged, axis=0).reshape(
        total_rows, top_count
    )
    token_attended = by_request[:, :new_len].reshape(total_rows, top_count, heads_local, head_dim)
    token_gates = (
        jnp.transpose(
            by_request[:, new_len, : top_count * new_len].reshape(requests, top_count, new_len),
            (0, 2, 1),
        )
        .reshape(total_rows, top_count)
        .astype(jnp.float32)
    )
    onehot = expert_onehot(route, experts)
    routed_attended = token_attended[:, :, None, :, :] * onehot[:, :, :, None, None].astype(
        jnp.bfloat16
    )
    projected = jnp.einsum(
        "tsehk,ehko->tso", routed_attended, expert_output_weight, preferred_element_type=jnp.float32
    )
    mixed_part = jnp.sum(token_gates[:, :, None] * projected, axis=1)
    output_sum = scatter_sum(scatter_sum(mixed_part, "cc"), "zz")
    return output_sum.astype(jnp.bfloat16)


TOKEN_AXES = ("zz", "cc")


def solution(mesh):
    gx_size, gy_size = mesh.devices.shape
    staged_mesh = Mesh(mesh.devices.reshape(gx_size, gy_size // 2, 2), ("gx",) + TOKEN_AXES)
    gy = TOKEN_AXES
    placed = (
        P(gy, "gx"),
        P("gx"),
        P("gx", None),
        P(None, "gx", gy, None),
        P("gx", gy, None),
        P(None, gy, None, "gx"),
        P("gx", gy, None, None),
        P("gx", gy, None, None),
        P(),
        P(),
        P(),
    )
    return jax.shard_map(
        per_device, mesh=staged_mesh, in_specs=placed, out_specs=P(gy, "gx"), check_vma=False
    )
```

```python
import jax
import jax.numpy as jnp
from jax import lax
from jax.experimental import pallas as pl
from jax.experimental.pallas import tpu as pltpu
from jax.sharding import Mesh, PartitionSpec as P

masked_score = -1e30
norm_eps = 1e-06
LANES = 128


def expert_onehot(route_rows, experts):
    return (route_rows[:, :, None] == jnp.arange(experts, dtype=jnp.int32)[None, None, :]).astype(
        jnp.float32
    )


def padded_width(width):
    return -(-width // LANES) * LANES


def scatter_sum(part, axis_name):
    members = lax.axis_size(axis_name)
    blocks = lax.all_to_all(
        part.reshape((members, part.shape[0] // members) + part.shape[1:]),
        axis_name,
        0,
        0,
        tiled=True,
    )
    return jnp.sum(blocks, axis=0)


def gather_rows(piece, axis_name):
    members = lax.axis_size(axis_name)
    copies = jnp.broadcast_to(piece[None], (members,) + piece.shape)
    gathered = lax.all_to_all(copies, axis_name, 0, 0, tiled=True)
    return gathered.reshape((members * piece.shape[0],) + piece.shape[1:])


def pack_kernel(order_ref, tok_ref, gain_ref, router_ref, weight_ref, route_ref, route_t_ref, out_ref):
    rows = tok_ref.shape[0] // order_ref.shape[0]
    block_rows = rows + EXTRA_ROWS
    head_dim = out_ref.shape[1] // 4
    experts = (weight_ref.shape[1] - 2 * head_dim) // head_dim
    contract_last = (((1,), (1,)), ((), ()))
    step = pl.program_id(0)
    for block in range(REQUESTS_PER_STEP):
        first_row = pl.multiple_of(order_ref[step * REQUESTS_PER_STEP + block] * rows, rows)
        widened = tok_ref[pl.ds(first_row, rows), :].astype(jnp.float32)
        scaled = (widened * gain_ref[...].astype(jnp.float32)).astype(jnp.bfloat16)
        projected = jnp.dot(scaled, weight_ref[...], preferred_element_type=jnp.float32)
        route = route_ref[pl.ds(first_row, rows), :]
        first = route[:, 0:1]
        second = route[:, 1:2]
        query_first = jnp.zeros((rows, head_dim), jnp.float32)
        query_second = jnp.zeros((rows, head_dim), jnp.float32)
        for expert in range(experts):
            part = projected[:, expert * head_dim : (expert + 1) * head_dim]
            query_first = query_first + jnp.where(first == expert, part, 0.0)
            query_second = query_second + jnp.where(second == expert, part, 0.0)
        top = block * block_rows
        out_ref[top : top + rows, 0:head_dim] = query_first
        out_ref[top : top + rows, head_dim : 2 * head_dim] = query_second
        out_ref[top : top + rows, 2 * head_dim :] = projected[:, experts * head_dim :]
        widened_t = jnp.transpose(widened)
        squares_row = jnp.sum(widened_t * widened_t, axis=0, keepdims=True)
        logits_t = lax.dot_general(
            router_ref[...], scaled, contract_last, preferred_element_type=jnp.float32
        )
        expert_row = lax.broadcasted_iota(jnp.int32, logits_t.shape, 0)
        route_t = route_t_ref[:, pl.ds(first_row, rows)]
        chosen_first = jnp.sum(
            jnp.where(expert_row == route_t[0:1, :], logits_t, 0.0), axis=0, keepdims=True
        )
        chosen_second = jnp.sum(
            jnp.where(expert_row == route_t[1:2, :], logits_t, 0.0), axis=0, keepdims=True
        )
        out_ref[top + rows : top + block_rows, :] = jnp.zeros((EXTRA_ROWS, out_ref.shape[1]), jnp.float32)
        out_ref[top + rows : top + rows + 1, 0:rows] = chosen_first
        out_ref[top + rows : top + rows + 1, rows : 2 * rows] = chosen_second
        out_ref[top + rows : top + rows + 1, 2 * rows : 3 * rows] = squares_row


EXTRA_ROWS = 8
REQUESTS_PER_STEP = 4


def packed_partials(order, gathered, gain, w_router, query_weight, keyval_weight, route):
    total_rows, width = gathered.shape
    requests = order.shape[0]
    rows = total_rows // requests
    experts, _, head_dim = query_weight.shape
    keyval_cols = keyval_weight.shape[1]
    packed_cols = 2 * head_dim + keyval_cols
    assert 3 * rows <= packed_cols and keyval_cols == 2 * head_dim
    block_rows = rows + EXTRA_ROWS
    weight = jnp.concatenate(
        [jnp.transpose(query_weight, (1, 0, 2)).reshape(width, experts * head_dim), keyval_weight],
        axis=1,
    )
    flops = 2 * total_rows * width * (weight.shape[1] + w_router.shape[1])
    moved = 2 * total_rows * width + 4 * requests * block_rows * packed_cols + 2 * weight.size
    whole = lambda shape: pl.BlockSpec(shape, lambda s, order_ref: (0,) * len(shape))
    route_t = jnp.transpose(route)
    return pl.pallas_call(
        pack_kernel,
        out_shape=jax.ShapeDtypeStruct((requests * block_rows, packed_cols), jnp.float32),
        grid_spec=pltpu.PrefetchScalarGridSpec(
            num_scalar_prefetch=1,
            grid=(requests // REQUESTS_PER_STEP,),
            in_specs=[
                whole(gathered.shape),
                whole((1, width)),
                whole((w_router.shape[1], width)),
                whole(weight.shape),
                whole(route.shape),
                whole(route_t.shape),
            ],
            out_specs=pl.BlockSpec(
                (REQUESTS_PER_STEP * block_rows, packed_cols), lambda s, order_ref: (s, 0)
            ),
        ),
        cost_estimate=pl.CostEstimate(flops=flops, transcendentals=0, bytes_accessed=moved),
    )(order, gathered, gain.reshape(1, width), jnp.transpose(w_router), weight, route, route_t)


def attend_kernel(length_ref, blocks_ref, cache_k_ref, cache_v_ref, out_ref):
    members, block_rows, packed_cols = blocks_ref.shape
    rows = block_rows - EXTRA_ROWS
    head_dim = cache_k_ref.shape[1]
    full_width = members * LANES
    summed = blocks_ref[0]
    for member in range(1, members):
        summed = summed + blocks_ref[member]
    partials = summed[0:rows]
    extra = summed[rows:block_rows]
    extra_t = jnp.transpose(extra)
    inverse_col = lax.rsqrt(extra_t[2 * rows : 3 * rows, 0:1] / full_width + norm_eps)
    inverse_row = lax.rsqrt(extra[0:1, 2 * rows : 3 * rows] / full_width + norm_eps)
    gate_gap = extra[0:1, 0:rows] * inverse_row - extra[0:1, rows : 2 * rows] * inverse_row
    gate_row = jnp.concatenate([jax.nn.sigmoid(gate_gap), jax.nn.sigmoid(-gate_gap)], axis=1)
    gate_row = gate_row.astype(jnp.bfloat16).astype(jnp.float32)
    scaled = partials * inverse_col
    query = jnp.concatenate(
        [scaled[:, 0:head_dim], scaled[:, head_dim : 2 * head_dim]], axis=0
    ).astype(jnp.bfloat16)
    fresh_keys = scaled[:, 2 * head_dim : 3 * head_dim].astype(jnp.bfloat16)
    fresh_values = scaled[:, 3 * head_dim : 4 * head_dim].astype(jnp.bfloat16)
    score_scale = head_dim ** (-0.5)
    contract_last = (((1,), (1,)), ((), ()))
    cached = lax.dot_general(query, cache_k_ref[...], contract_last, preferred_element_type=jnp.float32)
    cached = cached * score_scale
    key_col = lax.broadcasted_iota(jnp.int32, cached.shape, 1)
    cached = jnp.where(key_col < length_ref[0], cached, masked_score)
    fresh = lax.dot_general(query, fresh_keys, contract_last, preferred_element_type=jnp.float32)
    fresh = fresh * score_scale
    fresh_col = lax.broadcasted_iota(jnp.int32, fresh.shape, 1)
    query_token = lax.broadcasted_iota(jnp.int32, fresh.shape, 0) % rows
    fresh = jnp.where(fresh_col <= query_token, fresh, masked_score)
    top = jnp.maximum(
        jnp.max(cached, axis=1, keepdims=True), jnp.max(fresh, axis=1, keepdims=True)
    )
    cached_weights = jnp.exp(cached - top)
    fresh_weights = jnp.exp(fresh - top)
    denominator = jnp.sum(cached_weights, axis=1, keepdims=True) + jnp.sum(
        fresh_weights, axis=1, keepdims=True
    )
    attended = jnp.dot(
        cached_weights.astype(jnp.bfloat16), cache_v_ref[...], preferred_element_type=jnp.float32
    ) + jnp.dot(fresh_weights.astype(jnp.bfloat16), fresh_values, preferred_element_type=jnp.float32)
    attended = (attended / denominator).astype(jnp.bfloat16)
    first_slot = attended[0:rows]
    second_slot = attended[rows : 2 * rows]
    extra_row = lax.broadcasted_iota(jnp.int32, (EXTRA_ROWS, 2 * rows), 0)
    gate_block = jnp.where(
        extra_row == 0, jnp.broadcast_to(gate_row, (EXTRA_ROWS, 2 * rows)), 0.0
    ).astype(jnp.bfloat16)
    for member in range(out_ref.shape[0]):
        out_ref[member, 0:rows, 0:head_dim] = first_slot
        out_ref[member, 0:rows, head_dim : 2 * head_dim] = second_slot
        out_ref[member, rows:block_rows, :] = gate_block


def attend(length, blocks, cache_k, cache_v):
    members, block_rows, packed_cols = blocks.shape
    rows = block_rows - EXTRA_ROWS
    span, head_dim = cache_k.shape
    full = lambda shape: pl.BlockSpec(shape, lambda i, length_ref: (0,) * len(shape))
    out_shape = (members, block_rows, 2 * head_dim)
    keys = span + rows
    query_rows = 2 * rows
    return pl.pallas_call(
        attend_kernel,
        out_shape=jax.ShapeDtypeStruct(out_shape, jnp.bfloat16),
        grid_spec=pltpu.PrefetchScalarGridSpec(
            num_scalar_prefetch=1,
            grid=(1,),
            in_specs=[full(blocks.shape), full(cache_k.shape), full(cache_v.shape)],
            out_specs=full(out_shape),
        ),
        cost_estimate=pl.CostEstimate(
            flops=4 * query_rows * keys * head_dim,
            transcendentals=query_rows * keys,
            bytes_accessed=4 * blocks.size + 4 * span * head_dim + 2 * members * block_rows * 2 * head_dim,
        ),
    )(length.reshape(1), blocks, cache_k, cache_v)


def per_device(
    tokens,
    gain,
    w_router,
    expert_query_weight,
    key_value_weight,
    expert_output_weight,
    cache_keys,
    cached_value_slots,
    lengths,
    deal,
    route,
):
    requests = lengths.shape[0]
    experts = expert_query_weight.shape[0]
    heads_local = expert_query_weight.shape[2]
    head_dim = expert_query_weight.shape[3]
    top_count = route.shape[1]
    gathered = lax.all_gather(tokens, TOKEN_AXES, axis=0, tiled=True)
    total_rows, local_width = gathered.shape
    new_len = total_rows // requests
    full_width = local_width * lax.axis_size("gx")
    slot_index = lax.axis_index("gx")
    inverse = jnp.zeros((requests,), jnp.int32).at[deal].set(jnp.arange(requests, dtype=jnp.int32))
    assert heads_local == 1
    packed = packed_partials(
        inverse,
        gathered,
        gain,
        w_router,
        expert_query_weight.reshape(experts, local_width, head_dim),
        key_value_weight.reshape(local_width, 2 * head_dim),
        route,
    )
    query_cols = top_count * heads_local * head_dim
    keyval_cols = heads_local * 2 * head_dim
    members = lax.axis_size("gx")
    blocks = lax.all_to_all(
        packed.reshape(members, packed.shape[0] // members, packed.shape[1]), "gx", 0, 0, tiled=True
    )
    length = jnp.take(lengths, jnp.take(inverse, slot_index))
    copies = attend(length, blocks, cache_keys[0, 0], cached_value_slots[0, 0])
    extra_rows = EXTRA_ROWS
    all_shipped = lax.all_to_all(copies, "gx", 0, 0, tiled=True).reshape(
        requests, new_len + extra_rows, query_cols
    )
    cores = lax.axis_size("cc")
    chips = lax.axis_size("zz")
    staged = jnp.arange(requests, dtype=jnp.int32).reshape(chips, cores).T.reshape(requests)
    by_request = jnp.take(all_shipped, jnp.take(deal, staged), axis=0)
    route = jnp.take(route.reshape(requests, new_len, top_count), staged, axis=0).reshape(
        total_rows, top_count
    )
    token_attended = by_request[:, :new_len].reshape(total_rows, top_count, heads_local, head_dim)
    token_gates = (
        jnp.transpose(
            by_request[:, new_len, : top_count * new_len].reshape(requests, top_count, new_len),
            (0, 2, 1),
        )
        .reshape(total_rows, top_count)
        .astype(jnp.float32)
    )
    onehot = expert_onehot(route, experts)
    routed_attended = token_attended[:, :, None, :, :] * onehot[:, :, :, None, None].astype(
        jnp.bfloat16
    )
    projected = jnp.einsum(
        "tsehk,ehko->tso", routed_attended, expert_output_weight, preferred_element_type=jnp.float32
    )
    mixed_part = jnp.sum(token_gates[:, :, None] * projected, axis=1)
    output_sum = scatter_sum(scatter_sum(mixed_part, "cc"), "zz")
    return output_sum.astype(jnp.bfloat16)


TOKEN_AXES = ("zz", "cc")


def solution(mesh):
    gx_size, gy_size = mesh.devices.shape
    staged_mesh = Mesh(mesh.devices.reshape(gx_size, gy_size // 2, 2), ("gx",) + TOKEN_AXES)
    gy = TOKEN_AXES
    placed = (
        P(gy, "gx"),
        P("gx"),
        P("gx", None),
        P(None, "gx", gy, None),
        P("gx", gy, None),
        P(None, gy, None, "gx"),
        P("gx", gy, None, None),
        P("gx", gy, None, None),
        P(),
        P(),
        P(),
    )
    return jax.shard_map(
        per_device, mesh=staged_mesh, in_specs=placed, out_specs=P(gy, "gx"), check_vma=False
    )
```

```python
import jax
import jax.numpy as jnp
from jax import lax
from jax.experimental import pallas as pl
from jax.experimental.pallas import tpu as pltpu
from jax.sharding import Mesh, PartitionSpec as P

masked_score = -1e30
norm_eps = 1e-06
LANES = 128


def expert_onehot(route_rows, experts):
    return (route_rows[:, :, None] == jnp.arange(experts, dtype=jnp.int32)[None, None, :]).astype(
        jnp.float32
    )


def padded_width(width):
    return -(-width // LANES) * LANES


def scatter_sum(part, axis_name):
    members = lax.axis_size(axis_name)
    blocks = lax.all_to_all(
        part.reshape((members, part.shape[0] // members) + part.shape[1:]),
        axis_name,
        0,
        0,
        tiled=True,
    )
    return jnp.sum(blocks, axis=0)


def gather_rows(piece, axis_name):
    members = lax.axis_size(axis_name)
    copies = jnp.broadcast_to(piece[None], (members,) + piece.shape)
    gathered = lax.all_to_all(copies, axis_name, 0, 0, tiled=True)
    return gathered.reshape((members * piece.shape[0],) + piece.shape[1:])


def pack_kernel(order_ref, tok_ref, gain_ref, router_ref, weight_ref, route_ref, route_t_ref, out_ref):
    rows = tok_ref.shape[0] // order_ref.shape[0]
    block_rows = rows + EXTRA_ROWS
    head_dim = out_ref.shape[1] // 4
    experts = (weight_ref.shape[1] - 2 * head_dim) // head_dim
    contract_last = (((1,), (1,)), ((), ()))
    step = pl.program_id(0)
    for block in range(REQUESTS_PER_STEP):
        first_row = pl.multiple_of(order_ref[step * REQUESTS_PER_STEP + block] * rows, rows)
        widened = tok_ref[pl.ds(first_row, rows), :].astype(jnp.float32)
        scaled = (widened * gain_ref[...].astype(jnp.float32)).astype(jnp.bfloat16)
        projected = jnp.dot(scaled, weight_ref[...], preferred_element_type=jnp.float32)
        route = route_ref[pl.ds(first_row, rows), :]
        first = route[:, 0:1]
        second = route[:, 1:2]
        query_first = jnp.zeros((rows, head_dim), jnp.float32)
        query_second = jnp.zeros((rows, head_dim), jnp.float32)
        for expert in range(experts):
            part = projected[:, expert * head_dim : (expert + 1) * head_dim]
            query_first = query_first + jnp.where(first == expert, part, 0.0)
            query_second = query_second + jnp.where(second == expert, part, 0.0)
        top = block * block_rows
        out_ref[top : top + rows, 0:head_dim] = query_first
        out_ref[top : top + rows, head_dim : 2 * head_dim] = query_second
        out_ref[top : top + rows, 2 * head_dim :] = projected[:, experts * head_dim :]
        widened_t = jnp.transpose(widened)
        squares_row = jnp.sum(widened_t * widened_t, axis=0, keepdims=True)
        logits_t = lax.dot_general(
            router_ref[...], scaled, contract_last, preferred_element_type=jnp.float32
        )
        expert_row = lax.broadcasted_iota(jnp.int32, logits_t.shape, 0)
        route_t = route_t_ref[:, pl.ds(first_row, rows)]
        chosen_first = jnp.sum(
            jnp.where(expert_row == route_t[0:1, :], logits_t, 0.0), axis=0, keepdims=True
        )
        chosen_second = jnp.sum(
            jnp.where(expert_row == route_t[1:2, :], logits_t, 0.0), axis=0, keepdims=True
        )
        out_ref[top + rows : top + block_rows, :] = jnp.zeros((EXTRA_ROWS, out_ref.shape[1]), jnp.float32)
        out_ref[top + rows : top + rows + 1, 0:rows] = chosen_first
        out_ref[top + rows : top + rows + 1, rows : 2 * rows] = chosen_second
        out_ref[top + rows : top + rows + 1, 2 * rows : 3 * rows] = squares_row


EXTRA_ROWS = 8
REQUESTS_PER_STEP = 4


def packed_partials(order, gathered, gain, w_router, query_weight, keyval_weight, route):
    total_rows, width = gathered.shape
    requests = order.shape[0]
    rows = total_rows // requests
    experts, _, head_dim = query_weight.shape
    keyval_cols = keyval_weight.shape[1]
    packed_cols = 2 * head_dim + keyval_cols
    assert 3 * rows <= packed_cols and keyval_cols == 2 * head_dim
    block_rows = rows + EXTRA_ROWS
    weight = jnp.concatenate(
        [jnp.transpose(query_weight, (1, 0, 2)).reshape(width, experts * head_dim), keyval_weight],
        axis=1,
    )
    flops = 2 * total_rows * width * (weight.shape[1] + w_router.shape[1])
    moved = 2 * total_rows * width + 4 * requests * block_rows * packed_cols + 2 * weight.size
    whole = lambda shape: pl.BlockSpec(shape, lambda s, order_ref: (0,) * len(shape))
    route_t = jnp.transpose(route)
    return pl.pallas_call(
        pack_kernel,
        out_shape=jax.ShapeDtypeStruct((requests * block_rows, packed_cols), jnp.float32),
        grid_spec=pltpu.PrefetchScalarGridSpec(
            num_scalar_prefetch=1,
            grid=(requests // REQUESTS_PER_STEP,),
            in_specs=[
                whole(gathered.shape),
                whole((1, width)),
                whole((w_router.shape[1], width)),
                whole(weight.shape),
                whole(route.shape),
                whole(route_t.shape),
            ],
            out_specs=pl.BlockSpec(
                (REQUESTS_PER_STEP * block_rows, packed_cols), lambda s, order_ref: (s, 0)
            ),
        ),
        cost_estimate=pl.CostEstimate(flops=flops, transcendentals=0, bytes_accessed=moved),
    )(order, gathered, gain.reshape(1, width), jnp.transpose(w_router), weight, route, route_t)


def attend_kernel(length_ref, blocks_ref, cache_k_ref, cache_v_ref, out_ref):
    members, block_rows, packed_cols = blocks_ref.shape
    rows = block_rows - EXTRA_ROWS
    head_dim = cache_k_ref.shape[1]
    full_width = members * LANES
    summed = blocks_ref[0]
    for member in range(1, members):
        summed = summed + blocks_ref[member]
    partials = summed[0:rows]
    extra = summed[rows:block_rows]
    extra_t = jnp.transpose(extra)
    inverse_col = lax.rsqrt(extra_t[2 * rows : 3 * rows, 0:1] / full_width + norm_eps)
    inverse_row = lax.rsqrt(extra[0:1, 2 * rows : 3 * rows] / full_width + norm_eps)
    gate_gap = extra[0:1, 0:rows] * inverse_row - extra[0:1, rows : 2 * rows] * inverse_row
    gate_row = jnp.concatenate([jax.nn.sigmoid(gate_gap), jax.nn.sigmoid(-gate_gap)], axis=1)
    gate_row = gate_row.astype(jnp.bfloat16).astype(jnp.float32)
    scaled = partials * inverse_col
    query = jnp.concatenate(
        [scaled[:, 0:head_dim], scaled[:, head_dim : 2 * head_dim]], axis=0
    ).astype(jnp.bfloat16)
    fresh_keys = scaled[:, 2 * head_dim : 3 * head_dim].astype(jnp.bfloat16)
    fresh_values = scaled[:, 3 * head_dim : 4 * head_dim].astype(jnp.bfloat16)
    score_scale = head_dim ** (-0.5)
    contract_last = (((1,), (1,)), ((), ()))
    cached = lax.dot_general(query, cache_k_ref[...], contract_last, preferred_element_type=jnp.float32)
    cached = cached * score_scale
    key_col = lax.broadcasted_iota(jnp.int32, cached.shape, 1)
    cached = jnp.where(key_col < length_ref[0], cached, masked_score)
    fresh = lax.dot_general(query, fresh_keys, contract_last, preferred_element_type=jnp.float32)
    fresh = fresh * score_scale
    fresh_col = lax.broadcasted_iota(jnp.int32, fresh.shape, 1)
    query_token = lax.broadcasted_iota(jnp.int32, fresh.shape, 0) % rows
    fresh = jnp.where(fresh_col <= query_token, fresh, masked_score)
    top = jnp.maximum(
        jnp.max(cached, axis=1, keepdims=True), jnp.max(fresh, axis=1, keepdims=True)
    )
    cached_weights = jnp.exp(cached - top)
    fresh_weights = jnp.exp(fresh - top)
    denominator = jnp.sum(cached_weights, axis=1, keepdims=True) + jnp.sum(
        fresh_weights, axis=1, keepdims=True
    )
    attended = jnp.dot(
        cached_weights.astype(jnp.bfloat16), cache_v_ref[...], preferred_element_type=jnp.float32
    ) + jnp.dot(fresh_weights.astype(jnp.bfloat16), fresh_values, preferred_element_type=jnp.float32)
    attended = (attended / denominator).astype(jnp.bfloat16)
    first_slot = attended[0:rows]
    second_slot = attended[rows : 2 * rows]
    extra_row = lax.broadcasted_iota(jnp.int32, (EXTRA_ROWS, 2 * rows), 0)
    gate_block = jnp.where(
        extra_row == 0, jnp.broadcast_to(gate_row, (EXTRA_ROWS, 2 * rows)), 0.0
    ).astype(jnp.bfloat16)
    for member in range(out_ref.shape[0]):
        out_ref[member, 0:rows, 0:head_dim] = first_slot
        out_ref[member, 0:rows, head_dim : 2 * head_dim] = second_slot
        out_ref[member, rows:block_rows, :] = gate_block


def attend(length, blocks, cache_k, cache_v):
    members, block_rows, packed_cols = blocks.shape
    rows = block_rows - EXTRA_ROWS
    span, head_dim = cache_k.shape
    full = lambda shape: pl.BlockSpec(shape, lambda i, length_ref: (0,) * len(shape))
    out_shape = (members, block_rows, 2 * head_dim)
    keys = span + rows
    query_rows = 2 * rows
    return pl.pallas_call(
        attend_kernel,
        out_shape=jax.ShapeDtypeStruct(out_shape, jnp.bfloat16),
        grid_spec=pltpu.PrefetchScalarGridSpec(
            num_scalar_prefetch=1,
            grid=(1,),
            in_specs=[full(blocks.shape), full(cache_k.shape), full(cache_v.shape)],
            out_specs=full(out_shape),
        ),
        cost_estimate=pl.CostEstimate(
            flops=4 * query_rows * keys * head_dim,
            transcendentals=query_rows * keys,
            bytes_accessed=4 * blocks.size + 4 * span * head_dim + 2 * members * block_rows * 2 * head_dim,
        ),
    )(length.reshape(1), blocks, cache_k, cache_v)


def per_device(
    tokens,
    gain,
    w_router,
    expert_query_weight,
    key_value_weight,
    expert_output_weight,
    cache_keys,
    cached_value_slots,
    lengths,
    deal,
    route,
):
    requests = lengths.shape[0]
    experts = expert_query_weight.shape[0]
    heads_local = expert_query_weight.shape[2]
    head_dim = expert_query_weight.shape[3]
    top_count = route.shape[1]
    gathered = lax.all_gather(
        lax.all_gather(tokens, TOKEN_AXES[1], axis=0, tiled=True), TOKEN_AXES[0], axis=0, tiled=True
    )
    total_rows, local_width = gathered.shape
    new_len = total_rows // requests
    full_width = local_width * lax.axis_size("gx")
    slot_index = lax.axis_index("gx")
    inverse = jnp.zeros((requests,), jnp.int32).at[deal].set(jnp.arange(requests, dtype=jnp.int32))
    assert heads_local == 1
    packed = packed_partials(
        inverse,
        gathered,
        gain,
        w_router,
        expert_query_weight.reshape(experts, local_width, head_dim),
        key_value_weight.reshape(local_width, 2 * head_dim),
        route,
    )
    query_cols = top_count * heads_local * head_dim
    keyval_cols = heads_local * 2 * head_dim
    members = lax.axis_size("gx")
    blocks = lax.all_to_all(
        packed.reshape(members, packed.shape[0] // members, packed.shape[1]), "gx", 0, 0, tiled=True
    )
    length = jnp.take(lengths, jnp.take(inverse, slot_index))
    copies = attend(length, blocks, cache_keys[0, 0], cached_value_slots[0, 0])
    extra_rows = EXTRA_ROWS
    all_shipped = lax.all_to_all(copies, "gx", 0, 0, tiled=True).reshape(
        requests, new_len + extra_rows, query_cols
    )
    cores = lax.axis_size("cc")
    chips = lax.axis_size("zz")
    staged = jnp.arange(requests, dtype=jnp.int32).reshape(chips, cores).T.reshape(requests)
    by_request = jnp.take(all_shipped, jnp.take(deal, staged), axis=0)
    route = jnp.take(route.reshape(requests, new_len, top_count), staged, axis=0).reshape(
        total_rows, top_count
    )
    token_attended = by_request[:, :new_len].reshape(total_rows, top_count, heads_local, head_dim)
    token_gates = (
        jnp.transpose(
            by_request[:, new_len, : top_count * new_len].reshape(requests, top_count, new_len),
            (0, 2, 1),
        )
        .reshape(total_rows, top_count)
        .astype(jnp.float32)
    )
    onehot = expert_onehot(route, experts)
    routed_attended = token_attended[:, :, None, :, :] * onehot[:, :, :, None, None].astype(
        jnp.bfloat16
    )
    projected = jnp.einsum(
        "tsehk,ehko->tso", routed_attended, expert_output_weight, preferred_element_type=jnp.float32
    )
    mixed_part = jnp.sum(token_gates[:, :, None] * projected, axis=1)
    output_sum = scatter_sum(scatter_sum(mixed_part, "cc"), "zz")
    return output_sum.astype(jnp.bfloat16)


TOKEN_AXES = ("zz", "cc")


def solution(mesh):
    gx_size, gy_size = mesh.devices.shape
    staged_mesh = Mesh(mesh.devices.reshape(gx_size, gy_size // 2, 2), ("gx",) + TOKEN_AXES)
    gy = TOKEN_AXES
    placed = (
        P(gy, "gx"),
        P("gx"),
        P("gx", None),
        P(None, "gx", gy, None),
        P("gx", gy, None),
        P(None, gy, None, "gx"),
        P("gx", gy, None, None),
        P("gx", gy, None, None),
        P(),
        P(),
        P(),
    )
    return jax.shard_map(
        per_device, mesh=staged_mesh, in_specs=placed, out_specs=P(gy, "gx"), check_vma=False
    )
```

```python
import jax
import jax.numpy as jnp
from jax import lax
from jax.experimental import pallas as pl
from jax.experimental.pallas import tpu as pltpu
from jax.sharding import Mesh, PartitionSpec as P

masked_score = -1e30
norm_eps = 1e-06
LANES = 128


def expert_onehot(route_rows, experts):
    return (route_rows[:, :, None] == jnp.arange(experts, dtype=jnp.int32)[None, None, :]).astype(
        jnp.float32
    )


def padded_width(width):
    return -(-width // LANES) * LANES


def scatter_sum(part, axis_name):
    members = lax.axis_size(axis_name)
    blocks = lax.all_to_all(
        part.reshape((members, part.shape[0] // members) + part.shape[1:]),
        axis_name,
        0,
        0,
        tiled=True,
    )
    return jnp.sum(blocks, axis=0)


def gather_rows(piece, axis_name):
    members = lax.axis_size(axis_name)
    copies = jnp.broadcast_to(piece[None], (members,) + piece.shape)
    gathered = lax.all_to_all(copies, axis_name, 0, 0, tiled=True)
    return gathered.reshape((members * piece.shape[0],) + piece.shape[1:])


def pack_kernel(
    order_ref, token_order_ref, tok_ref, gain_ref, router_ref, weight_ref, route_ref, route_t_ref, out_ref
):
    rows = tok_ref.shape[0] // order_ref.shape[0]
    block_rows = rows + EXTRA_ROWS
    head_dim = out_ref.shape[1] // 4
    experts = (weight_ref.shape[1] - 2 * head_dim) // head_dim
    contract_last = (((1,), (1,)), ((), ()))
    step = pl.program_id(0)
    for block in range(REQUESTS_PER_STEP):
        first_row = pl.multiple_of(order_ref[step * REQUESTS_PER_STEP + block] * rows, rows)
        token_row = pl.multiple_of(token_order_ref[step * REQUESTS_PER_STEP + block] * rows, rows)
        widened = tok_ref[pl.ds(token_row, rows), :].astype(jnp.float32)
        scaled = (widened * gain_ref[...].astype(jnp.float32)).astype(jnp.bfloat16)
        projected = jnp.dot(scaled, weight_ref[...], preferred_element_type=jnp.float32)
        route = route_ref[pl.ds(first_row, rows), :]
        first = route[:, 0:1]
        second = route[:, 1:2]
        query_first = jnp.zeros((rows, head_dim), jnp.float32)
        query_second = jnp.zeros((rows, head_dim), jnp.float32)
        for expert in range(experts):
            part = projected[:, expert * head_dim : (expert + 1) * head_dim]
            query_first = query_first + jnp.where(first == expert, part, 0.0)
            query_second = query_second + jnp.where(second == expert, part, 0.0)
        top = block * block_rows
        out_ref[top : top + rows, 0:head_dim] = query_first
        out_ref[top : top + rows, head_dim : 2 * head_dim] = query_second
        out_ref[top : top + rows, 2 * head_dim :] = projected[:, experts * head_dim :]
        widened_t = jnp.transpose(widened)
        squares_row = jnp.sum(widened_t * widened_t, axis=0, keepdims=True)
        logits_t = lax.dot_general(
            router_ref[...], scaled, contract_last, preferred_element_type=jnp.float32
        )
        expert_row = lax.broadcasted_iota(jnp.int32, logits_t.shape, 0)
        route_t = route_t_ref[:, pl.ds(first_row, rows)]
        chosen_first = jnp.sum(
            jnp.where(expert_row == route_t[0:1, :], logits_t, 0.0), axis=0, keepdims=True
        )
        chosen_second = jnp.sum(
            jnp.where(expert_row == route_t[1:2, :], logits_t, 0.0), axis=0, keepdims=True
        )
        out_ref[top + rows : top + block_rows, :] = jnp.zeros((EXTRA_ROWS, out_ref.shape[1]), jnp.float32)
        out_ref[top + rows : top + rows + 1, 0:rows] = chosen_first
        out_ref[top + rows : top + rows + 1, rows : 2 * rows] = chosen_second
        out_ref[top + rows : top + rows + 1, 2 * rows : 3 * rows] = squares_row


EXTRA_ROWS = 8
REQUESTS_PER_STEP = 4


def packed_partials(order, token_order, gathered, gain, w_router, query_weight, keyval_weight, route):
    total_rows, width = gathered.shape
    requests = order.shape[0]
    rows = total_rows // requests
    experts, _, head_dim = query_weight.shape
    keyval_cols = keyval_weight.shape[1]
    packed_cols = 2 * head_dim + keyval_cols
    assert 3 * rows <= packed_cols and keyval_cols == 2 * head_dim
    block_rows = rows + EXTRA_ROWS
    weight = jnp.concatenate(
        [jnp.transpose(query_weight, (1, 0, 2)).reshape(width, experts * head_dim), keyval_weight],
        axis=1,
    )
    flops = 2 * total_rows * width * (weight.shape[1] + w_router.shape[1])
    moved = 2 * total_rows * width + 4 * requests * block_rows * packed_cols + 2 * weight.size
    whole = lambda shape: pl.BlockSpec(shape, lambda s, order_ref, token_ref: (0,) * len(shape))
    route_t = jnp.transpose(route)
    return pl.pallas_call(
        pack_kernel,
        out_shape=jax.ShapeDtypeStruct((requests * block_rows, packed_cols), jnp.float32),
        grid_spec=pltpu.PrefetchScalarGridSpec(
            num_scalar_prefetch=2,
            grid=(requests // REQUESTS_PER_STEP,),
            in_specs=[
                whole(gathered.shape),
                whole((1, width)),
                whole((w_router.shape[1], width)),
                whole(weight.shape),
                whole(route.shape),
                whole(route_t.shape),
            ],
            out_specs=pl.BlockSpec(
                (REQUESTS_PER_STEP * block_rows, packed_cols), lambda s, order_ref, token_ref: (s, 0)
            ),
        ),
        cost_estimate=pl.CostEstimate(flops=flops, transcendentals=0, bytes_accessed=moved),
    )(order, token_order, gathered, gain.reshape(1, width), jnp.transpose(w_router), weight, route, route_t)


def attend_kernel(length_ref, blocks_ref, cache_k_ref, cache_v_ref, out_ref):
    members, block_rows, packed_cols = blocks_ref.shape
    rows = block_rows - EXTRA_ROWS
    head_dim = cache_k_ref.shape[1]
    full_width = members * LANES
    summed = blocks_ref[0]
    for member in range(1, members):
        summed = summed + blocks_ref[member]
    partials = summed[0:rows]
    extra = summed[rows:block_rows]
    extra_t = jnp.transpose(extra)
    inverse_col = lax.rsqrt(extra_t[2 * rows : 3 * rows, 0:1] / full_width + norm_eps)
    inverse_row = lax.rsqrt(extra[0:1, 2 * rows : 3 * rows] / full_width + norm_eps)
    gate_gap = extra[0:1, 0:rows] * inverse_row - extra[0:1, rows : 2 * rows] * inverse_row
    gate_row = jnp.concatenate([jax.nn.sigmoid(gate_gap), jax.nn.sigmoid(-gate_gap)], axis=1)
    gate_row = gate_row.astype(jnp.bfloat16).astype(jnp.float32)
    scaled = partials * inverse_col
    query = jnp.concatenate(
        [scaled[:, 0:head_dim], scaled[:, head_dim : 2 * head_dim]], axis=0
    ).astype(jnp.bfloat16)
    fresh_keys = scaled[:, 2 * head_dim : 3 * head_dim].astype(jnp.bfloat16)
    fresh_values = scaled[:, 3 * head_dim : 4 * head_dim].astype(jnp.bfloat16)
    score_scale = head_dim ** (-0.5)
    contract_last = (((1,), (1,)), ((), ()))
    cached = lax.dot_general(query, cache_k_ref[...], contract_last, preferred_element_type=jnp.float32)
    cached = cached * score_scale
    key_col = lax.broadcasted_iota(jnp.int32, cached.shape, 1)
    cached = jnp.where(key_col < length_ref[0], cached, masked_score)
    fresh = lax.dot_general(query, fresh_keys, contract_last, preferred_element_type=jnp.float32)
    fresh = fresh * score_scale
    fresh_col = lax.broadcasted_iota(jnp.int32, fresh.shape, 1)
    query_token = lax.broadcasted_iota(jnp.int32, fresh.shape, 0) % rows
    fresh = jnp.where(fresh_col <= query_token, fresh, masked_score)
    top = jnp.maximum(
        jnp.max(cached, axis=1, keepdims=True), jnp.max(fresh, axis=1, keepdims=True)
    )
    cached_weights = jnp.exp(cached - top)
    fresh_weights = jnp.exp(fresh - top)
    denominator = jnp.sum(cached_weights, axis=1, keepdims=True) + jnp.sum(
        fresh_weights, axis=1, keepdims=True
    )
    attended = jnp.dot(
        cached_weights.astype(jnp.bfloat16), cache_v_ref[...], preferred_element_type=jnp.float32
    ) + jnp.dot(fresh_weights.astype(jnp.bfloat16), fresh_values, preferred_element_type=jnp.float32)
    attended = (attended / denominator).astype(jnp.bfloat16)
    first_slot = attended[0:rows]
    second_slot = attended[rows : 2 * rows]
    extra_row = lax.broadcasted_iota(jnp.int32, (EXTRA_ROWS, 2 * rows), 0)
    gate_block = jnp.where(
        extra_row == 0, jnp.broadcast_to(gate_row, (EXTRA_ROWS, 2 * rows)), 0.0
    ).astype(jnp.bfloat16)
    for member in range(out_ref.shape[0]):
        out_ref[member, 0:rows, 0:head_dim] = first_slot
        out_ref[member, 0:rows, head_dim : 2 * head_dim] = second_slot
        out_ref[member, rows:block_rows, :] = gate_block


def attend(length, blocks, cache_k, cache_v):
    members, block_rows, packed_cols = blocks.shape
    rows = block_rows - EXTRA_ROWS
    span, head_dim = cache_k.shape
    full = lambda shape: pl.BlockSpec(shape, lambda i, length_ref: (0,) * len(shape))
    out_shape = (members, block_rows, 2 * head_dim)
    keys = span + rows
    query_rows = 2 * rows
    return pl.pallas_call(
        attend_kernel,
        out_shape=jax.ShapeDtypeStruct(out_shape, jnp.bfloat16),
        grid_spec=pltpu.PrefetchScalarGridSpec(
            num_scalar_prefetch=1,
            grid=(1,),
            in_specs=[full(blocks.shape), full(cache_k.shape), full(cache_v.shape)],
            out_specs=full(out_shape),
        ),
        cost_estimate=pl.CostEstimate(
            flops=4 * query_rows * keys * head_dim,
            transcendentals=query_rows * keys,
            bytes_accessed=4 * blocks.size + 4 * span * head_dim + 2 * members * block_rows * 2 * head_dim,
        ),
    )(length.reshape(1), blocks, cache_k, cache_v)


def per_device(
    tokens,
    gain,
    w_router,
    expert_query_weight,
    key_value_weight,
    expert_output_weight,
    cache_keys,
    cached_value_slots,
    lengths,
    deal,
    route,
):
    requests = lengths.shape[0]
    experts = expert_query_weight.shape[0]
    heads_local = expert_query_weight.shape[2]
    head_dim = expert_query_weight.shape[3]
    top_count = route.shape[1]
    gathered = lax.all_gather(
        lax.all_gather(tokens, TOKEN_AXES[0], axis=0, tiled=True), TOKEN_AXES[1], axis=0, tiled=True
    )
    total_rows, local_width = gathered.shape
    new_len = total_rows // requests
    full_width = local_width * lax.axis_size("gx")
    slot_index = lax.axis_index("gx")
    inverse = jnp.zeros((requests,), jnp.int32).at[deal].set(jnp.arange(requests, dtype=jnp.int32))
    assert heads_local == 1
    gather_cores = lax.axis_size(TOKEN_AXES[1])
    gather_chips = lax.axis_size(TOKEN_AXES[0])
    token_order = (inverse % gather_cores) * gather_chips + inverse // gather_cores
    packed = packed_partials(
        inverse,
        token_order,
        gathered,
        gain,
        w_router,
        expert_query_weight.reshape(experts, local_width, head_dim),
        key_value_weight.reshape(local_width, 2 * head_dim),
        route,
    )
    query_cols = top_count * heads_local * head_dim
    keyval_cols = heads_local * 2 * head_dim
    members = lax.axis_size("gx")
    blocks = lax.all_to_all(
        packed.reshape(members, packed.shape[0] // members, packed.shape[1]), "gx", 0, 0, tiled=True
    )
    length = jnp.take(lengths, jnp.take(inverse, slot_index))
    copies = attend(length, blocks, cache_keys[0, 0], cached_value_slots[0, 0])
    extra_rows = EXTRA_ROWS
    all_shipped = lax.all_to_all(copies, "gx", 0, 0, tiled=True).reshape(
        requests, new_len + extra_rows, query_cols
    )
    cores = lax.axis_size("cc")
    chips = lax.axis_size("zz")
    staged = jnp.arange(requests, dtype=jnp.int32).reshape(chips, cores).T.reshape(requests)
    by_request = jnp.take(all_shipped, jnp.take(deal, staged), axis=0)
    route = jnp.take(route.reshape(requests, new_len, top_count), staged, axis=0).reshape(
        total_rows, top_count
    )
    token_attended = by_request[:, :new_len].reshape(total_rows, top_count, heads_local, head_dim)
    token_gates = (
        jnp.transpose(
            by_request[:, new_len, : top_count * new_len].reshape(requests, top_count, new_len),
            (0, 2, 1),
        )
        .reshape(total_rows, top_count)
        .astype(jnp.float32)
    )
    onehot = expert_onehot(route, experts)
    routed_attended = token_attended[:, :, None, :, :] * onehot[:, :, :, None, None].astype(
        jnp.bfloat16
    )
    projected = jnp.einsum(
        "tsehk,ehko->tso", routed_attended, expert_output_weight, preferred_element_type=jnp.float32
    )
    mixed_part = jnp.sum(token_gates[:, :, None] * projected, axis=1)
    output_sum = scatter_sum(scatter_sum(mixed_part, "cc"), "zz")
    return output_sum.astype(jnp.bfloat16)


TOKEN_AXES = ("zz", "cc")


def solution(mesh):
    gx_size, gy_size = mesh.devices.shape
    staged_mesh = Mesh(mesh.devices.reshape(gx_size, gy_size // 2, 2), ("gx",) + TOKEN_AXES)
    gy = TOKEN_AXES
    placed = (
        P(gy, "gx"),
        P("gx"),
        P("gx", None),
        P(None, "gx", gy, None),
        P("gx", gy, None),
        P(None, gy, None, "gx"),
        P("gx", gy, None, None),
        P("gx", gy, None, None),
        P(),
        P(),
        P(),
    )
    return jax.shard_map(
        per_device, mesh=staged_mesh, in_specs=placed, out_specs=P(gy, "gx"), check_vma=False
    )
```

```python
import jax
import jax.numpy as jnp
from jax import lax
from jax.experimental import pallas as pl
from jax.experimental.pallas import tpu as pltpu
from jax.sharding import Mesh, PartitionSpec as P

masked_score = -1e30
norm_eps = 1e-06
LANES = 128


def expert_onehot(route_rows, experts):
    return (route_rows[:, :, None] == jnp.arange(experts, dtype=jnp.int32)[None, None, :]).astype(
        jnp.float32
    )


def padded_width(width):
    return -(-width // LANES) * LANES


def scatter_sum(part, axis_name):
    members = lax.axis_size(axis_name)
    blocks = lax.all_to_all(
        part.reshape((members, part.shape[0] // members) + part.shape[1:]),
        axis_name,
        0,
        0,
        tiled=True,
    )
    return jnp.sum(blocks, axis=0)


def gather_rows(piece, axis_name):
    members = lax.axis_size(axis_name)
    copies = jnp.broadcast_to(piece[None], (members,) + piece.shape)
    gathered = lax.all_to_all(copies, axis_name, 0, 0, tiled=True)
    return gathered.reshape((members * piece.shape[0],) + piece.shape[1:])


def pack_kernel(order_ref, tok_ref, gain_ref, router_ref, weight_ref, route_ref, route_t_ref, out_ref):
    rows = tok_ref.shape[0] // order_ref.shape[0]
    block_rows = rows + EXTRA_ROWS
    head_dim = out_ref.shape[1] // 4
    experts = (weight_ref.shape[1] - 2 * head_dim) // head_dim
    contract_last = (((1,), (1,)), ((), ()))
    step = pl.program_id(0)
    first_rows = [
        pl.multiple_of(order_ref[step * REQUESTS_PER_STEP + block] * rows, rows)
        for block in range(REQUESTS_PER_STEP)
    ]
    widened_all = jnp.concatenate(
        [tok_ref[pl.ds(first_row, rows), :] for first_row in first_rows], axis=0
    ).astype(jnp.float32)
    scaled_all = (widened_all * gain_ref[...].astype(jnp.float32)).astype(jnp.bfloat16)
    projected_all = jnp.dot(scaled_all, weight_ref[...], preferred_element_type=jnp.float32)
    for block in range(REQUESTS_PER_STEP):
        first_row = first_rows[block]
        widened = widened_all[block * rows : (block + 1) * rows]
        scaled = scaled_all[block * rows : (block + 1) * rows]
        projected = projected_all[block * rows : (block + 1) * rows]
        route = route_ref[pl.ds(first_row, rows), :]
        first = route[:, 0:1]
        second = route[:, 1:2]
        query_first = jnp.zeros((rows, head_dim), jnp.float32)
        query_second = jnp.zeros((rows, head_dim), jnp.float32)
        for expert in range(experts):
            part = projected[:, expert * head_dim : (expert + 1) * head_dim]
            query_first = query_first + jnp.where(first == expert, part, 0.0)
            query_second = query_second + jnp.where(second == expert, part, 0.0)
        top = block * block_rows
        out_ref[top : top + rows, 0:head_dim] = query_first
        out_ref[top : top + rows, head_dim : 2 * head_dim] = query_second
        out_ref[top : top + rows, 2 * head_dim :] = projected[:, experts * head_dim :]
        widened_t = jnp.transpose(widened)
        squares_row = jnp.sum(widened_t * widened_t, axis=0, keepdims=True)
        logits_t = lax.dot_general(
            router_ref[...], scaled, contract_last, preferred_element_type=jnp.float32
        )
        expert_row = lax.broadcasted_iota(jnp.int32, logits_t.shape, 0)
        route_t = route_t_ref[:, pl.ds(first_row, rows)]
        chosen_first = jnp.sum(
            jnp.where(expert_row == route_t[0:1, :], logits_t, 0.0), axis=0, keepdims=True
        )
        chosen_second = jnp.sum(
            jnp.where(expert_row == route_t[1:2, :], logits_t, 0.0), axis=0, keepdims=True
        )
        out_ref[top + rows : top + block_rows, :] = jnp.zeros((EXTRA_ROWS, out_ref.shape[1]), jnp.float32)
        out_ref[top + rows : top + rows + 1, 0:rows] = chosen_first
        out_ref[top + rows : top + rows + 1, rows : 2 * rows] = chosen_second
        out_ref[top + rows : top + rows + 1, 2 * rows : 3 * rows] = squares_row


EXTRA_ROWS = 8
REQUESTS_PER_STEP = 4


def packed_partials(order, gathered, gain, w_router, query_weight, keyval_weight, route):
    total_rows, width = gathered.shape
    requests = order.shape[0]
    rows = total_rows // requests
    experts, _, head_dim = query_weight.shape
    keyval_cols = keyval_weight.shape[1]
    packed_cols = 2 * head_dim + keyval_cols
    assert 3 * rows <= packed_cols and keyval_cols == 2 * head_dim
    block_rows = rows + EXTRA_ROWS
    weight = jnp.concatenate(
        [jnp.transpose(query_weight, (1, 0, 2)).reshape(width, experts * head_dim), keyval_weight],
        axis=1,
    )
    flops = 2 * total_rows * width * (weight.shape[1] + w_router.shape[1])
    moved = 2 * total_rows * width + 4 * requests * block_rows * packed_cols + 2 * weight.size
    whole = lambda shape: pl.BlockSpec(shape, lambda s, order_ref: (0,) * len(shape))
    route_t = jnp.transpose(route)
    return pl.pallas_call(
        pack_kernel,
        out_shape=jax.ShapeDtypeStruct((requests * block_rows, packed_cols), jnp.float32),
        grid_spec=pltpu.PrefetchScalarGridSpec(
            num_scalar_prefetch=1,
            grid=(requests // REQUESTS_PER_STEP,),
            in_specs=[
                whole(gathered.shape),
                whole((1, width)),
                whole((w_router.shape[1], width)),
                whole(weight.shape),
                whole(route.shape),
                whole(route_t.shape),
            ],
            out_specs=pl.BlockSpec(
                (REQUESTS_PER_STEP * block_rows, packed_cols), lambda s, order_ref: (s, 0)
            ),
        ),
        cost_estimate=pl.CostEstimate(flops=flops, transcendentals=0, bytes_accessed=moved),
    )(order, gathered, gain.reshape(1, width), jnp.transpose(w_router), weight, route, route_t)


def attend_kernel(length_ref, blocks_ref, cache_k_ref, cache_v_ref, out_ref):
    members, block_rows, packed_cols = blocks_ref.shape
    rows = block_rows - EXTRA_ROWS
    head_dim = cache_k_ref.shape[1]
    full_width = members * LANES
    summed = blocks_ref[0]
    for member in range(1, members):
        summed = summed + blocks_ref[member]
    partials = summed[0:rows]
    extra = summed[rows:block_rows]
    extra_t = jnp.transpose(extra)
    inverse_col = lax.rsqrt(extra_t[2 * rows : 3 * rows, 0:1] / full_width + norm_eps)
    inverse_row = lax.rsqrt(extra[0:1, 2 * rows : 3 * rows] / full_width + norm_eps)
    gate_gap = extra[0:1, 0:rows] * inverse_row - extra[0:1, rows : 2 * rows] * inverse_row
    gate_row = jnp.concatenate([jax.nn.sigmoid(gate_gap), jax.nn.sigmoid(-gate_gap)], axis=1)
    gate_row = gate_row.astype(jnp.bfloat16).astype(jnp.float32)
    scaled = partials * inverse_col
    query = jnp.concatenate(
        [scaled[:, 0:head_dim], scaled[:, head_dim : 2 * head_dim]], axis=0
    ).astype(jnp.bfloat16)
    fresh_keys = scaled[:, 2 * head_dim : 3 * head_dim].astype(jnp.bfloat16)
    fresh_values = scaled[:, 3 * head_dim : 4 * head_dim].astype(jnp.bfloat16)
    score_scale = head_dim ** (-0.5)
    contract_last = (((1,), (1,)), ((), ()))
    cached = lax.dot_general(query, cache_k_ref[...], contract_last, preferred_element_type=jnp.float32)
    cached = cached * score_scale
    key_col = lax.broadcasted_iota(jnp.int32, cached.shape, 1)
    cached = jnp.where(key_col < length_ref[0], cached, masked_score)
    fresh = lax.dot_general(query, fresh_keys, contract_last, preferred_element_type=jnp.float32)
    fresh = fresh * score_scale
    fresh_col = lax.broadcasted_iota(jnp.int32, fresh.shape, 1)
    query_token = lax.broadcasted_iota(jnp.int32, fresh.shape, 0) % rows
    fresh = jnp.where(fresh_col <= query_token, fresh, masked_score)
    top = jnp.maximum(
        jnp.max(cached, axis=1, keepdims=True), jnp.max(fresh, axis=1, keepdims=True)
    )
    cached_weights = jnp.exp(cached - top)
    fresh_weights = jnp.exp(fresh - top)
    denominator = jnp.sum(cached_weights, axis=1, keepdims=True) + jnp.sum(
        fresh_weights, axis=1, keepdims=True
    )
    attended = jnp.dot(
        cached_weights.astype(jnp.bfloat16), cache_v_ref[...], preferred_element_type=jnp.float32
    ) + jnp.dot(fresh_weights.astype(jnp.bfloat16), fresh_values, preferred_element_type=jnp.float32)
    attended = (attended / denominator).astype(jnp.bfloat16)
    first_slot = attended[0:rows]
    second_slot = attended[rows : 2 * rows]
    extra_row = lax.broadcasted_iota(jnp.int32, (EXTRA_ROWS, 2 * rows), 0)
    gate_block = jnp.where(
        extra_row == 0, jnp.broadcast_to(gate_row, (EXTRA_ROWS, 2 * rows)), 0.0
    ).astype(jnp.bfloat16)
    for member in range(out_ref.shape[0]):
        out_ref[member, 0:rows, 0:head_dim] = first_slot
        out_ref[member, 0:rows, head_dim : 2 * head_dim] = second_slot
        out_ref[member, rows:block_rows, :] = gate_block


def attend(length, blocks, cache_k, cache_v):
    members, block_rows, packed_cols = blocks.shape
    rows = block_rows - EXTRA_ROWS
    span, head_dim = cache_k.shape
    full = lambda shape: pl.BlockSpec(shape, lambda i, length_ref: (0,) * len(shape))
    out_shape = (members, block_rows, 2 * head_dim)
    keys = span + rows
    query_rows = 2 * rows
    return pl.pallas_call(
        attend_kernel,
        out_shape=jax.ShapeDtypeStruct(out_shape, jnp.bfloat16),
        grid_spec=pltpu.PrefetchScalarGridSpec(
            num_scalar_prefetch=1,
            grid=(1,),
            in_specs=[full(blocks.shape), full(cache_k.shape), full(cache_v.shape)],
            out_specs=full(out_shape),
        ),
        cost_estimate=pl.CostEstimate(
            flops=4 * query_rows * keys * head_dim,
            transcendentals=query_rows * keys,
            bytes_accessed=4 * blocks.size + 4 * span * head_dim + 2 * members * block_rows * 2 * head_dim,
        ),
    )(length.reshape(1), blocks, cache_k, cache_v)


def per_device(
    tokens,
    gain,
    w_router,
    expert_query_weight,
    key_value_weight,
    expert_output_weight,
    cache_keys,
    cached_value_slots,
    lengths,
    deal,
    route,
):
    requests = lengths.shape[0]
    experts = expert_query_weight.shape[0]
    heads_local = expert_query_weight.shape[2]
    head_dim = expert_query_weight.shape[3]
    top_count = route.shape[1]
    gathered = lax.all_gather(
        lax.all_gather(tokens, TOKEN_AXES[1], axis=0, tiled=True), TOKEN_AXES[0], axis=0, tiled=True
    )
    total_rows, local_width = gathered.shape
    new_len = total_rows // requests
    full_width = local_width * lax.axis_size("gx")
    slot_index = lax.axis_index("gx")
    inverse = jnp.zeros((requests,), jnp.int32).at[deal].set(jnp.arange(requests, dtype=jnp.int32))
    assert heads_local == 1
    packed = packed_partials(
        inverse,
        gathered,
        gain,
        w_router,
        expert_query_weight.reshape(experts, local_width, head_dim),
        key_value_weight.reshape(local_width, 2 * head_dim),
        route,
    )
    query_cols = top_count * heads_local * head_dim
    keyval_cols = heads_local * 2 * head_dim
    members = lax.axis_size("gx")
    blocks = lax.all_to_all(
        packed.reshape(members, packed.shape[0] // members, packed.shape[1]), "gx", 0, 0, tiled=True
    )
    length = jnp.take(lengths, jnp.take(inverse, slot_index))
    copies = attend(length, blocks, cache_keys[0, 0], cached_value_slots[0, 0])
    extra_rows = EXTRA_ROWS
    all_shipped = lax.all_to_all(copies, "gx", 0, 0, tiled=True).reshape(
        requests, new_len + extra_rows, query_cols
    )
    cores = lax.axis_size("cc")
    chips = lax.axis_size("zz")
    staged = jnp.arange(requests, dtype=jnp.int32).reshape(chips, cores).T.reshape(requests)
    by_request = jnp.take(all_shipped, jnp.take(deal, staged), axis=0)
    route = jnp.take(route.reshape(requests, new_len, top_count), staged, axis=0).reshape(
        total_rows, top_count
    )
    token_attended = by_request[:, :new_len].reshape(total_rows, top_count, heads_local, head_dim)
    token_gates = (
        jnp.transpose(
            by_request[:, new_len, : top_count * new_len].reshape(requests, top_count, new_len),
            (0, 2, 1),
        )
        .reshape(total_rows, top_count)
        .astype(jnp.float32)
    )
    onehot = expert_onehot(route, experts)
    routed_attended = token_attended[:, :, None, :, :] * onehot[:, :, :, None, None].astype(
        jnp.bfloat16
    )
    projected = jnp.einsum(
        "tsehk,ehko->tso", routed_attended, expert_output_weight, preferred_element_type=jnp.float32
    )
    mixed_part = jnp.sum(token_gates[:, :, None] * projected, axis=1)
    output_sum = scatter_sum(scatter_sum(mixed_part, "cc"), "zz")
    return output_sum.astype(jnp.bfloat16)


TOKEN_AXES = ("zz", "cc")


def solution(mesh):
    gx_size, gy_size = mesh.devices.shape
    staged_mesh = Mesh(mesh.devices.reshape(gx_size, gy_size // 2, 2), ("gx",) + TOKEN_AXES)
    gy = TOKEN_AXES
    placed = (
        P(gy, "gx"),
        P("gx"),
        P("gx", None),
        P(None, "gx", gy, None),
        P("gx", gy, None),
        P(None, gy, None, "gx"),
        P("gx", gy, None, None),
        P("gx", gy, None, None),
        P(),
        P(),
        P(),
    )
    return jax.shard_map(
        per_device, mesh=staged_mesh, in_specs=placed, out_specs=P(gy, "gx"), check_vma=False
    )
```

```python
import jax
import jax.numpy as jnp
from jax import lax
from jax.experimental import pallas as pl
from jax.experimental.pallas import tpu as pltpu
from jax.sharding import Mesh, PartitionSpec as P

masked_score = -1e30
norm_eps = 1e-06
LANES = 128


def expert_onehot(route_rows, experts):
    return (route_rows[:, :, None] == jnp.arange(experts, dtype=jnp.int32)[None, None, :]).astype(
        jnp.float32
    )


def padded_width(width):
    return -(-width // LANES) * LANES


def scatter_sum(part, axis_name):
    members = lax.axis_size(axis_name)
    blocks = lax.all_to_all(
        part.reshape((members, part.shape[0] // members) + part.shape[1:]),
        axis_name,
        0,
        0,
        tiled=True,
    )
    return jnp.sum(blocks, axis=0)


def gather_rows(piece, axis_name):
    members = lax.axis_size(axis_name)
    copies = jnp.broadcast_to(piece[None], (members,) + piece.shape)
    gathered = lax.all_to_all(copies, axis_name, 0, 0, tiled=True)
    return gathered.reshape((members * piece.shape[0],) + piece.shape[1:])


def pack_kernel(order_ref, tok_ref, gain_ref, router_ref, weight_ref, route_ref, route_t_ref, out_ref):
    rows = tok_ref.shape[0] // order_ref.shape[0]
    block_rows = rows + EXTRA_ROWS
    head_dim = out_ref.shape[1] // 4
    experts = (weight_ref.shape[1] - 2 * head_dim) // head_dim
    contract_last = (((1,), (1,)), ((), ()))
    step = pl.program_id(0)
    for block in range(REQUESTS_PER_STEP):
        first_row = pl.multiple_of(order_ref[step * REQUESTS_PER_STEP + block] * rows, rows)
        widened = tok_ref[pl.ds(first_row, rows), :].astype(jnp.float32)
        scaled = (widened * gain_ref[...].astype(jnp.float32)).astype(jnp.bfloat16)
        projected = jnp.dot(scaled, weight_ref[...], preferred_element_type=jnp.float32)
        route = route_ref[pl.ds(first_row, rows), :]
        first = route[:, 0:1]
        second = route[:, 1:2]
        query_first = jnp.zeros((rows, head_dim), jnp.float32)
        query_second = jnp.zeros((rows, head_dim), jnp.float32)
        for expert in range(experts):
            part = projected[:, expert * head_dim : (expert + 1) * head_dim]
            query_first = query_first + jnp.where(first == expert, part, 0.0)
            query_second = query_second + jnp.where(second == expert, part, 0.0)
        top = block * block_rows
        out_ref[top : top + rows, 0:head_dim] = query_first
        out_ref[top : top + rows, head_dim : 2 * head_dim] = query_second
        out_ref[top : top + rows, 2 * head_dim :] = projected[:, experts * head_dim :]
        widened_t = jnp.transpose(widened)
        squares_row = jnp.sum(widened_t * widened_t, axis=0, keepdims=True)
        logits_t = lax.dot_general(
            router_ref[...], scaled, contract_last, preferred_element_type=jnp.float32
        )
        expert_row = lax.broadcasted_iota(jnp.int32, logits_t.shape, 0)
        route_t = route_t_ref[:, pl.ds(first_row, rows)]
        chosen_first = jnp.sum(
            jnp.where(expert_row == route_t[0:1, :], logits_t, 0.0), axis=0, keepdims=True
        )
        chosen_second = jnp.sum(
            jnp.where(expert_row == route_t[1:2, :], logits_t, 0.0), axis=0, keepdims=True
        )
        out_ref[top + rows : top + block_rows, :] = jnp.zeros((EXTRA_ROWS, out_ref.shape[1]), jnp.float32)
        out_ref[top + rows : top + rows + 1, 0:rows] = chosen_first
        out_ref[top + rows : top + rows + 1, rows : 2 * rows] = chosen_second
        out_ref[top + rows : top + rows + 1, 2 * rows : 3 * rows] = squares_row


EXTRA_ROWS = 8
REQUESTS_PER_STEP = 8


def packed_partials(order, gathered, gain, w_router, query_weight, keyval_weight, route):
    total_rows, width = gathered.shape
    requests = order.shape[0]
    rows = total_rows // requests
    experts, _, head_dim = query_weight.shape
    keyval_cols = keyval_weight.shape[1]
    packed_cols = 2 * head_dim + keyval_cols
    assert 3 * rows <= packed_cols and keyval_cols == 2 * head_dim
    block_rows = rows + EXTRA_ROWS
    weight = jnp.concatenate(
        [jnp.transpose(query_weight, (1, 0, 2)).reshape(width, experts * head_dim), keyval_weight],
        axis=1,
    )
    flops = 2 * total_rows * width * (weight.shape[1] + w_router.shape[1])
    moved = 2 * total_rows * width + 4 * requests * block_rows * packed_cols + 2 * weight.size
    whole = lambda shape: pl.BlockSpec(shape, lambda s, order_ref: (0,) * len(shape))
    route_t = jnp.transpose(route)
    return pl.pallas_call(
        pack_kernel,
        out_shape=jax.ShapeDtypeStruct((requests * block_rows, packed_cols), jnp.float32),
        grid_spec=pltpu.PrefetchScalarGridSpec(
            num_scalar_prefetch=1,
            grid=(requests // REQUESTS_PER_STEP,),
            in_specs=[
                whole(gathered.shape),
                whole((1, width)),
                whole((w_router.shape[1], width)),
                whole(weight.shape),
                whole(route.shape),
                whole(route_t.shape),
            ],
            out_specs=pl.BlockSpec(
                (REQUESTS_PER_STEP * block_rows, packed_cols), lambda s, order_ref: (s, 0)
            ),
        ),
        cost_estimate=pl.CostEstimate(flops=flops, transcendentals=0, bytes_accessed=moved),
    )(order, gathered, gain.reshape(1, width), jnp.transpose(w_router), weight, route, route_t)


def attend_kernel(length_ref, blocks_ref, cache_k_ref, cache_v_ref, out_ref):
    members, block_rows, packed_cols = blocks_ref.shape
    rows = block_rows - EXTRA_ROWS
    head_dim = cache_k_ref.shape[1]
    full_width = members * LANES
    summed = blocks_ref[0]
    for member in range(1, members):
        summed = summed + blocks_ref[member]
    partials = summed[0:rows]
    extra = summed[rows:block_rows]
    extra_t = jnp.transpose(extra)
    inverse_col = lax.rsqrt(extra_t[2 * rows : 3 * rows, 0:1] / full_width + norm_eps)
    inverse_row = lax.rsqrt(extra[0:1, 2 * rows : 3 * rows] / full_width + norm_eps)
    gate_gap = extra[0:1, 0:rows] * inverse_row - extra[0:1, rows : 2 * rows] * inverse_row
    gate_row = jnp.concatenate([jax.nn.sigmoid(gate_gap), jax.nn.sigmoid(-gate_gap)], axis=1)
    gate_row = gate_row.astype(jnp.bfloat16).astype(jnp.float32)
    scaled = partials * inverse_col
    query = jnp.concatenate(
        [scaled[:, 0:head_dim], scaled[:, head_dim : 2 * head_dim]], axis=0
    ).astype(jnp.bfloat16)
    fresh_keys = scaled[:, 2 * head_dim : 3 * head_dim].astype(jnp.bfloat16)
    fresh_values = scaled[:, 3 * head_dim : 4 * head_dim].astype(jnp.bfloat16)
    score_scale = head_dim ** (-0.5)
    contract_last = (((1,), (1,)), ((), ()))
    cached = lax.dot_general(query, cache_k_ref[...], contract_last, preferred_element_type=jnp.float32)
    cached = cached * score_scale
    key_col = lax.broadcasted_iota(jnp.int32, cached.shape, 1)
    cached = jnp.where(key_col < length_ref[0], cached, masked_score)
    fresh = lax.dot_general(query, fresh_keys, contract_last, preferred_element_type=jnp.float32)
    fresh = fresh * score_scale
    fresh_col = lax.broadcasted_iota(jnp.int32, fresh.shape, 1)
    query_token = lax.broadcasted_iota(jnp.int32, fresh.shape, 0) % rows
    fresh = jnp.where(fresh_col <= query_token, fresh, masked_score)
    top = jnp.maximum(
        jnp.max(cached, axis=1, keepdims=True), jnp.max(fresh, axis=1, keepdims=True)
    )
    cached_weights = jnp.exp(cached - top)
    fresh_weights = jnp.exp(fresh - top)
    denominator = jnp.sum(cached_weights, axis=1, keepdims=True) + jnp.sum(
        fresh_weights, axis=1, keepdims=True
    )
    attended = jnp.dot(
        cached_weights.astype(jnp.bfloat16), cache_v_ref[...], preferred_element_type=jnp.float32
    ) + jnp.dot(fresh_weights.astype(jnp.bfloat16), fresh_values, preferred_element_type=jnp.float32)
    attended = (attended / denominator).astype(jnp.bfloat16)
    first_slot = attended[0:rows]
    second_slot = attended[rows : 2 * rows]
    extra_row = lax.broadcasted_iota(jnp.int32, (EXTRA_ROWS, 2 * rows), 0)
    gate_block = jnp.where(
        extra_row == 0, jnp.broadcast_to(gate_row, (EXTRA_ROWS, 2 * rows)), 0.0
    ).astype(jnp.bfloat16)
    for member in range(out_ref.shape[0]):
        out_ref[member, 0:rows, 0:head_dim] = first_slot
        out_ref[member, 0:rows, head_dim : 2 * head_dim] = second_slot
        out_ref[member, rows:block_rows, :] = gate_block


def attend(length, blocks, cache_k, cache_v):
    members, block_rows, packed_cols = blocks.shape
    rows = block_rows - EXTRA_ROWS
    span, head_dim = cache_k.shape
    full = lambda shape: pl.BlockSpec(shape, lambda i, length_ref: (0,) * len(shape))
    out_shape = (members, block_rows, 2 * head_dim)
    keys = span + rows
    query_rows = 2 * rows
    return pl.pallas_call(
        attend_kernel,
        out_shape=jax.ShapeDtypeStruct(out_shape, jnp.bfloat16),
        grid_spec=pltpu.PrefetchScalarGridSpec(
            num_scalar_prefetch=1,
            grid=(1,),
            in_specs=[full(blocks.shape), full(cache_k.shape), full(cache_v.shape)],
            out_specs=full(out_shape),
        ),
        cost_estimate=pl.CostEstimate(
            flops=4 * query_rows * keys * head_dim,
            transcendentals=query_rows * keys,
            bytes_accessed=4 * blocks.size + 4 * span * head_dim + 2 * members * block_rows * 2 * head_dim,
        ),
    )(length.reshape(1), blocks, cache_k, cache_v)


def per_device(
    tokens,
    gain,
    w_router,
    expert_query_weight,
    key_value_weight,
    expert_output_weight,
    cache_keys,
    cached_value_slots,
    lengths,
    deal,
    route,
):
    requests = lengths.shape[0]
    experts = expert_query_weight.shape[0]
    heads_local = expert_query_weight.shape[2]
    head_dim = expert_query_weight.shape[3]
    top_count = route.shape[1]
    gathered = lax.all_gather(
        lax.all_gather(tokens, TOKEN_AXES[1], axis=0, tiled=True), TOKEN_AXES[0], axis=0, tiled=True
    )
    total_rows, local_width = gathered.shape
    new_len = total_rows // requests
    full_width = local_width * lax.axis_size("gx")
    slot_index = lax.axis_index("gx")
    inverse = jnp.zeros((requests,), jnp.int32).at[deal].set(jnp.arange(requests, dtype=jnp.int32))
    assert heads_local == 1
    packed = packed_partials(
        inverse,
        gathered,
        gain,
        w_router,
        expert_query_weight.reshape(experts, local_width, head_dim),
        key_value_weight.reshape(local_width, 2 * head_dim),
        route,
    )
    query_cols = top_count * heads_local * head_dim
    keyval_cols = heads_local * 2 * head_dim
    members = lax.axis_size("gx")
    blocks = lax.all_to_all(
        packed.reshape(members, packed.shape[0] // members, packed.shape[1]), "gx", 0, 0, tiled=True
    )
    length = jnp.take(lengths, jnp.take(inverse, slot_index))
    copies = attend(length, blocks, cache_keys[0, 0], cached_value_slots[0, 0])
    extra_rows = EXTRA_ROWS
    all_shipped = lax.all_to_all(copies, "gx", 0, 0, tiled=True).reshape(
        requests, new_len + extra_rows, query_cols
    )
    cores = lax.axis_size("cc")
    chips = lax.axis_size("zz")
    staged = jnp.arange(requests, dtype=jnp.int32).reshape(chips, cores).T.reshape(requests)
    by_request = jnp.take(all_shipped, jnp.take(deal, staged), axis=0)
    route = jnp.take(route.reshape(requests, new_len, top_count), staged, axis=0).reshape(
        total_rows, top_count
    )
    token_attended = by_request[:, :new_len].reshape(total_rows, top_count, heads_local, head_dim)
    token_gates = (
        jnp.transpose(
            by_request[:, new_len, : top_count * new_len].reshape(requests, top_count, new_len),
            (0, 2, 1),
        )
        .reshape(total_rows, top_count)
        .astype(jnp.float32)
    )
    onehot = expert_onehot(route, experts)
    routed_attended = token_attended[:, :, None, :, :] * onehot[:, :, :, None, None].astype(
        jnp.bfloat16
    )
    projected = jnp.einsum(
        "tsehk,ehko->tso", routed_attended, expert_output_weight, preferred_element_type=jnp.float32
    )
    mixed_part = jnp.sum(token_gates[:, :, None] * projected, axis=1)
    output_sum = scatter_sum(scatter_sum(mixed_part, "cc"), "zz")
    return output_sum.astype(jnp.bfloat16)


TOKEN_AXES = ("zz", "cc")


def solution(mesh):
    gx_size, gy_size = mesh.devices.shape
    staged_mesh = Mesh(mesh.devices.reshape(gx_size, gy_size // 2, 2), ("gx",) + TOKEN_AXES)
    gy = TOKEN_AXES
    placed = (
        P(gy, "gx"),
        P("gx"),
        P("gx", None),
        P(None, "gx", gy, None),
        P("gx", gy, None),
        P(None, gy, None, "gx"),
        P("gx", gy, None, None),
        P("gx", gy, None, None),
        P(),
        P(),
        P(),
    )
    return jax.shard_map(
        per_device, mesh=staged_mesh, in_specs=placed, out_specs=P(gy, "gx"), check_vma=False
    )
```

```python
import jax
import jax.numpy as jnp
from jax import lax
from jax.experimental import pallas as pl
from jax.experimental.pallas import tpu as pltpu
from jax.sharding import Mesh, PartitionSpec as P

masked_score = -1e30
norm_eps = 1e-06
LANES = 128


def expert_onehot(route_rows, experts):
    return (route_rows[:, :, None] == jnp.arange(experts, dtype=jnp.int32)[None, None, :]).astype(
        jnp.float32
    )


def padded_width(width):
    return -(-width // LANES) * LANES


def scatter_sum(part, axis_name):
    members = lax.axis_size(axis_name)
    blocks = lax.all_to_all(
        part.reshape((members, part.shape[0] // members) + part.shape[1:]),
        axis_name,
        0,
        0,
        tiled=True,
    )
    return jnp.sum(blocks, axis=0)


def gather_rows(piece, axis_name):
    members = lax.axis_size(axis_name)
    copies = jnp.broadcast_to(piece[None], (members,) + piece.shape)
    gathered = lax.all_to_all(copies, axis_name, 0, 0, tiled=True)
    return gathered.reshape((members * piece.shape[0],) + piece.shape[1:])


def pack_kernel(order_ref, tok_ref, gain_ref, router_ref, weight_ref, route_ref, route_t_ref, out_ref):
    rows = tok_ref.shape[0] // order_ref.shape[0]
    block_rows = rows + EXTRA_ROWS
    head_dim = out_ref.shape[1] // 4
    experts = (weight_ref.shape[1] - 2 * head_dim) // head_dim
    contract_last = (((1,), (1,)), ((), ()))
    step = pl.program_id(0)
    for block in range(REQUESTS_PER_STEP):
        first_row = pl.multiple_of(order_ref[step * REQUESTS_PER_STEP + block] * rows, rows)
        widened = tok_ref[pl.ds(first_row, rows), :].astype(jnp.float32)
        scaled = (widened * gain_ref[...].astype(jnp.float32)).astype(jnp.bfloat16)
        projected = jnp.dot(scaled, weight_ref[...], preferred_element_type=jnp.float32)
        route = route_ref[pl.ds(first_row, rows), :]
        first = route[:, 0:1]
        second = route[:, 1:2]
        query_first = jnp.zeros((rows, head_dim), jnp.float32)
        query_second = jnp.zeros((rows, head_dim), jnp.float32)
        for expert in range(experts):
            part = projected[:, expert * head_dim : (expert + 1) * head_dim]
            query_first = query_first + jnp.where(first == expert, part, 0.0)
            query_second = query_second + jnp.where(second == expert, part, 0.0)
        top = block * block_rows
        out_ref[top : top + rows, 0:head_dim] = query_first
        out_ref[top : top + rows, head_dim : 2 * head_dim] = query_second
        out_ref[top : top + rows, 2 * head_dim :] = projected[:, experts * head_dim :]
        widened_t = jnp.transpose(widened)
        squares_row = jnp.sum(widened_t * widened_t, axis=0, keepdims=True)
        logits_t = lax.dot_general(
            router_ref[...], scaled, contract_last, preferred_element_type=jnp.float32
        )
        expert_row = lax.broadcasted_iota(jnp.int32, logits_t.shape, 0)
        route_t = route_t_ref[:, pl.ds(first_row, rows)]
        chosen_first = jnp.sum(
            jnp.where(expert_row == route_t[0:1, :], logits_t, 0.0), axis=0, keepdims=True
        )
        chosen_second = jnp.sum(
            jnp.where(expert_row == route_t[1:2, :], logits_t, 0.0), axis=0, keepdims=True
        )
        out_ref[top + rows : top + block_rows, :] = jnp.zeros((EXTRA_ROWS, out_ref.shape[1]), jnp.float32)
        out_ref[top + rows : top + rows + 1, 0:rows] = chosen_first
        out_ref[top + rows : top + rows + 1, rows : 2 * rows] = chosen_second
        out_ref[top + rows : top + rows + 1, 2 * rows : 3 * rows] = squares_row


EXTRA_ROWS = 8
REQUESTS_PER_STEP = 2


def packed_partials(order, gathered, gain, w_router, query_weight, keyval_weight, route):
    total_rows, width = gathered.shape
    requests = order.shape[0]
    rows = total_rows // requests
    experts, _, head_dim = query_weight.shape
    keyval_cols = keyval_weight.shape[1]
    packed_cols = 2 * head_dim + keyval_cols
    assert 3 * rows <= packed_cols and keyval_cols == 2 * head_dim
    block_rows = rows + EXTRA_ROWS
    weight = jnp.concatenate(
        [jnp.transpose(query_weight, (1, 0, 2)).reshape(width, experts * head_dim), keyval_weight],
        axis=1,
    )
    flops = 2 * total_rows * width * (weight.shape[1] + w_router.shape[1])
    moved = 2 * total_rows * width + 4 * requests * block_rows * packed_cols + 2 * weight.size
    whole = lambda shape: pl.BlockSpec(shape, lambda s, order_ref: (0,) * len(shape))
    route_t = jnp.transpose(route)
    return pl.pallas_call(
        pack_kernel,
        out_shape=jax.ShapeDtypeStruct((requests * block_rows, packed_cols), jnp.float32),
        grid_spec=pltpu.PrefetchScalarGridSpec(
            num_scalar_prefetch=1,
            grid=(requests // REQUESTS_PER_STEP,),
            in_specs=[
                whole(gathered.shape),
                whole((1, width)),
                whole((w_router.shape[1], width)),
                whole(weight.shape),
                whole(route.shape),
                whole(route_t.shape),
            ],
            out_specs=pl.BlockSpec(
                (REQUESTS_PER_STEP * block_rows, packed_cols), lambda s, order_ref: (s, 0)
            ),
        ),
        cost_estimate=pl.CostEstimate(flops=flops, transcendentals=0, bytes_accessed=moved),
    )(order, gathered, gain.reshape(1, width), jnp.transpose(w_router), weight, route, route_t)


def attend_kernel(length_ref, blocks_ref, cache_k_ref, cache_v_ref, out_ref):
    members, block_rows, packed_cols = blocks_ref.shape
    rows = block_rows - EXTRA_ROWS
    head_dim = cache_k_ref.shape[1]
    full_width = members * LANES
    summed = blocks_ref[0]
    for member in range(1, members):
        summed = summed + blocks_ref[member]
    partials = summed[0:rows]
    extra = summed[rows:block_rows]
    extra_t = jnp.transpose(extra)
    inverse_col = lax.rsqrt(extra_t[2 * rows : 3 * rows, 0:1] / full_width + norm_eps)
    inverse_row = lax.rsqrt(extra[0:1, 2 * rows : 3 * rows] / full_width + norm_eps)
    gate_gap = extra[0:1, 0:rows] * inverse_row - extra[0:1, rows : 2 * rows] * inverse_row
    gate_row = jnp.concatenate([jax.nn.sigmoid(gate_gap), jax.nn.sigmoid(-gate_gap)], axis=1)
    gate_row = gate_row.astype(jnp.bfloat16).astype(jnp.float32)
    scaled = partials * inverse_col
    query = jnp.concatenate(
        [scaled[:, 0:head_dim], scaled[:, head_dim : 2 * head_dim]], axis=0
    ).astype(jnp.bfloat16)
    fresh_keys = scaled[:, 2 * head_dim : 3 * head_dim].astype(jnp.bfloat16)
    fresh_values = scaled[:, 3 * head_dim : 4 * head_dim].astype(jnp.bfloat16)
    score_scale = head_dim ** (-0.5)
    contract_last = (((1,), (1,)), ((), ()))
    cached = lax.dot_general(query, cache_k_ref[...], contract_last, preferred_element_type=jnp.float32)
    cached = cached * score_scale
    key_col = lax.broadcasted_iota(jnp.int32, cached.shape, 1)
    cached = jnp.where(key_col < length_ref[0], cached, masked_score)
    fresh = lax.dot_general(query, fresh_keys, contract_last, preferred_element_type=jnp.float32)
    fresh = fresh * score_scale
    fresh_col = lax.broadcasted_iota(jnp.int32, fresh.shape, 1)
    query_token = lax.broadcasted_iota(jnp.int32, fresh.shape, 0) % rows
    fresh = jnp.where(fresh_col <= query_token, fresh, masked_score)
    top = jnp.maximum(
        jnp.max(cached, axis=1, keepdims=True), jnp.max(fresh, axis=1, keepdims=True)
    )
    cached_weights = jnp.exp(cached - top)
    fresh_weights = jnp.exp(fresh - top)
    denominator = jnp.sum(cached_weights, axis=1, keepdims=True) + jnp.sum(
        fresh_weights, axis=1, keepdims=True
    )
    attended = jnp.dot(
        cached_weights.astype(jnp.bfloat16), cache_v_ref[...], preferred_element_type=jnp.float32
    ) + jnp.dot(fresh_weights.astype(jnp.bfloat16), fresh_values, preferred_element_type=jnp.float32)
    attended = (attended / denominator).astype(jnp.bfloat16)
    first_slot = attended[0:rows]
    second_slot = attended[rows : 2 * rows]
    extra_row = lax.broadcasted_iota(jnp.int32, (EXTRA_ROWS, 2 * rows), 0)
    gate_block = jnp.where(
        extra_row == 0, jnp.broadcast_to(gate_row, (EXTRA_ROWS, 2 * rows)), 0.0
    ).astype(jnp.bfloat16)
    for member in range(out_ref.shape[0]):
        out_ref[member, 0:rows, 0:head_dim] = first_slot
        out_ref[member, 0:rows, head_dim : 2 * head_dim] = second_slot
        out_ref[member, rows:block_rows, :] = gate_block


def attend(length, blocks, cache_k, cache_v):
    members, block_rows, packed_cols = blocks.shape
    rows = block_rows - EXTRA_ROWS
    span, head_dim = cache_k.shape
    full = lambda shape: pl.BlockSpec(shape, lambda i, length_ref: (0,) * len(shape))
    out_shape = (members, block_rows, 2 * head_dim)
    keys = span + rows
    query_rows = 2 * rows
    return pl.pallas_call(
        attend_kernel,
        out_shape=jax.ShapeDtypeStruct(out_shape, jnp.bfloat16),
        grid_spec=pltpu.PrefetchScalarGridSpec(
            num_scalar_prefetch=1,
            grid=(1,),
            in_specs=[full(blocks.shape), full(cache_k.shape), full(cache_v.shape)],
            out_specs=full(out_shape),
        ),
        cost_estimate=pl.CostEstimate(
            flops=4 * query_rows * keys * head_dim,
            transcendentals=query_rows * keys,
            bytes_accessed=4 * blocks.size + 4 * span * head_dim + 2 * members * block_rows * 2 * head_dim,
        ),
    )(length.reshape(1), blocks, cache_k, cache_v)


def per_device(
    tokens,
    gain,
    w_router,
    expert_query_weight,
    key_value_weight,
    expert_output_weight,
    cache_keys,
    cached_value_slots,
    lengths,
    deal,
    route,
):
    requests = lengths.shape[0]
    experts = expert_query_weight.shape[0]
    heads_local = expert_query_weight.shape[2]
    head_dim = expert_query_weight.shape[3]
    top_count = route.shape[1]
    gathered = lax.all_gather(
        lax.all_gather(tokens, TOKEN_AXES[1], axis=0, tiled=True), TOKEN_AXES[0], axis=0, tiled=True
    )
    total_rows, local_width = gathered.shape
    new_len = total_rows // requests
    full_width = local_width * lax.axis_size("gx")
    slot_index = lax.axis_index("gx")
    inverse = jnp.zeros((requests,), jnp.int32).at[deal].set(jnp.arange(requests, dtype=jnp.int32))
    assert heads_local == 1
    packed = packed_partials(
        inverse,
        gathered,
        gain,
        w_router,
        expert_query_weight.reshape(experts, local_width, head_dim),
        key_value_weight.reshape(local_width, 2 * head_dim),
        route,
    )
    query_cols = top_count * heads_local * head_dim
    keyval_cols = heads_local * 2 * head_dim
    members = lax.axis_size("gx")
    blocks = lax.all_to_all(
        packed.reshape(members, packed.shape[0] // members, packed.shape[1]), "gx", 0, 0, tiled=True
    )
    length = jnp.take(lengths, jnp.take(inverse, slot_index))
    copies = attend(length, blocks, cache_keys[0, 0], cached_value_slots[0, 0])
    extra_rows = EXTRA_ROWS
    all_shipped = lax.all_to_all(copies, "gx", 0, 0, tiled=True).reshape(
        requests, new_len + extra_rows, query_cols
    )
    cores = lax.axis_size("cc")
    chips = lax.axis_size("zz")
    staged = jnp.arange(requests, dtype=jnp.int32).reshape(chips, cores).T.reshape(requests)
    by_request = jnp.take(all_shipped, jnp.take(deal, staged), axis=0)
    route = jnp.take(route.reshape(requests, new_len, top_count), staged, axis=0).reshape(
        total_rows, top_count
    )
    token_attended = by_request[:, :new_len].reshape(total_rows, top_count, heads_local, head_dim)
    token_gates = (
        jnp.transpose(
            by_request[:, new_len, : top_count * new_len].reshape(requests, top_count, new_len),
            (0, 2, 1),
        )
        .reshape(total_rows, top_count)
        .astype(jnp.float32)
    )
    onehot = expert_onehot(route, experts)
    routed_attended = token_attended[:, :, None, :, :] * onehot[:, :, :, None, None].astype(
        jnp.bfloat16
    )
    projected = jnp.einsum(
        "tsehk,ehko->tso", routed_attended, expert_output_weight, preferred_element_type=jnp.float32
    )
    mixed_part = jnp.sum(token_gates[:, :, None] * projected, axis=1)
    output_sum = scatter_sum(scatter_sum(mixed_part, "cc"), "zz")
    return output_sum.astype(jnp.bfloat16)


TOKEN_AXES = ("zz", "cc")


def solution(mesh):
    gx_size, gy_size = mesh.devices.shape
    staged_mesh = Mesh(mesh.devices.reshape(gx_size, gy_size // 2, 2), ("gx",) + TOKEN_AXES)
    gy = TOKEN_AXES
    placed = (
        P(gy, "gx"),
        P("gx"),
        P("gx", None),
        P(None, "gx", gy, None),
        P("gx", gy, None),
        P(None, gy, None, "gx"),
        P("gx", gy, None, None),
        P("gx", gy, None, None),
        P(),
        P(),
        P(),
    )
    return jax.shard_map(
        per_device, mesh=staged_mesh, in_specs=placed, out_specs=P(gy, "gx"), check_vma=False
    )
```
